32 devices in a mesh: tx: 4 (over y, x), ty: 8 (over z, core).
Axes of the slice: x: 2, y: 2, z: 4, core: 2. Of those that a mesh axis runs over, the one named last changes fastest.
Arguments:
- stack: bfloat16 [32, 2, 128, 4096], P('tx', None, None, 'ty'), may hold values from -6 to 6
- filt_re: bfloat16 [32, 32], replicated, may hold values from -0.75 to 0.75
- filt_im: bfloat16 [32, 32], replicated, may hold values from -0.75 to 0.75
- pre_ids: int32 [32], replicated, may hold values from 0 to 15
- post_ids: int32 [32], replicated, may hold values from 16 to 31
Outputs:
- coherence: float32 [32, 128, 4096], P(None, 'ty', 'tx')
- change: float32 [32, 128, 4096], P(None, 'ty', 'tx')
The draws below stay inside these ranges and needn't reach their ends.
All inputs are finite; a program needn't handle non-finite values.
Results may differ from the reference program's by a relative error of at most 0.0065.
Values may be sent and summed in bfloat16 or wider, within the bound.
No kernel may reach another device: no remote copies, remote signals or barrier semaphores. Data moves between devices by JAX's collectives and lax.ppermute only.
A program may use at most 128 MiB of HBM per device.

```python
import jax
import jax.numpy as jnp
from jax import lax

ACQ = 32
PRE = 16
PAIRS = 32
RADIUS = 4
TR = 16
H = 128
W = 4096


def with_ends(drawn, stream_key, low, top_value):
    spot = [jax.random.randint(jax.random.fold_in(stream_key, axis), (), 0, length) for axis, length in enumerate(drawn.shape)]
    main_axis = drawn.shape.index(max(drawn.shape))
    beside = spot[:main_axis] + [(spot[main_axis] + 1) % drawn.shape[main_axis]] + spot[main_axis + 1:]
    return drawn.at[tuple(spot)].set(low).at[tuple(beside)].set(top_value)


def level_of(rng, shape, shards, smallest, top_value):
    level = 1.0
    for axis_at, parts in shards:
        draws = jax.random.uniform(jax.random.fold_in(jax.random.fold_in(rng, 6), axis_at), (parts,), jnp.float32, smallest / len(shards), top_value / len(shards))
        level = level * jnp.repeat(jnp.exp(draws), shape[axis_at] // parts).reshape((-1,) + (1,) * (len(shape) - 1 - axis_at))
    return level


def scatter_about(key, extent, width, reach, cuts=(), kind=jnp.bfloat16):
    level = level_of(key, extent, cuts, -0.22, 0.18) if cuts else 1.0
    result = jax.random.normal(key, extent, jnp.float32) * width * level
    return jnp.minimum(jnp.maximum(result, -reach), reach).astype(kind)


def setup_inputs(seed: int = 0) -> dict:
    seeds = jax.random.split(jax.random.key(seed), 6)
    stack = scatter_about(seeds[0], (ACQ, 2, H, W), 1.0, 6.0, ((0, 4), (3, 8)))
    filt_re = scatter_about(seeds[1], (ACQ, ACQ), (2 * ACQ) ** -0.5, 0.75)
    filt_im = scatter_about(seeds[2], (ACQ, ACQ), (2 * ACQ) ** -0.5, 0.75)
    pre_ids = with_ends(jax.random.randint(seeds[3], (PAIRS,), 0, PRE), jax.random.fold_in(seeds[3], 1), 0, PRE - 1).astype(jnp.int32)
    post_ids = with_ends(jax.random.randint(seeds[4], (PAIRS,), PRE, ACQ), jax.random.fold_in(seeds[4], 1), PRE, ACQ - 1).astype(jnp.int32)
    return {"stack": stack, "filt_re": filt_re, "filt_im": filt_im, "pre_ids": pre_ids, "post_ids": post_ids}


def box_mean(fields, tile_rows, tile_cols, radius):
    window = 2 * radius + 1
    rowsum = fields[:, 0:tile_rows]
    for offset in range(1, window):
        rowsum = rowsum + fields[:, offset:offset + tile_rows]
    colsum = rowsum[:, :, 0:tile_cols]
    for offset in range(1, window):
        colsum = colsum + rowsum[:, :, offset:offset + tile_cols]
    return colsum / float(window * window)

def pair_maps(padded, pre_ids, post_ids, tile_rows, tile_cols, radius):
    widened = padded.astype(jnp.float32)
    power = widened[:, 0] * widened[:, 0] + widened[:, 1] * widened[:, 1]
    pre_side = jnp.take(widened, pre_ids, axis=0)
    post_side = jnp.take(widened, post_ids, axis=0)
    cross_re = pre_side[:, 0] * post_side[:, 0] + pre_side[:, 1] * post_side[:, 1]
    cross_im = pre_side[:, 1] * post_side[:, 0] - pre_side[:, 0] * post_side[:, 1]
    fields = jnp.concatenate([power, cross_re, cross_im], axis=0)
    means = box_mean(fields, tile_rows, tile_cols, radius)
    count_acq = power.shape[0]
    count_pairs = pre_ids.shape[0]
    power_mean = means[:count_acq] + 1e-06
    pre_power = jnp.take(power_mean, pre_ids, axis=0)
    post_power = jnp.take(power_mean, post_ids, axis=0)
    real_mean = means[count_acq:count_acq + count_pairs]
    imag_mean = means[count_acq + count_pairs:]
    coherence = jnp.sqrt(real_mean * real_mean + imag_mean * imag_mean) / jnp.sqrt(pre_power * post_power)
    change = jnp.log(post_power / pre_power)
    return (coherence, change)

def reference(stack, filt_re, filt_im, pre_ids, post_ids):
    real_f = filt_re.astype(jnp.float32)
    imag_f = filt_im.astype(jnp.float32)

    def one_block(index):
        rows_at = index * TR - RADIUS + jnp.arange(TR + 2 * RADIUS).astype(jnp.int32)
        clipped = jnp.clip(rows_at, 0, H - 1).astype(jnp.int32)
        valid = (rows_at >= 0) & (rows_at < H)
        piece = jnp.take(stack, clipped, axis=2).astype(jnp.float32)
        piece = jnp.where(valid[None, None, :, None], piece, jnp.zeros_like(piece))
        piece = jnp.pad(piece, ((0, 0), (0, 0), (0, 0), (RADIUS, RADIUS)))
        real_part = jnp.einsum('ab,bhw->ahw', real_f, piece[:, 0]) - jnp.einsum('ab,bhw->ahw', imag_f, piece[:, 1])
        imag_part = jnp.einsum('ab,bhw->ahw', real_f, piece[:, 1]) + jnp.einsum('ab,bhw->ahw', imag_f, piece[:, 0])
        filtered = jnp.stack([real_part, imag_part], axis=1).astype(jnp.bfloat16)
        return pair_maps(filtered, pre_ids, post_ids, TR, W, RADIUS)
    blocks = jnp.arange(H // TR).astype(jnp.int32)
    coh_blocks, change_blocks = lax.map(one_block, blocks)
    coherence = jnp.transpose(coh_blocks, (1, 0, 2, 3)).reshape(PAIRS, H, W)
    change = jnp.transpose(change_blocks, (1, 0, 2, 3)).reshape(PAIRS, H, W)
    return (coherence, change)
```

```python
import jax
import jax.numpy as jnp
from jax import lax
from jax.sharding import PartitionSpec as P

RADIUS = 4


def with_halo(block, sides, width):
    for axis, dim in sides:
        count = lax.axis_size(axis)
        forward = [(i, i + 1) for i in range(count - 1)]
        backward = [(target, source) for source, target in forward]
        low = lax.ppermute(
            lax.slice_in_dim(block, block.shape[dim] - width, None, axis=dim), axis, forward
        )
        high = lax.ppermute(lax.slice_in_dim(block, 0, width, axis=dim), axis, backward)
        block = jnp.concatenate([low, block, high], axis=dim)
    return block


def box_mean(fields, tile_rows, tile_cols, radius):
    window = 2 * radius + 1
    rowsum = fields[:, 0:tile_rows]
    for offset in range(1, window):
        rowsum = rowsum + fields[:, offset : offset + tile_rows]
    colsum = rowsum[:, :, 0:tile_cols]
    for offset in range(1, window):
        colsum = colsum + rowsum[:, :, offset : offset + tile_cols]
    return colsum / float(window * window)


def shards(stack, filt_re, filt_im, pre_ids, post_ids):
    count_acq = filt_re.shape[0]
    count_pairs = pre_ids.shape[0]
    n_rows = lax.axis_size("ty")
    n_cols = lax.axis_size("tx")
    local_acq, _, height, local_cols = stack.shape
    tile_rows = height // n_rows
    blocks_per_tile = n_rows // n_cols
    tile_cols = local_cols * blocks_per_tile

    x = stack.reshape(local_acq, 2, n_rows, tile_rows, local_cols)
    x = jnp.transpose(x, (2, 0, 1, 3, 4))
    x = lax.all_to_all(x, "ty", 0, 0, tiled=True)
    x = x.reshape(n_cols, blocks_per_tile, local_acq, 2, tile_rows, local_cols)
    x = lax.all_to_all(x, "tx", 0, 0, tiled=True)
    x = jnp.transpose(x, (0, 2, 3, 4, 1, 5))
    x = x.reshape(2 * count_acq, tile_rows, tile_cols)
    x = with_halo(x, (("ty", 1), ("tx", 2)), RADIUS)

    mixing = jnp.stack([jnp.stack([filt_re, -filt_im], -1), jnp.stack([filt_im, filt_re], -1)], 1)
    mixing = mixing.reshape(count_acq, 2, 2 * count_acq)
    wide = jnp.concatenate(
        [mixing, jnp.take(mixing, pre_ids, axis=0), jnp.take(mixing, post_ids, axis=0)], axis=0
    )
    wide = wide.reshape(-1, 2 * count_acq)
    result = jnp.einsum("kc,chw->khw", wide, x, preferred_element_type=jnp.float32)
    filtered = result.astype(jnp.bfloat16).astype(jnp.float32)
    filtered = filtered.reshape(count_acq + 2 * count_pairs, 2, *filtered.shape[1:])

    own = filtered[:count_acq]
    pre_side = filtered[count_acq : count_acq + count_pairs]
    post_side = filtered[count_acq + count_pairs :]
    power = own[:, 0] * own[:, 0] + own[:, 1] * own[:, 1]
    cross_re = pre_side[:, 0] * post_side[:, 0] + pre_side[:, 1] * post_side[:, 1]
    cross_im = pre_side[:, 1] * post_side[:, 0] - pre_side[:, 0] * post_side[:, 1]
    fields = jnp.concatenate([power, cross_re, cross_im], axis=0)
    means = box_mean(fields, tile_rows, tile_cols, RADIUS)
    power_mean = means[:count_acq] + 1e-06
    pre_power = jnp.take(power_mean, pre_ids, axis=0)
    post_power = jnp.take(power_mean, post_ids, axis=0)
    real_mean = means[count_acq : count_acq + count_pairs]
    imag_mean = means[count_acq + count_pairs :]
    coherence = jnp.sqrt(real_mean * real_mean + imag_mean * imag_mean) / jnp.sqrt(
        pre_power * post_power
    )
    change = jnp.log(post_power / pre_power)
    return (coherence, change)


def solution(mesh):
    in_specs = (P("tx", None, None, "ty"), P(), P(), P(), P())
    out_specs = (P(None, "ty", "tx"), P(None, "ty", "tx"))
    return jax.shard_map(shards, mesh=mesh, in_specs=in_specs, out_specs=out_specs, check_vma=False)
```

```python
import functools

import jax
import jax.numpy as jnp
from jax import lax
from jax.experimental import pallas as pl
from jax.experimental.pallas import tpu as pltpu
from jax.sharding import PartitionSpec as P

RADIUS = 4
LANES = 128
PAIRS_PER_STEP = 2
FIELDS = 4


def with_halo(block, sides, width):
    for axis, dim in sides:
        count = lax.axis_size(axis)
        forward = [(i, i + 1) for i in range(count - 1)]
        backward = [(target, source) for source, target in forward]
        low = lax.ppermute(
            lax.slice_in_dim(block, block.shape[dim] - width, None, axis=dim), axis, forward
        )
        high = lax.ppermute(lax.slice_in_dim(block, 0, width, axis=dim), axis, backward)
        yield low, high
        block = jnp.concatenate([low, block, high], axis=dim)


def pair_kernel(pre_ref, post_ref, *refs, tile_rows, tile_cols):
    del pre_ref, post_ref
    pp = PAIRS_PER_STEP
    sides = refs[: 2 * pp]
    band_ref, coh_ref, chg_ref, field_ref, rows_ref, stack_ref = refs[2 * pp :]
    window = 2 * RADIUS + 1
    padded_cols = tile_cols + LANES
    rows = pp * FIELDS * tile_rows
    blocks = tile_cols // LANES
    for p in range(pp):
        a = sides[2 * p]
        b = sides[2 * p + 1]
        pr = a[0, 0].astype(jnp.float32)
        pi = a[0, 1].astype(jnp.float32)
        qr = b[0, 0].astype(jnp.float32)
        qi = b[0, 1].astype(jnp.float32)
        fields = (pr * pr + pi * pi, qr * qr + qi * qi, pr * qr + pi * qi, pi * qr - pr * qi)
        for f, value in enumerate(fields):
            field_ref[...] = value
            acc = field_ref[pl.ds(0, tile_rows), :]
            for k in range(1, window):
                acc = acc + field_ref[pl.ds(k, tile_rows), :]
            at = (p * FIELDS + f) * tile_rows
            rows_ref[pl.ds(at, tile_rows), pl.ds(LANES, padded_cols)] = acc
            rows_ref[pl.ds(at, tile_rows), pl.ds(0, LANES)] = acc[:, padded_cols - LANES :]
    rowsum = rows_ref[...]
    high = rowsum.astype(jnp.bfloat16)
    low = (rowsum - high.astype(jnp.float32)).astype(jnp.bfloat16)
    width = 3 * LANES
    for j in range(blocks):
        stack_ref[pl.ds(j * rows, rows), pl.ds(0, width)] = high[:, j * LANES : j * LANES + width]
        stack_ref[pl.ds(j * rows, rows), pl.ds(width, width)] = low[:, j * LANES : j * LANES + width]
    sums = jnp.dot(stack_ref[...], band_ref[...], preferred_element_type=jnp.float32)
    means = sums / float(window * window)
    for j in range(blocks):
        for p in range(pp):
            base = j * rows + p * FIELDS * tile_rows
            pre_power = means[base : base + tile_rows] + 1e-06
            post_power = means[base + tile_rows : base + 2 * tile_rows] + 1e-06
            real_mean = means[base + 2 * tile_rows : base + 3 * tile_rows]
            imag_mean = means[base + 3 * tile_rows : base + 4 * tile_rows]
            coh = jnp.sqrt(real_mean * real_mean + imag_mean * imag_mean) / jnp.sqrt(
                pre_power * post_power
            )
            coh_ref[p, :, pl.ds(j * LANES, LANES)] = coh
            chg_ref[p, :, pl.ds(j * LANES, LANES)] = jnp.log(post_power / pre_power)


def pair_maps(filtered, pre_ids, post_ids, tile_rows, tile_cols):
    count_pairs = pre_ids.shape[0]
    pp = PAIRS_PER_STEP
    padded_rows, padded_cols = filtered.shape[2:]
    width = 3 * LANES
    lane_in = jnp.arange(width)[:, None]
    lane_out = jnp.arange(LANES)[None, :]
    gap = lane_in - LANES - lane_out
    band = jnp.where((gap >= -RADIUS) & (gap <= RADIUS), 1.0, 0.0).astype(jnp.bfloat16)
    band = jnp.concatenate([band, band], axis=0)
    block = (1, 2, padded_rows, padded_cols)

    def side_spec(p, which):
        def index(i, pre, post):
            ids = pre if which == 0 else post
            return (ids[i * pp + p], 0, 0, 0)

        return pl.BlockSpec(block, index)

    in_specs = []
    operands = []
    for p in range(pp):
        in_specs += [side_spec(p, 0), side_spec(p, 1)]
        operands += [filtered, filtered]
    in_specs.append(pl.BlockSpec((2 * width, LANES), lambda i, pre, post: (0, 0)))
    operands.append(band)
    out_block = pl.BlockSpec((pp, tile_rows, tile_cols), lambda i, pre, post: (i, 0, 0))
    rows = pp * FIELDS * tile_rows
    blocks = tile_cols // LANES
    grid_spec = pltpu.PrefetchScalarGridSpec(
        num_scalar_prefetch=2,
        grid=(count_pairs // pp,),
        in_specs=in_specs,
        out_specs=[out_block, out_block],
        scratch_shapes=[
            pltpu.VMEM((padded_rows, padded_cols), jnp.float32),
            pltpu.VMEM((rows, padded_cols + LANES), jnp.float32),
            pltpu.VMEM((blocks * rows, 2 * width), jnp.bfloat16),
        ],
    )
    out_shape = jax.ShapeDtypeStruct((count_pairs, tile_rows, tile_cols), jnp.float32)
    kernel = functools.partial(pair_kernel, tile_rows=tile_rows, tile_cols=tile_cols)
    return pl.pallas_call(
        kernel,
        grid_spec=grid_spec,
        out_shape=[out_shape, out_shape],
    )(pre_ids, post_ids, *operands)


def shards(stack, filt_re, filt_im, pre_ids, post_ids):
    count_acq = filt_re.shape[0]
    n_rows = lax.axis_size("ty")
    n_cols = lax.axis_size("tx")
    local_acq, _, height, local_cols = stack.shape
    tile_rows = height // n_rows
    blocks_per_tile = n_rows // n_cols
    tile_cols = local_cols * blocks_per_tile

    x = stack.reshape(local_acq, 2, n_rows, tile_rows, local_cols)
    x = jnp.transpose(x, (2, 0, 1, 3, 4))
    x = lax.all_to_all(x, "ty", 0, 0, tiled=True)
    x = x.reshape(n_cols, blocks_per_tile, local_acq, 2, tile_rows, local_cols)
    x = lax.all_to_all(x, "tx", 0, 0, tiled=True)
    x = jnp.transpose(x, (0, 2, 3, 4, 1, 5))
    x = x.reshape(2 * count_acq, tile_rows, tile_cols)

    halos = with_halo(x, (("ty", 1), ("tx", 2)), RADIUS)
    top, bottom = next(halos)
    x = jnp.concatenate([top, x, bottom], axis=1)
    left, right = next(halos)
    gap = jnp.zeros((2 * count_acq, x.shape[1], LANES - 2 * RADIUS), x.dtype)
    x = jnp.concatenate([x, right, gap, left], axis=2)

    mixing = jnp.stack([jnp.stack([filt_re, -filt_im], -1), jnp.stack([filt_im, filt_re], -1)], 1)
    mixing = mixing.reshape(2 * count_acq, 2 * count_acq)
    result = jnp.einsum("kc,chw->khw", mixing, x, preferred_element_type=jnp.float32)
    filtered = result.astype(jnp.bfloat16).reshape(count_acq, 2, *x.shape[1:])
    return pair_maps(filtered, pre_ids, post_ids, tile_rows, tile_cols)


def solution(mesh):
    in_specs = (P("tx", None, None, "ty"), P(), P(), P(), P())
    out_specs = (P(None, "ty", "tx"), P(None, "ty", "tx"))
    return jax.shard_map(shards, mesh=mesh, in_specs=in_specs, out_specs=out_specs, check_vma=False)
```

```python
import functools

import jax
import jax.numpy as jnp
from jax import lax
from jax.experimental import pallas as pl
from jax.experimental.pallas import tpu as pltpu
from jax.sharding import PartitionSpec as P

RADIUS = 4
LANES = 128
PAIRS_PER_STEP = 2
FIELDS = 4


def with_halo(block, sides, width):
    for axis, dim in sides:
        count = lax.axis_size(axis)
        forward = [(i, i + 1) for i in range(count - 1)]
        backward = [(target, source) for source, target in forward]
        low = lax.ppermute(
            lax.slice_in_dim(block, block.shape[dim] - width, None, axis=dim), axis, forward
        )
        high = lax.ppermute(lax.slice_in_dim(block, 0, width, axis=dim), axis, backward)
        yield low, high
        block = jnp.concatenate([low, block, high], axis=dim)


def pair_kernel(pre_ref, post_ref, *refs, tile_rows, tile_cols):
    del pre_ref, post_ref
    pp = PAIRS_PER_STEP
    sides = refs[: 2 * pp]
    band_ref, coh_ref, chg_ref, field_ref, rows_ref, stack_ref = refs[2 * pp :]
    window = 2 * RADIUS + 1
    padded_cols = tile_cols + LANES
    rows = pp * FIELDS * tile_rows
    blocks = tile_cols // LANES
    for p in range(pp):
        a = sides[2 * p]
        b = sides[2 * p + 1]
        pr = a[0, 0].astype(jnp.float32)
        pi = a[0, 1].astype(jnp.float32)
        qr = b[0, 0].astype(jnp.float32)
        qi = b[0, 1].astype(jnp.float32)
        fields = (pr * pr + pi * pi, qr * qr + qi * qi, pr * qr + pi * qi, pi * qr - pr * qi)
        for f, value in enumerate(fields):
            field_ref[...] = value
            acc = field_ref[pl.ds(0, tile_rows), :]
            for k in range(1, window):
                acc = acc + field_ref[pl.ds(k, tile_rows), :]
            at = (p * FIELDS + f) * tile_rows
            rows_ref[pl.ds(at, tile_rows), pl.ds(LANES, padded_cols)] = acc
            rows_ref[pl.ds(at, tile_rows), pl.ds(0, LANES)] = acc[:, padded_cols - LANES :]
    rowsum = rows_ref[...]
    high = rowsum.astype(jnp.bfloat16)
    low = (rowsum - high.astype(jnp.float32)).astype(jnp.bfloat16)
    width = 3 * LANES
    for j in range(blocks):
        stack_ref[pl.ds(j * rows, rows), pl.ds(0, width)] = high[:, j * LANES : j * LANES + width]
        stack_ref[pl.ds(j * rows, rows), pl.ds(width, width)] = low[:, j * LANES : j * LANES + width]
    sums = jnp.dot(stack_ref[...], band_ref[...], preferred_element_type=jnp.float32)
    means = sums / float(window * window)
    for j in range(blocks):
        for p in range(pp):
            base = j * rows + p * FIELDS * tile_rows
            pre_power = means[base : base + tile_rows] + 1e-06
            post_power = means[base + tile_rows : base + 2 * tile_rows] + 1e-06
            real_mean = means[base + 2 * tile_rows : base + 3 * tile_rows]
            imag_mean = means[base + 3 * tile_rows : base + 4 * tile_rows]
            coh = jnp.sqrt(real_mean * real_mean + imag_mean * imag_mean) / jnp.sqrt(
                pre_power * post_power
            )
            coh_ref[p, :, pl.ds(j * LANES, LANES)] = coh
            chg_ref[p, :, pl.ds(j * LANES, LANES)] = jnp.log(post_power / pre_power)


def pair_maps(filtered, pre_ids, post_ids, tile_rows, tile_cols):
    count_pairs = pre_ids.shape[0]
    pp = PAIRS_PER_STEP
    padded_rows, padded_cols = filtered.shape[2:]
    width = 3 * LANES
    lane_in = jnp.arange(width)[:, None]
    lane_out = jnp.arange(LANES)[None, :]
    gap = lane_in - LANES - lane_out
    band = jnp.where((gap >= -RADIUS) & (gap <= RADIUS), 1.0, 0.0).astype(jnp.bfloat16)
    band = jnp.concatenate([band, band], axis=0)
    block = (1, 2, padded_rows, padded_cols)

    def side_spec(p, which):
        def index(i, pre, post):
            ids = pre if which == 0 else post
            return (ids[i * pp + p], 0, 0, 0)

        return pl.BlockSpec(block, index)

    in_specs = []
    operands = []
    for p in range(pp):
        in_specs += [side_spec(p, 0), side_spec(p, 1)]
        operands += [filtered, filtered]
    in_specs.append(pl.BlockSpec((2 * width, LANES), lambda i, pre, post: (0, 0)))
    operands.append(band)
    out_block = pl.BlockSpec((pp, tile_rows, tile_cols), lambda i, pre, post: (i, 0, 0))
    rows = pp * FIELDS * tile_rows
    blocks = tile_cols // LANES
    grid_spec = pltpu.PrefetchScalarGridSpec(
        num_scalar_prefetch=2,
        grid=(count_pairs // pp,),
        in_specs=in_specs,
        out_specs=[out_block, out_block],
        scratch_shapes=[
            pltpu.VMEM((padded_rows, padded_cols), jnp.float32),
            pltpu.VMEM((rows, padded_cols + LANES), jnp.float32),
            pltpu.VMEM((blocks * rows, 2 * width), jnp.bfloat16),
        ],
    )
    out_shape = jax.ShapeDtypeStruct((count_pairs, tile_rows, tile_cols), jnp.float32)
    kernel = functools.partial(pair_kernel, tile_rows=tile_rows, tile_cols=tile_cols)
    return pl.pallas_call(
        kernel,
        grid_spec=grid_spec,
        out_shape=[out_shape, out_shape],
    )(pre_ids, post_ids, *operands)


def shards(stack, filt_re, filt_im, pre_ids, post_ids):
    count_acq = filt_re.shape[0]
    n_rows = lax.axis_size("ty")
    n_cols = lax.axis_size("tx")
    local_acq, _, height, local_cols = stack.shape
    tile_rows = height // n_rows
    blocks_per_tile = n_rows // n_cols
    tile_cols = local_cols * blocks_per_tile

    me_col = lax.axis_index("tx")
    me_row = lax.axis_index("ty")
    x = stack.reshape(local_acq, 2, n_rows, tile_rows, local_cols)
    x = jnp.transpose(x, (2, 0, 1, 3, 4))
    start = me_col * blocks_per_tile + me_row % blocks_per_tile
    received = []
    for m in range(n_rows):
        pairs = []
        for col in range(n_cols):
            for row in range(n_rows):
                to_row = (m + col * blocks_per_tile + row % blocks_per_tile) % n_rows
                pairs.append((col * n_rows + row, (row // blocks_per_tile) * n_rows + to_row))
        chunk = lax.dynamic_index_in_dim(x, (start + m) % n_rows, axis=0, keepdims=False)
        received.append(lax.ppermute(chunk, ("tx", "ty"), pairs))
    received = jnp.stack(received, axis=0)
    order = (me_row - jnp.arange(n_rows)) % n_rows
    x = jnp.take(received, order, axis=0)
    x = x.reshape(n_cols, blocks_per_tile, local_acq, 2, tile_rows, local_cols)
    x = jnp.transpose(x, (0, 2, 3, 4, 1, 5))
    x = x.reshape(2 * count_acq, tile_rows, tile_cols)

    halos = with_halo(x, (("ty", 1), ("tx", 2)), RADIUS)
    top, bottom = next(halos)
    x = jnp.concatenate([top, x, bottom], axis=1)
    left, right = next(halos)
    gap = jnp.zeros((2 * count_acq, x.shape[1], LANES - 2 * RADIUS), x.dtype)
    x = jnp.concatenate([x, right, gap, left], axis=2)

    mixing = jnp.stack([jnp.stack([filt_re, -filt_im], -1), jnp.stack([filt_im, filt_re], -1)], 1)
    mixing = mixing.reshape(2 * count_acq, 2 * count_acq)
    result = jnp.einsum("kc,chw->khw", mixing, x, preferred_element_type=jnp.float32)
    filtered = result.astype(jnp.bfloat16).reshape(count_acq, 2, *x.shape[1:])
    return pair_maps(filtered, pre_ids, post_ids, tile_rows, tile_cols)


def solution(mesh):
    in_specs = (P("tx", None, None, "ty"), P(), P(), P(), P())
    out_specs = (P(None, "ty", "tx"), P(None, "ty", "tx"))
    return jax.shard_map(shards, mesh=mesh, in_specs=in_specs, out_specs=out_specs, check_vma=False)
```

```python
import functools

import jax
import jax.numpy as jnp
from jax import lax
from jax.experimental import pallas as pl
from jax.experimental.pallas import tpu as pltpu
from jax.sharding import PartitionSpec as P

RADIUS = 4
LANES = 128
PAIRS_PER_STEP = 2
FIELDS = 4


def pair_kernel(pre_ref, post_ref, *refs, tile_rows, tile_cols):
    del pre_ref, post_ref
    pp = PAIRS_PER_STEP
    sides = refs[: 4 * pp]
    band_ref, coh_ref, chg_ref, field_ref, rows_ref, stack_ref = refs[4 * pp :]
    window = 2 * RADIUS + 1
    padded_cols = tile_cols + LANES
    rows = pp * FIELDS * tile_rows
    blocks = tile_cols // LANES
    for p in range(pp):
        a_main, a_edge, b_main, b_edge = sides[4 * p : 4 * p + 4]
        pieces = [(c * a_main.shape[-1], a_main[c, 0], b_main[c, 0]) for c in range(a_main.shape[0])]
        pieces.append((tile_cols, a_edge[0], b_edge[0]))
        for at, a, b in pieces:
            width = a.shape[-1]
            pr = a[0].astype(jnp.float32)
            pi = a[1].astype(jnp.float32)
            qr = b[0].astype(jnp.float32)
            qi = b[1].astype(jnp.float32)
            fields = (pr * pr + pi * pi, qr * qr + qi * qi, pr * qr + pi * qi, pi * qr - pr * qi)
            for f, value in enumerate(fields):
                field_ref[f, :, pl.ds(at, width)] = value
        for f in range(FIELDS):
            acc = field_ref[f, pl.ds(0, tile_rows), :]
            for k in range(1, window):
                acc = acc + field_ref[f, pl.ds(k, tile_rows), :]
            at = (p * FIELDS + f) * tile_rows
            rows_ref[pl.ds(at, tile_rows), pl.ds(LANES, padded_cols)] = acc
            rows_ref[pl.ds(at, tile_rows), pl.ds(0, LANES)] = acc[:, padded_cols - LANES :]
    rowsum = rows_ref[...]
    high = rowsum.astype(jnp.bfloat16)
    low = (rowsum - high.astype(jnp.float32)).astype(jnp.bfloat16)
    width = 3 * LANES
    for j in range(blocks):
        stack_ref[pl.ds(j * rows, rows), pl.ds(0, width)] = high[:, j * LANES : j * LANES + width]
        stack_ref[pl.ds(j * rows, rows), pl.ds(width, width)] = low[:, j * LANES : j * LANES + width]
    sums = jnp.dot(stack_ref[...], band_ref[...], preferred_element_type=jnp.float32)
    means = sums / float(window * window)
    for j in range(blocks):
        for p in range(pp):
            base = j * rows + p * FIELDS * tile_rows
            pre_power = means[base : base + tile_rows] + 1e-06
            post_power = means[base + tile_rows : base + 2 * tile_rows] + 1e-06
            real_mean = means[base + 2 * tile_rows : base + 3 * tile_rows]
            imag_mean = means[base + 3 * tile_rows : base + 4 * tile_rows]
            coh = jnp.sqrt(real_mean * real_mean + imag_mean * imag_mean) / jnp.sqrt(
                pre_power * post_power
            )
            coh_ref[p, :, pl.ds(j * LANES, LANES)] = coh
            chg_ref[p, :, pl.ds(j * LANES, LANES)] = jnp.log(post_power / pre_power)


def pair_maps(main, edge, pre_ids, post_ids, tile_rows, tile_cols):
    count_pairs = pre_ids.shape[0]
    pp = PAIRS_PER_STEP
    blocks_per_tile, _, _, padded_rows, block_cols = main.shape
    width = 3 * LANES
    lane_in = jnp.arange(width)[:, None]
    lane_out = jnp.arange(LANES)[None, :]
    gap = lane_in - LANES - lane_out
    band = jnp.where((gap >= -RADIUS) & (gap <= RADIUS), 1.0, 0.0).astype(jnp.bfloat16)
    band = jnp.concatenate([band, band], axis=0)
    main_block = (blocks_per_tile, 1, 2, padded_rows, block_cols)
    edge_block = (1, 2, padded_rows, LANES)

    def specs(p, which):
        def main_index(i, pre, post):
            ids = pre if which == 0 else post
            return (0, ids[i * pp + p], 0, 0, 0)

        def edge_index(i, pre, post):
            ids = pre if which == 0 else post
            return (ids[i * pp + p], 0, 0, 0)

        return [pl.BlockSpec(main_block, main_index), pl.BlockSpec(edge_block, edge_index)]

    in_specs = []
    operands = []
    for p in range(pp):
        in_specs += specs(p, 0) + specs(p, 1)
        operands += [main, edge, main, edge]
    in_specs.append(pl.BlockSpec((2 * width, LANES), lambda i, pre, post: (0, 0)))
    operands.append(band)
    out_block = pl.BlockSpec((pp, tile_rows, tile_cols), lambda i, pre, post: (i, 0, 0))
    rows = pp * FIELDS * tile_rows
    blocks = tile_cols // LANES
    padded_cols = tile_cols + LANES
    grid_spec = pltpu.PrefetchScalarGridSpec(
        num_scalar_prefetch=2,
        grid=(count_pairs // pp,),
        in_specs=in_specs,
        out_specs=[out_block, out_block],
        scratch_shapes=[
            pltpu.VMEM((FIELDS, padded_rows, padded_cols), jnp.float32),
            pltpu.VMEM((rows, padded_cols + LANES), jnp.float32),
            pltpu.VMEM((blocks * rows, 2 * width), jnp.bfloat16),
        ],
    )
    out_shape = jax.ShapeDtypeStruct((count_pairs, tile_rows, tile_cols), jnp.float32)
    kernel = functools.partial(pair_kernel, tile_rows=tile_rows, tile_cols=tile_cols)
    return pl.pallas_call(
        kernel,
        grid_spec=grid_spec,
        out_shape=[out_shape, out_shape],
    )(pre_ids, post_ids, *operands)


def shards(stack, filt_re, filt_im, pre_ids, post_ids):
    count_acq = filt_re.shape[0]
    n_rows = lax.axis_size("ty")
    n_cols = lax.axis_size("tx")
    local_acq, _, height, local_cols = stack.shape
    tile_rows = height // n_rows
    blocks_per_tile = n_rows // n_cols
    tile_cols = local_cols * blocks_per_tile
    padded_rows = tile_rows + 2 * RADIUS

    me_col = lax.axis_index("tx")
    me_row = lax.axis_index("ty")
    x = jnp.pad(stack, ((0, 0), (0, 0), (RADIUS, RADIUS), (0, 0)))
    start = me_col * blocks_per_tile + me_row % blocks_per_tile
    received = []
    for m in range(n_rows):
        pairs = []
        for col in range(n_cols):
            for row in range(n_rows):
                to_row = (m + col * blocks_per_tile + row % blocks_per_tile) % n_rows
                pairs.append((col * n_rows + row, (row // blocks_per_tile) * n_rows + to_row))
        first = ((start + m) % n_rows) * tile_rows
        chunk = lax.dynamic_slice_in_dim(x, first, padded_rows, axis=2)
        received.append(lax.ppermute(chunk, ("tx", "ty"), pairs))
    received = jnp.stack(received, axis=0)
    source = jnp.arange(blocks_per_tile)[:, None] + blocks_per_tile * jnp.arange(n_cols)[None, :]
    order = (me_row - source) % n_rows
    x = jnp.take(received, order.reshape(-1), axis=0)
    x = x.reshape(blocks_per_tile, 2 * count_acq, padded_rows, local_cols)

    forward = [(i, i + 1) for i in range(n_cols - 1)]
    backward = [(target, source) for source, target in forward]
    left = lax.ppermute(x[blocks_per_tile - 1, :, :, local_cols - RADIUS :], "tx", forward)
    right = lax.ppermute(x[0, :, :, :RADIUS], "tx", backward)
    gap = jnp.zeros((2 * count_acq, padded_rows, LANES - 2 * RADIUS), x.dtype)
    edge = jnp.concatenate([right, gap, left], axis=2)

    mixing = jnp.stack([jnp.stack([filt_re, -filt_im], -1), jnp.stack([filt_im, filt_re], -1)], 1)
    mixing = mixing.reshape(2 * count_acq, 2 * count_acq)
    main = jnp.einsum("kc,bchw->bkhw", mixing, x, preferred_element_type=jnp.float32)
    main = main.astype(jnp.bfloat16).reshape(blocks_per_tile, count_acq, 2, padded_rows, local_cols)
    edge = jnp.einsum("kc,chw->khw", mixing, edge, preferred_element_type=jnp.float32)
    edge = edge.astype(jnp.bfloat16).reshape(count_acq, 2, padded_rows, LANES)
    return pair_maps(main, edge, pre_ids, post_ids, tile_rows, tile_cols)


def solution(mesh):
    in_specs = (P("tx", None, None, "ty"), P(), P(), P(), P())
    out_specs = (P(None, "ty", "tx"), P(None, "ty", "tx"))
    return jax.shard_map(shards, mesh=mesh, in_specs=in_specs, out_specs=out_specs, check_vma=False)
```

```python
import functools

import jax
import jax.numpy as jnp
from jax import lax
from jax.experimental import pallas as pl
from jax.experimental.pallas import tpu as pltpu
from jax.sharding import PartitionSpec as P

RADIUS = 4
LANES = 128
PAIRS_PER_STEP = 4
FIELDS = 4


def pair_kernel(pre_ref, post_ref, *refs, tile_rows, tile_cols):
    del pre_ref, post_ref
    pp = PAIRS_PER_STEP
    sides = refs[: 4 * pp]
    band_ref, coh_ref, chg_ref, field_ref, rows_ref, stack_ref = refs[4 * pp :]
    window = 2 * RADIUS + 1
    padded_cols = tile_cols + LANES
    rows = pp * FIELDS * tile_rows
    blocks = tile_cols // LANES
    for p in range(pp):
        a_main, a_edge, b_main, b_edge = sides[4 * p : 4 * p + 4]
        pieces = [(c * a_main.shape[-1], a_main[c, 0], b_main[c, 0]) for c in range(a_main.shape[0])]
        pieces.append((tile_cols, a_edge[0], b_edge[0]))
        for at, a, b in pieces:
            width = a.shape[-1]
            pr = a[0].astype(jnp.float32)
            pi = a[1].astype(jnp.float32)
            qr = b[0].astype(jnp.float32)
            qi = b[1].astype(jnp.float32)
            fields = (pr * pr + pi * pi, qr * qr + qi * qi, pr * qr + pi * qi, pi * qr - pr * qi)
            for f, value in enumerate(fields):
                field_ref[f, :, pl.ds(at, width)] = value
        for f in range(FIELDS):
            acc = field_ref[f, pl.ds(0, tile_rows), :]
            for k in range(1, window):
                acc = acc + field_ref[f, pl.ds(k, tile_rows), :]
            at = (p * FIELDS + f) * tile_rows
            rows_ref[pl.ds(at, tile_rows), pl.ds(LANES, padded_cols)] = acc
            rows_ref[pl.ds(at, tile_rows), pl.ds(0, LANES)] = acc[:, padded_cols - LANES :]
    rowsum = rows_ref[...]
    high = rowsum.astype(jnp.bfloat16)
    low = (rowsum - high.astype(jnp.float32)).astype(jnp.bfloat16)
    width = 3 * LANES
    for j in range(blocks):
        stack_ref[pl.ds(j * rows, rows), pl.ds(0, width)] = high[:, j * LANES : j * LANES + width]
        stack_ref[pl.ds(j * rows, rows), pl.ds(width, width)] = low[:, j * LANES : j * LANES + width]
    sums = jnp.dot(stack_ref[...], band_ref[...], preferred_element_type=jnp.float32)
    means = sums / float(window * window)
    for j in range(blocks):
        for p in range(pp):
            base = j * rows + p * FIELDS * tile_rows
            pre_power = means[base : base + tile_rows] + 1e-06
            post_power = means[base + tile_rows : base + 2 * tile_rows] + 1e-06
            real_mean = means[base + 2 * tile_rows : base + 3 * tile_rows]
            imag_mean = means[base + 3 * tile_rows : base + 4 * tile_rows]
            coh = jnp.sqrt(real_mean * real_mean + imag_mean * imag_mean) / jnp.sqrt(
                pre_power * post_power
            )
            coh_ref[p, :, pl.ds(j * LANES, LANES)] = coh
            chg_ref[p, :, pl.ds(j * LANES, LANES)] = jnp.log(post_power / pre_power)


def pair_maps(main, edge, pre_ids, post_ids, tile_rows, tile_cols):
    count_pairs = pre_ids.shape[0]
    pp = PAIRS_PER_STEP
    blocks_per_tile, _, _, padded_rows, block_cols = main.shape
    width = 3 * LANES
    lane_in = jnp.arange(width)[:, None]
    lane_out = jnp.arange(LANES)[None, :]
    gap = lane_in - LANES - lane_out
    band = jnp.where((gap >= -RADIUS) & (gap <= RADIUS), 1.0, 0.0).astype(jnp.bfloat16)
    band = jnp.concatenate([band, band], axis=0)
    main_block = (blocks_per_tile, 1, 2, padded_rows, block_cols)
    edge_block = (1, 2, padded_rows, LANES)

    def specs(p, which):
        def main_index(i, pre, post):
            ids = pre if which == 0 else post
            return (0, ids[i * pp + p], 0, 0, 0)

        def edge_index(i, pre, post):
            ids = pre if which == 0 else post
            return (ids[i * pp + p], 0, 0, 0)

        return [pl.BlockSpec(main_block, main_index), pl.BlockSpec(edge_block, edge_index)]

    in_specs = []
    operands = []
    for p in range(pp):
        in_specs += specs(p, 0) + specs(p, 1)
        operands += [main, edge, main, edge]
    in_specs.append(pl.BlockSpec((2 * width, LANES), lambda i, pre, post: (0, 0)))
    operands.append(band)
    out_block = pl.BlockSpec((pp, tile_rows, tile_cols), lambda i, pre, post: (i, 0, 0))
    rows = pp * FIELDS * tile_rows
    blocks = tile_cols // LANES
    padded_cols = tile_cols + LANES
    grid_spec = pltpu.PrefetchScalarGridSpec(
        num_scalar_prefetch=2,
        grid=(count_pairs // pp,),
        in_specs=in_specs,
        out_specs=[out_block, out_block],
        scratch_shapes=[
            pltpu.VMEM((FIELDS, padded_rows, padded_cols), jnp.float32),
            pltpu.VMEM((rows, padded_cols + LANES), jnp.float32),
            pltpu.VMEM((blocks * rows, 2 * width), jnp.bfloat16),
        ],
    )
    out_shape = jax.ShapeDtypeStruct((count_pairs, tile_rows, tile_cols), jnp.float32)
    kernel = functools.partial(pair_kernel, tile_rows=tile_rows, tile_cols=tile_cols)
    return pl.pallas_call(
        kernel,
        grid_spec=grid_spec,
        out_shape=[out_shape, out_shape],
    )(pre_ids, post_ids, *operands)


def shards(stack, filt_re, filt_im, pre_ids, post_ids):
    count_acq = filt_re.shape[0]
    n_rows = lax.axis_size("ty")
    n_cols = lax.axis_size("tx")
    local_acq, _, height, local_cols = stack.shape
    tile_rows = height // n_rows
    blocks_per_tile = n_rows // n_cols
    tile_cols = local_cols * blocks_per_tile
    padded_rows = tile_rows + 2 * RADIUS

    me_col = lax.axis_index("tx")
    me_row = lax.axis_index("ty")
    x = jnp.pad(stack, ((0, 0), (0, 0), (RADIUS, RADIUS), (0, 0)))
    start = me_col * blocks_per_tile + me_row % blocks_per_tile
    received = []
    for m in range(n_rows):
        pairs = []
        for col in range(n_cols):
            for row in range(n_rows):
                to_row = (m + col * blocks_per_tile + row % blocks_per_tile) % n_rows
                pairs.append((col * n_rows + row, (row // blocks_per_tile) * n_rows + to_row))
        first = ((start + m) % n_rows) * tile_rows
        chunk = lax.dynamic_slice_in_dim(x, first, padded_rows, axis=2)
        received.append(lax.ppermute(chunk, ("tx", "ty"), pairs))
    received = jnp.stack(received, axis=0)
    source = jnp.arange(blocks_per_tile)[:, None] + blocks_per_tile * jnp.arange(n_cols)[None, :]
    order = (me_row - source) % n_rows
    x = jnp.take(received, order.reshape(-1), axis=0)
    x = x.reshape(blocks_per_tile, 2 * count_acq, padded_rows, local_cols)

    forward = [(i, i + 1) for i in range(n_cols - 1)]
    backward = [(target, source) for source, target in forward]
    left = lax.ppermute(x[blocks_per_tile - 1, :, :, local_cols - RADIUS :], "tx", forward)
    right = lax.ppermute(x[0, :, :, :RADIUS], "tx", backward)
    gap = jnp.zeros((2 * count_acq, padded_rows, LANES - 2 * RADIUS), x.dtype)
    edge = jnp.concatenate([right, gap, left], axis=2)

    mixing = jnp.stack([jnp.stack([filt_re, -filt_im], -1), jnp.stack([filt_im, filt_re], -1)], 1)
    mixing = mixing.reshape(2 * count_acq, 2 * count_acq)
    main = jnp.einsum("kc,bchw->bkhw", mixing, x, preferred_element_type=jnp.float32)
    main = main.astype(jnp.bfloat16).reshape(blocks_per_tile, count_acq, 2, padded_rows, local_cols)
    edge = jnp.einsum("kc,chw->khw", mixing, edge, preferred_element_type=jnp.float32)
    edge = edge.astype(jnp.bfloat16).reshape(count_acq, 2, padded_rows, LANES)
    return pair_maps(main, edge, pre_ids, post_ids, tile_rows, tile_cols)


def solution(mesh):
    in_specs = (P("tx", None, None, "ty"), P(), P(), P(), P())
    out_specs = (P(None, "ty", "tx"), P(None, "ty", "tx"))
    return jax.shard_map(shards, mesh=mesh, in_specs=in_specs, out_specs=out_specs, check_vma=False)
```

```python
import functools

import jax
import jax.numpy as jnp
from jax import lax
from jax.experimental import pallas as pl
from jax.experimental.pallas import tpu as pltpu
from jax.sharding import PartitionSpec as P

RADIUS = 4
LANES = 128
PAIRS_PER_STEP = 4
ACQ_PER_STEP = 4
FIELDS = 4


def assemble(field_ref, sides, fields_of, tile_cols):
    count = 0
    for main, edge in sides:
        pieces = [(c * main[0].shape[-1], [m[c, 0] for m in main]) for c in range(main[0].shape[0])]
        pieces.append((tile_cols, [e[0] for e in edge]))
        for at, parts in pieces:
            width = parts[0].shape[-1]
            values = fields_of(*[(part[0].astype(jnp.float32), part[1].astype(jnp.float32)) for part in parts])
            for f, value in enumerate(values):
                field_ref[count + f, :, pl.ds(at, width)] = value
        count += len(values)
    return count


def box_means(field_ref, rows_ref, band_ref, count, tile_rows, tile_cols):
    window = 2 * RADIUS + 1
    padded_cols = tile_cols + LANES
    for f in range(count):
        acc = field_ref[f, pl.ds(0, tile_rows), :]
        for k in range(1, window):
            acc = acc + field_ref[f, pl.ds(k, tile_rows), :]
        rows_ref[pl.ds(f * tile_rows, tile_rows), pl.ds(LANES, padded_cols)] = acc
        rows_ref[pl.ds(f * tile_rows, tile_rows), pl.ds(0, LANES)] = acc[:, padded_cols - LANES :]
    rowsum = rows_ref[pl.ds(0, count * tile_rows), :]
    high = rowsum.astype(jnp.bfloat16)
    low = (rowsum - high.astype(jnp.float32)).astype(jnp.bfloat16)
    band = band_ref[...]
    width = 3 * LANES
    for j in range(tile_cols // LANES):
        sums = jnp.dot(high[:, j * LANES : j * LANES + width], band, preferred_element_type=jnp.float32)
        sums = sums + jnp.dot(low[:, j * LANES : j * LANES + width], band, preferred_element_type=jnp.float32)
        yield j, sums / float(window * window)


def power_fields(side):
    re, im = side
    return (re * re + im * im,)


def cross_fields(pre, post):
    pr, pi = pre
    qr, qi = post
    return (pr * qr + pi * qi, pi * qr - pr * qi)


def power_kernel(main_ref, edge_ref, band_ref, out_ref, field_ref, rows_ref, *, tile_rows, tile_cols):
    step = main_ref.shape[1]
    sides = [([main_ref.at[:, a : a + 1]], [edge_ref.at[a : a + 1]]) for a in range(step)]
    count = assemble(field_ref, sides, power_fields, tile_cols)
    for j, means in box_means(field_ref, rows_ref, band_ref, count, tile_rows, tile_cols):
        for a in range(step):
            out_ref[a, :, pl.ds(j * LANES, LANES)] = means[a * tile_rows : (a + 1) * tile_rows] + 1e-06


def pair_kernel(pre_ref, post_ref, *refs, tile_rows, tile_cols):
    del pre_ref, post_ref
    pp = PAIRS_PER_STEP
    sides = refs[: 6 * pp]
    band_ref, coh_ref, chg_ref, field_ref, rows_ref = refs[6 * pp :]
    count = 0
    for p in range(pp):
        a_main, a_edge, b_main, b_edge = sides[6 * p : 6 * p + 4]
        count += assemble(field_ref.at[count:], [([a_main, b_main], [a_edge, b_edge])], cross_fields, tile_cols)
    for j, means in box_means(field_ref, rows_ref, band_ref, count, tile_rows, tile_cols):
        for p in range(pp):
            pre_power = sides[6 * p + 4][0, :, pl.ds(j * LANES, LANES)]
            post_power = sides[6 * p + 5][0, :, pl.ds(j * LANES, LANES)]
            base = 2 * p * tile_rows
            real_mean = means[base : base + tile_rows]
            imag_mean = means[base + tile_rows : base + 2 * tile_rows]
            coh = jnp.sqrt(real_mean * real_mean + imag_mean * imag_mean) / jnp.sqrt(
                pre_power * post_power
            )
            coh_ref[p, :, pl.ds(j * LANES, LANES)] = coh
            chg_ref[p, :, pl.ds(j * LANES, LANES)] = jnp.log(post_power / pre_power)


def make_band():
    width = 3 * LANES
    lane_in = jnp.arange(width)[:, None]
    lane_out = jnp.arange(LANES)[None, :]
    gap = lane_in - LANES - lane_out
    return jnp.where((gap >= -RADIUS) & (gap <= RADIUS), 1.0, 0.0).astype(jnp.bfloat16)


def pair_maps(main, edge, pre_ids, post_ids, tile_rows, tile_cols):
    count_pairs = pre_ids.shape[0]
    pp = PAIRS_PER_STEP
    blocks_per_tile, count_acq, _, padded_rows, block_cols = main.shape
    band = make_band()
    padded_cols = tile_cols + LANES
    width = 3 * LANES

    ap = ACQ_PER_STEP
    power = pl.pallas_call(
        functools.partial(power_kernel, tile_rows=tile_rows, tile_cols=tile_cols),
        grid=(count_acq // ap,),
        in_specs=[
            pl.BlockSpec((blocks_per_tile, ap, 2, padded_rows, block_cols), lambda i: (0, i, 0, 0, 0)),
            pl.BlockSpec((ap, 2, padded_rows, LANES), lambda i: (i, 0, 0, 0)),
            pl.BlockSpec((width, LANES), lambda i: (0, 0)),
        ],
        out_specs=pl.BlockSpec((ap, tile_rows, tile_cols), lambda i: (i, 0, 0)),
        out_shape=jax.ShapeDtypeStruct((count_acq, tile_rows, tile_cols), jnp.float32),
        scratch_shapes=[
            pltpu.VMEM((ap, padded_rows, padded_cols), jnp.float32),
            pltpu.VMEM((ap * tile_rows, padded_cols + LANES), jnp.float32),
        ],
    )(main, edge, band)

    main_block = (blocks_per_tile, 1, 2, padded_rows, block_cols)
    edge_block = (1, 2, padded_rows, LANES)
    power_block = (1, tile_rows, tile_cols)

    def specs(p):
        return [
            pl.BlockSpec(main_block, lambda i, pre, post: (0, pre[i * pp + p], 0, 0, 0)),
            pl.BlockSpec(edge_block, lambda i, pre, post: (pre[i * pp + p], 0, 0, 0)),
            pl.BlockSpec(main_block, lambda i, pre, post: (0, post[i * pp + p], 0, 0, 0)),
            pl.BlockSpec(edge_block, lambda i, pre, post: (post[i * pp + p], 0, 0, 0)),
            pl.BlockSpec(power_block, lambda i, pre, post: (pre[i * pp + p], 0, 0)),
            pl.BlockSpec(power_block, lambda i, pre, post: (post[i * pp + p], 0, 0)),
        ]

    in_specs = []
    operands = []
    for p in range(pp):
        in_specs += specs(p)
        operands += [main, edge, main, edge, power, power]
    in_specs.append(pl.BlockSpec((width, LANES), lambda i, pre, post: (0, 0)))
    operands.append(band)
    out_block = pl.BlockSpec((pp, tile_rows, tile_cols), lambda i, pre, post: (i, 0, 0))
    grid_spec = pltpu.PrefetchScalarGridSpec(
        num_scalar_prefetch=2,
        grid=(count_pairs // pp,),
        in_specs=in_specs,
        out_specs=[out_block, out_block],
        scratch_shapes=[
            pltpu.VMEM((2 * pp, padded_rows, padded_cols), jnp.float32),
            pltpu.VMEM((2 * pp * tile_rows, padded_cols + LANES), jnp.float32),
        ],
    )
    out_shape = jax.ShapeDtypeStruct((count_pairs, tile_rows, tile_cols), jnp.float32)
    kernel = functools.partial(pair_kernel, tile_rows=tile_rows, tile_cols=tile_cols)
    return pl.pallas_call(
        kernel,
        grid_spec=grid_spec,
        out_shape=[out_shape, out_shape],
    )(pre_ids, post_ids, *operands)


def shards(stack, filt_re, filt_im, pre_ids, post_ids):
    count_acq = filt_re.shape[0]
    n_rows = lax.axis_size("ty")
    n_cols = lax.axis_size("tx")
    local_acq, _, height, local_cols = stack.shape
    tile_rows = height // n_rows
    blocks_per_tile = n_rows // n_cols
    tile_cols = local_cols * blocks_per_tile
    padded_rows = tile_rows + 2 * RADIUS

    me_col = lax.axis_index("tx")
    me_row = lax.axis_index("ty")
    x = jnp.pad(stack, ((0, 0), (0, 0), (RADIUS, RADIUS), (0, 0)))
    start = me_col * blocks_per_tile + me_row % blocks_per_tile
    received = []
    for m in range(n_rows):
        pairs = []
        for col in range(n_cols):
            for row in range(n_rows):
                to_row = (m + col * blocks_per_tile + row % blocks_per_tile) % n_rows
                pairs.append((col * n_rows + row, (row // blocks_per_tile) * n_rows + to_row))
        first = ((start + m) % n_rows) * tile_rows
        chunk = lax.dynamic_slice_in_dim(x, first, padded_rows, axis=2)
        received.append(lax.ppermute(chunk, ("tx", "ty"), pairs))
    received = jnp.stack(received, axis=0)
    source = jnp.arange(blocks_per_tile)[:, None] + blocks_per_tile * jnp.arange(n_cols)[None, :]
    order = (me_row - source) % n_rows
    x = jnp.take(received, order.reshape(-1), axis=0)
    x = x.reshape(blocks_per_tile, 2 * count_acq, padded_rows, local_cols)

    forward = [(i, i + 1) for i in range(n_cols - 1)]
    backward = [(target, source) for source, target in forward]
    left = lax.ppermute(x[blocks_per_tile - 1, :, :, local_cols - RADIUS :], "tx", forward)
    right = lax.ppermute(x[0, :, :, :RADIUS], "tx", backward)
    gap = jnp.zeros((2 * count_acq, padded_rows, LANES - 2 * RADIUS), x.dtype)
    edge = jnp.concatenate([right, gap, left], axis=2)

    mixing = jnp.stack([jnp.stack([filt_re, -filt_im], -1), jnp.stack([filt_im, filt_re], -1)], 1)
    mixing = mixing.reshape(2 * count_acq, 2 * count_acq)
    main = jnp.einsum("kc,bchw->bkhw", mixing, x, preferred_element_type=jnp.float32)
    main = main.astype(jnp.bfloat16).reshape(blocks_per_tile, count_acq, 2, padded_rows, local_cols)
    edge = jnp.einsum("kc,chw->khw", mixing, edge, preferred_element_type=jnp.float32)
    edge = edge.astype(jnp.bfloat16).reshape(count_acq, 2, padded_rows, LANES)
    return pair_maps(main, edge, pre_ids, post_ids, tile_rows, tile_cols)


def solution(mesh):
    in_specs = (P("tx", None, None, "ty"), P(), P(), P(), P())
    out_specs = (P(None, "ty", "tx"), P(None, "ty", "tx"))
    return jax.shard_map(shards, mesh=mesh, in_specs=in_specs, out_specs=out_specs, check_vma=False)
```

```python
import functools

import jax
import jax.numpy as jnp
from jax import lax
from jax.experimental import pallas as pl
from jax.experimental.pallas import tpu as pltpu
from jax.sharding import PartitionSpec as P

RADIUS = 4
LANES = 128
PAIRS_PER_STEP = 4
FIELDS = 4


def pair_kernel(pre_ref, post_ref, *refs, tile_rows, tile_cols):
    del pre_ref, post_ref
    pp = PAIRS_PER_STEP
    sides = refs[: 4 * pp]
    band_ref, coh_ref, chg_ref, field_ref, rows_ref, stack_ref = refs[4 * pp :]
    window = 2 * RADIUS + 1
    padded_cols = tile_cols + LANES
    rows = pp * FIELDS * tile_rows
    blocks = tile_cols // LANES
    for p in range(pp):
        a_main, a_edge, b_main, b_edge = sides[4 * p : 4 * p + 4]
        pieces = [(c * a_main.shape[-1], a_main[c, 0], b_main[c, 0]) for c in range(a_main.shape[0])]
        pieces.append((tile_cols, a_edge[0], b_edge[0]))
        for at, a, b in pieces:
            width = a.shape[-1]
            pr = a[0].astype(jnp.float32)
            pi = a[1].astype(jnp.float32)
            qr = b[0].astype(jnp.float32)
            qi = b[1].astype(jnp.float32)
            fields = (pr * pr + pi * pi, qr * qr + qi * qi, pr * qr + pi * qi, pi * qr - pr * qi)
            for f, value in enumerate(fields):
                field_ref[f, :, pl.ds(at, width)] = value
        for f in range(FIELDS):
            acc = field_ref[f, pl.ds(0, tile_rows), :]
            for k in range(1, window):
                acc = acc + field_ref[f, pl.ds(k, tile_rows), :]
            at = (p * FIELDS + f) * tile_rows
            rows_ref[pl.ds(at, tile_rows), pl.ds(LANES, padded_cols)] = acc
            rows_ref[pl.ds(at, tile_rows), pl.ds(0, LANES)] = acc[:, padded_cols - LANES :]
    rowsum = rows_ref[...]
    high = rowsum.astype(jnp.bfloat16)
    low = (rowsum - high.astype(jnp.float32)).astype(jnp.bfloat16)
    width = 3 * LANES
    for j in range(blocks):
        stack_ref[pl.ds(j * rows, rows), pl.ds(0, width)] = high[:, j * LANES : j * LANES + width]
        stack_ref[pl.ds(j * rows, rows), pl.ds(width, width)] = low[:, j * LANES : j * LANES + width]
    sums = jnp.dot(stack_ref[...], band_ref[...], preferred_element_type=jnp.float32)
    means = sums / float(window * window)
    for j in range(blocks):
        for p in range(pp):
            base = j * rows + p * FIELDS * tile_rows
            pre_power = means[base : base + tile_rows] + 1e-06
            post_power = means[base + tile_rows : base + 2 * tile_rows] + 1e-06
            real_mean = means[base + 2 * tile_rows : base + 3 * tile_rows]
            imag_mean = means[base + 3 * tile_rows : base + 4 * tile_rows]
            coh = jnp.sqrt(real_mean * real_mean + imag_mean * imag_mean) / jnp.sqrt(
                pre_power * post_power
            )
            coh_ref[p, :, pl.ds(j * LANES, LANES)] = coh
            chg_ref[p, :, pl.ds(j * LANES, LANES)] = jnp.log(post_power / pre_power)


def pair_maps(main, edge, pre_ids, post_ids, tile_rows, tile_cols):
    count_pairs = pre_ids.shape[0]
    pp = PAIRS_PER_STEP
    blocks_per_tile, _, _, padded_rows, block_cols = main.shape
    width = 3 * LANES
    lane_in = jnp.arange(width)[:, None]
    lane_out = jnp.arange(LANES)[None, :]
    gap = lane_in - LANES - lane_out
    band = jnp.where((gap >= -RADIUS) & (gap <= RADIUS), 1.0, 0.0).astype(jnp.bfloat16)
    band = jnp.concatenate([band, band], axis=0)
    main_block = (blocks_per_tile, 1, 2, padded_rows, block_cols)
    edge_block = (1, 2, padded_rows, LANES)

    def specs(p, which):
        def main_index(i, pre, post):
            ids = pre if which == 0 else post
            return (0, ids[i * pp + p], 0, 0, 0)

        def edge_index(i, pre, post):
            ids = pre if which == 0 else post
            return (ids[i * pp + p], 0, 0, 0)

        return [pl.BlockSpec(main_block, main_index), pl.BlockSpec(edge_block, edge_index)]

    in_specs = []
    operands = []
    for p in range(pp):
        in_specs += specs(p, 0) + specs(p, 1)
        operands += [main, edge, main, edge]
    in_specs.append(pl.BlockSpec((2 * width, LANES), lambda i, pre, post: (0, 0)))
    operands.append(band)
    out_block = pl.BlockSpec((pp, tile_rows, tile_cols), lambda i, pre, post: (i, 0, 0))
    rows = pp * FIELDS * tile_rows
    blocks = tile_cols // LANES
    padded_cols = tile_cols + LANES
    grid_spec = pltpu.PrefetchScalarGridSpec(
        num_scalar_prefetch=2,
        grid=(count_pairs // pp,),
        in_specs=in_specs,
        out_specs=[out_block, out_block],
        scratch_shapes=[
            pltpu.VMEM((FIELDS, padded_rows, padded_cols), jnp.float32),
            pltpu.VMEM((rows, padded_cols + LANES), jnp.float32),
            pltpu.VMEM((blocks * rows, 2 * width), jnp.bfloat16),
        ],
    )
    out_shape = jax.ShapeDtypeStruct((count_pairs, tile_rows, tile_cols), jnp.float32)
    kernel = functools.partial(pair_kernel, tile_rows=tile_rows, tile_cols=tile_cols)
    return pl.pallas_call(
        kernel,
        grid_spec=grid_spec,
        out_shape=[out_shape, out_shape],
    )(pre_ids, post_ids, *operands)


def shards(stack, filt_re, filt_im, pre_ids, post_ids):
    count_acq = filt_re.shape[0]
    n_rows = lax.axis_size("ty")
    n_cols = lax.axis_size("tx")
    local_acq, _, height, local_cols = stack.shape
    tile_rows = height // n_rows
    blocks_per_tile = n_rows // n_cols
    tile_cols = local_cols * blocks_per_tile
    padded_rows = tile_rows + 2 * RADIUS

    me_col = lax.axis_index("tx")
    me_row = lax.axis_index("ty")
    x = jnp.pad(stack, ((0, 0), (0, 0), (RADIUS, RADIUS), (0, 0)))
    side = jnp.where(me_row % blocks_per_tile == 0, x[..., :RADIUS], x[..., local_cols - RADIUS :])
    start = me_col * blocks_per_tile + me_row % blocks_per_tile
    strip_shape = (local_acq * 2 * padded_rows * RADIUS // LANES, LANES)
    received = []
    strips = []
    for m in range(n_rows):
        pairs = []
        side_pairs = []
        for col in range(n_cols):
            for row in range(n_rows):
                block = row % blocks_per_tile
                to_row = (m + col * blocks_per_tile + block) % n_rows
                source = col * n_rows + row
                pairs.append((source, (row // blocks_per_tile) * n_rows + to_row))
                if block == blocks_per_tile - 1 and row // blocks_per_tile + 1 < n_cols:
                    side_pairs.append((source, (row // blocks_per_tile + 1) * n_rows + to_row))
                elif block == 0 and row // blocks_per_tile > 0:
                    side_pairs.append((source, (row // blocks_per_tile - 1) * n_rows + to_row))
        first = ((start + m) % n_rows) * tile_rows
        chunk = lax.dynamic_slice_in_dim(x, first, padded_rows, axis=2)
        received.append(lax.ppermute(chunk, ("tx", "ty"), pairs))
        piece = lax.dynamic_slice_in_dim(side, first, padded_rows, axis=2).reshape(strip_shape)
        strips.append(lax.ppermute(piece, ("tx", "ty"), side_pairs))
    received = jnp.stack(received, axis=0)
    strips = jnp.stack(strips, axis=0)
    source = jnp.arange(blocks_per_tile)[:, None] + blocks_per_tile * jnp.arange(n_cols)[None, :]
    order = (me_row - source) % n_rows
    x = jnp.take(received, order.reshape(-1), axis=0)
    x = x.reshape(blocks_per_tile, 2 * count_acq, padded_rows, local_cols)
    strips = jnp.take(strips, order[jnp.array([0, blocks_per_tile - 1])].reshape(-1), axis=0)
    strips = strips.reshape(2, 2 * count_acq, padded_rows, RADIUS)
    gap = jnp.zeros((2 * count_acq, padded_rows, LANES - 2 * RADIUS), x.dtype)
    edge = jnp.concatenate([strips[0], gap, strips[1]], axis=2)

    mixing = jnp.stack([jnp.stack([filt_re, -filt_im], -1), jnp.stack([filt_im, filt_re], -1)], 1)
    mixing = mixing.reshape(2 * count_acq, 2 * count_acq)
    main = jnp.einsum("kc,bchw->bkhw", mixing, x, preferred_element_type=jnp.float32)
    main = main.astype(jnp.bfloat16).reshape(blocks_per_tile, count_acq, 2, padded_rows, local_cols)
    edge = jnp.einsum("kc,chw->khw", mixing, edge, preferred_element_type=jnp.float32)
    edge = edge.astype(jnp.bfloat16).reshape(count_acq, 2, padded_rows, LANES)
    return pair_maps(main, edge, pre_ids, post_ids, tile_rows, tile_cols)


def solution(mesh):
    in_specs = (P("tx", None, None, "ty"), P(), P(), P(), P())
    out_specs = (P(None, "ty", "tx"), P(None, "ty", "tx"))
    return jax.shard_map(shards, mesh=mesh, in_specs=in_specs, out_specs=out_specs, check_vma=False)
```

```python
import functools

import jax
import jax.numpy as jnp
from jax import lax
from jax.experimental import pallas as pl
from jax.experimental.pallas import tpu as pltpu
from jax.sharding import PartitionSpec as P

RADIUS = 4
LANES = 128
PAIRS_PER_STEP = 4
FIELDS = 4


def pair_kernel(pre_ref, post_ref, *refs, tile_rows, tile_cols):
    del pre_ref, post_ref
    pp = PAIRS_PER_STEP
    sides = refs[: 4 * pp]
    band_ref, coh_ref, chg_ref, field_ref, rows_ref, stack_ref = refs[4 * pp :]
    window = 2 * RADIUS + 1
    padded_cols = tile_cols + LANES
    rows = pp * FIELDS * tile_rows
    blocks = tile_cols // LANES
    for p in range(pp):
        a_main, a_edge, b_main, b_edge = sides[4 * p : 4 * p + 4]
        pieces = [(c * a_main.shape[-1], a_main[c, 0], b_main[c, 0]) for c in range(a_main.shape[0])]
        pieces.append((tile_cols, a_edge[0], b_edge[0]))
        for at, a, b in pieces:
            width = a.shape[-1]
            pr = a[0].astype(jnp.float32)
            pi = a[1].astype(jnp.float32)
            qr = b[0].astype(jnp.float32)
            qi = b[1].astype(jnp.float32)
            fields = (pr * pr + pi * pi, qr * qr + qi * qi, pr * qr + pi * qi, pi * qr - pr * qi)
            for f, value in enumerate(fields):
                field_ref[f, :, pl.ds(at, width)] = value
        for f in range(FIELDS):
            acc = field_ref[f, pl.ds(0, tile_rows), :]
            for k in range(1, window):
                acc = acc + field_ref[f, pl.ds(k, tile_rows), :]
            at = (p * FIELDS + f) * tile_rows
            rows_ref[pl.ds(at, tile_rows), pl.ds(LANES, padded_cols)] = acc
            rows_ref[pl.ds(at, tile_rows), pl.ds(0, LANES)] = acc[:, padded_cols - LANES :]
    rowsum = rows_ref[...]
    high = rowsum.astype(jnp.bfloat16)
    low = (rowsum - high.astype(jnp.float32)).astype(jnp.bfloat16)
    width = 3 * LANES
    for j in range(blocks):
        stack_ref[pl.ds(j * rows, rows), pl.ds(0, width)] = high[:, j * LANES : j * LANES + width]
        stack_ref[pl.ds(j * rows, rows), pl.ds(width, width)] = low[:, j * LANES : j * LANES + width]
    sums = jnp.dot(stack_ref[...], band_ref[...], preferred_element_type=jnp.float32)
    means = sums / float(window * window)
    for j in range(blocks):
        for p in range(pp):
            base = j * rows + p * FIELDS * tile_rows
            pre_power = means[base : base + tile_rows] + 1e-06
            post_power = means[base + tile_rows : base + 2 * tile_rows] + 1e-06
            real_mean = means[base + 2 * tile_rows : base + 3 * tile_rows]
            imag_mean = means[base + 3 * tile_rows : base + 4 * tile_rows]
            coh = jnp.sqrt(real_mean * real_mean + imag_mean * imag_mean) / jnp.sqrt(
                pre_power * post_power
            )
            coh_ref[p, :, pl.ds(j * LANES, LANES)] = coh
            chg_ref[p, :, pl.ds(j * LANES, LANES)] = jnp.log(post_power / pre_power)


def pair_maps(main, edge, pre_ids, post_ids, tile_rows, tile_cols):
    count_pairs = pre_ids.shape[0]
    pp = PAIRS_PER_STEP
    blocks_per_tile, _, _, padded_rows, block_cols = main.shape
    width = 3 * LANES
    lane_in = jnp.arange(width)[:, None]
    lane_out = jnp.arange(LANES)[None, :]
    gap = lane_in - LANES - lane_out
    band = jnp.where((gap >= -RADIUS) & (gap <= RADIUS), 1.0, 0.0).astype(jnp.bfloat16)
    band = jnp.concatenate([band, band], axis=0)
    main_block = (blocks_per_tile, 1, 2, padded_rows, block_cols)
    edge_block = (1, 2, padded_rows, LANES)

    def specs(p, which):
        def main_index(i, pre, post):
            ids = pre if which == 0 else post
            return (0, ids[i * pp + p], 0, 0, 0)

        def edge_index(i, pre, post):
            ids = pre if which == 0 else post
            return (ids[i * pp + p], 0, 0, 0)

        return [pl.BlockSpec(main_block, main_index), pl.BlockSpec(edge_block, edge_index)]

    in_specs = []
    operands = []
    for p in range(pp):
        in_specs += specs(p, 0) + specs(p, 1)
        operands += [main, edge, main, edge]
    in_specs.append(pl.BlockSpec((2 * width, LANES), lambda i, pre, post: (0, 0)))
    operands.append(band)
    out_block = pl.BlockSpec((pp, tile_rows, tile_cols), lambda i, pre, post: (i, 0, 0))
    rows = pp * FIELDS * tile_rows
    blocks = tile_cols // LANES
    padded_cols = tile_cols + LANES
    grid_spec = pltpu.PrefetchScalarGridSpec(
        num_scalar_prefetch=2,
        grid=(count_pairs // pp,),
        in_specs=in_specs,
        out_specs=[out_block, out_block],
        scratch_shapes=[
            pltpu.VMEM((FIELDS, padded_rows, padded_cols), jnp.float32),
            pltpu.VMEM((rows, padded_cols + LANES), jnp.float32),
            pltpu.VMEM((blocks * rows, 2 * width), jnp.bfloat16),
        ],
    )
    out_shape = jax.ShapeDtypeStruct((count_pairs, tile_rows, tile_cols), jnp.float32)
    kernel = functools.partial(pair_kernel, tile_rows=tile_rows, tile_cols=tile_cols)
    return pl.pallas_call(
        kernel,
        grid_spec=grid_spec,
        out_shape=[out_shape, out_shape],
    )(pre_ids, post_ids, *operands)


def shards(stack, filt_re, filt_im, pre_ids, post_ids):
    count_acq = filt_re.shape[0]
    n_rows = lax.axis_size("ty")
    n_cols = lax.axis_size("tx")
    local_acq, _, height, local_cols = stack.shape
    tile_rows = height // n_rows
    blocks_per_tile = n_rows // n_cols
    tile_cols = local_cols * blocks_per_tile
    padded_rows = tile_rows + 2 * RADIUS

    me_col = lax.axis_index("tx")
    me_row = lax.axis_index("ty")
    x = jnp.pad(stack, ((0, 0), (0, 0), (RADIUS, RADIUS), (0, 0)))
    start = me_col * blocks_per_tile + me_row % blocks_per_tile
    received = []
    for m in range(n_rows):
        pairs = []
        for col in range(n_cols):
            for row in range(n_rows):
                to_row = (m + col * blocks_per_tile + row % blocks_per_tile) % n_rows
                pairs.append((col * n_rows + row, (row // blocks_per_tile) * n_rows + to_row))
        first = ((start + m) % n_rows) * tile_rows
        chunk = lax.dynamic_slice_in_dim(x, first, padded_rows, axis=2)
        received.append(lax.ppermute(chunk, ("tx", "ty"), pairs))
    received = jnp.stack(received, axis=0)
    source = jnp.arange(blocks_per_tile)[:, None] + blocks_per_tile * jnp.arange(n_cols)[None, :]
    order = (me_row - source) % n_rows
    x = jnp.take(received, order.reshape(-1), axis=0)
    x = x.reshape(blocks_per_tile, 2 * count_acq, padded_rows, local_cols)

    forward = [(i, i + 1) for i in range(n_cols - 1)]
    backward = [(target, source) for source, target in forward]
    strip_shape = x.shape[1:3] + (RADIUS,)
    flat = (2 * count_acq * padded_rows * RADIUS // LANES, LANES)
    left = x[blocks_per_tile - 1, :, :, local_cols - RADIUS :].reshape(flat)
    right = x[0, :, :, :RADIUS].reshape(flat)
    left = lax.ppermute(left, "tx", forward).reshape(strip_shape)
    right = lax.ppermute(right, "tx", backward).reshape(strip_shape)
    gap = jnp.zeros((2 * count_acq, padded_rows, LANES - 2 * RADIUS), x.dtype)
    edge = jnp.concatenate([right, gap, left], axis=2)

    mixing = jnp.stack([jnp.stack([filt_re, -filt_im], -1), jnp.stack([filt_im, filt_re], -1)], 1)
    mixing = mixing.reshape(2 * count_acq, 2 * count_acq)
    main = jnp.einsum("kc,bchw->bkhw", mixing, x, preferred_element_type=jnp.float32)
    main = main.astype(jnp.bfloat16).reshape(blocks_per_tile, count_acq, 2, padded_rows, local_cols)
    edge = jnp.einsum("kc,chw->khw", mixing, edge, preferred_element_type=jnp.float32)
    edge = edge.astype(jnp.bfloat16).reshape(count_acq, 2, padded_rows, LANES)
    return pair_maps(main, edge, pre_ids, post_ids, tile_rows, tile_cols)


def solution(mesh):
    in_specs = (P("tx", None, None, "ty"), P(), P(), P(), P())
    out_specs = (P(None, "ty", "tx"), P(None, "ty", "tx"))
    return jax.shard_map(shards, mesh=mesh, in_specs=in_specs, out_specs=out_specs, check_vma=False)
```

```python
import functools

import jax
import jax.numpy as jnp
from jax import lax
from jax.experimental import pallas as pl
from jax.experimental.pallas import tpu as pltpu
from jax.sharding import PartitionSpec as P

RADIUS = 4
LANES = 128
PAIRS_PER_STEP = 4
FIELDS = 4


def window_rows(full, window):
    count = full.shape[0]
    total, offset, span, part = None, 0, 1, full
    remaining = window
    while remaining:
        if remaining & 1:
            shifted = part if offset == 0 else pltpu.roll(part, count - offset, 0)
            total = shifted if total is None else total + shifted
            offset += span
        remaining >>= 1
        if remaining:
            part = part + pltpu.roll(part, count - span, 0)
            span *= 2
    return total


def pair_kernel(pre_ref, post_ref, *refs, tile_rows, tile_cols):
    del pre_ref, post_ref
    pp = PAIRS_PER_STEP
    sides = refs[: 4 * pp]
    band_ref, coh_ref, chg_ref, field_ref, rows_ref, stack_ref = refs[4 * pp :]
    window = 2 * RADIUS + 1
    padded_cols = tile_cols + LANES
    rows = pp * FIELDS * tile_rows
    blocks = tile_cols // LANES
    for p in range(pp):
        a_main, a_edge, b_main, b_edge = sides[4 * p : 4 * p + 4]
        pieces = [(c * a_main.shape[-1], a_main[c, 0], b_main[c, 0]) for c in range(a_main.shape[0])]
        pieces.append((tile_cols, a_edge[0], b_edge[0]))
        for at, a, b in pieces:
            width = a.shape[-1]
            pr = a[0].astype(jnp.float32)
            pi = a[1].astype(jnp.float32)
            qr = b[0].astype(jnp.float32)
            qi = b[1].astype(jnp.float32)
            fields = (pr * pr + pi * pi, qr * qr + qi * qi, pr * qr + pi * qi, pi * qr - pr * qi)
            for f, value in enumerate(fields):
                field_ref[f, :, pl.ds(at, width)] = value
        for f in range(FIELDS):
            acc = window_rows(field_ref[f], window)[:tile_rows]
            at = (p * FIELDS + f) * tile_rows
            rows_ref[pl.ds(at, tile_rows), pl.ds(LANES, padded_cols)] = acc
            rows_ref[pl.ds(at, tile_rows), pl.ds(0, LANES)] = acc[:, padded_cols - LANES :]
    rowsum = rows_ref[...]
    high = rowsum.astype(jnp.bfloat16)
    low = (rowsum - high.astype(jnp.float32)).astype(jnp.bfloat16)
    width = 3 * LANES
    for j in range(blocks):
        stack_ref[pl.ds(j * rows, rows), pl.ds(0, width)] = high[:, j * LANES : j * LANES + width]
        stack_ref[pl.ds(j * rows, rows), pl.ds(width, width)] = low[:, j * LANES : j * LANES + width]
    sums = jnp.dot(stack_ref[...], band_ref[...], preferred_element_type=jnp.float32)
    means = sums / float(window * window)
    for j in range(blocks):
        for p in range(pp):
            base = j * rows + p * FIELDS * tile_rows
            pre_power = means[base : base + tile_rows] + 1e-06
            post_power = means[base + tile_rows : base + 2 * tile_rows] + 1e-06
            real_mean = means[base + 2 * tile_rows : base + 3 * tile_rows]
            imag_mean = means[base + 3 * tile_rows : base + 4 * tile_rows]
            coh = jnp.sqrt(real_mean * real_mean + imag_mean * imag_mean) / jnp.sqrt(
                pre_power * post_power
            )
            coh_ref[p, :, pl.ds(j * LANES, LANES)] = coh
            chg_ref[p, :, pl.ds(j * LANES, LANES)] = jnp.log(post_power / pre_power)


def pair_maps(main, edge, pre_ids, post_ids, tile_rows, tile_cols):
    count_pairs = pre_ids.shape[0]
    pp = PAIRS_PER_STEP
    blocks_per_tile, _, _, padded_rows, block_cols = main.shape
    width = 3 * LANES
    lane_in = jnp.arange(width)[:, None]
    lane_out = jnp.arange(LANES)[None, :]
    gap = lane_in - LANES - lane_out
    band = jnp.where((gap >= -RADIUS) & (gap <= RADIUS), 1.0, 0.0).astype(jnp.bfloat16)
    band = jnp.concatenate([band, band], axis=0)
    main_block = (blocks_per_tile, 1, 2, padded_rows, block_cols)
    edge_block = (1, 2, padded_rows, LANES)

    def specs(p, which):
        def main_index(i, pre, post):
            ids = pre if which == 0 else post
            return (0, ids[i * pp + p], 0, 0, 0)

        def edge_index(i, pre, post):
            ids = pre if which == 0 else post
            return (ids[i * pp + p], 0, 0, 0)

        return [pl.BlockSpec(main_block, main_index), pl.BlockSpec(edge_block, edge_index)]

    in_specs = []
    operands = []
    for p in range(pp):
        in_specs += specs(p, 0) + specs(p, 1)
        operands += [main, edge, main, edge]
    in_specs.append(pl.BlockSpec((2 * width, LANES), lambda i, pre, post: (0, 0)))
    operands.append(band)
    out_block = pl.BlockSpec((pp, tile_rows, tile_cols), lambda i, pre, post: (i, 0, 0))
    rows = pp * FIELDS * tile_rows
    blocks = tile_cols // LANES
    padded_cols = tile_cols + LANES
    grid_spec = pltpu.PrefetchScalarGridSpec(
        num_scalar_prefetch=2,
        grid=(count_pairs // pp,),
        in_specs=in_specs,
        out_specs=[out_block, out_block],
        scratch_shapes=[
            pltpu.VMEM((FIELDS, padded_rows, padded_cols), jnp.float32),
            pltpu.VMEM((rows, padded_cols + LANES), jnp.float32),
            pltpu.VMEM((blocks * rows, 2 * width), jnp.bfloat16),
        ],
    )
    out_shape = jax.ShapeDtypeStruct((count_pairs, tile_rows, tile_cols), jnp.float32)
    kernel = functools.partial(pair_kernel, tile_rows=tile_rows, tile_cols=tile_cols)
    return pl.pallas_call(
        kernel,
        grid_spec=grid_spec,
        out_shape=[out_shape, out_shape],
    )(pre_ids, post_ids, *operands)


def shards(stack, filt_re, filt_im, pre_ids, post_ids):
    count_acq = filt_re.shape[0]
    n_rows = lax.axis_size("ty")
    n_cols = lax.axis_size("tx")
    local_acq, _, height, local_cols = stack.shape
    tile_rows = height // n_rows
    blocks_per_tile = n_rows // n_cols
    tile_cols = local_cols * blocks_per_tile
    padded_rows = tile_rows + 2 * RADIUS

    me_col = lax.axis_index("tx")
    me_row = lax.axis_index("ty")
    x = jnp.pad(stack, ((0, 0), (0, 0), (RADIUS, RADIUS), (0, 0)))
    start = me_col * blocks_per_tile + me_row % blocks_per_tile
    received = []
    for m in range(n_rows):
        pairs = []
        for col in range(n_cols):
            for row in range(n_rows):
                to_row = (m + col * blocks_per_tile + row % blocks_per_tile) % n_rows
                pairs.append((col * n_rows + row, (row // blocks_per_tile) * n_rows + to_row))
        first = ((start + m) % n_rows) * tile_rows
        chunk = lax.dynamic_slice_in_dim(x, first, padded_rows, axis=2)
        received.append(lax.ppermute(chunk, ("tx", "ty"), pairs))
    received = jnp.stack(received, axis=0)
    source = jnp.arange(blocks_per_tile)[:, None] + blocks_per_tile * jnp.arange(n_cols)[None, :]
    order = (me_row - source) % n_rows
    x = jnp.take(received, order.reshape(-1), axis=0)
    x = x.reshape(blocks_per_tile, 2 * count_acq, padded_rows, local_cols)

    forward = [(i, i + 1) for i in range(n_cols - 1)]
    backward = [(target, source) for source, target in forward]
    strip_shape = x.shape[1:3] + (RADIUS,)
    flat = (2 * count_acq * padded_rows * RADIUS // LANES, LANES)
    left = x[blocks_per_tile - 1, :, :, local_cols - RADIUS :].reshape(flat)
    right = x[0, :, :, :RADIUS].reshape(flat)
    left = lax.ppermute(left, "tx", forward).reshape(strip_shape)
    right = lax.ppermute(right, "tx", backward).reshape(strip_shape)
    gap = jnp.zeros((2 * count_acq, padded_rows, LANES - 2 * RADIUS), x.dtype)
    edge = jnp.concatenate([right, gap, left], axis=2)

    mixing = jnp.stack([jnp.stack([filt_re, -filt_im], -1), jnp.stack([filt_im, filt_re], -1)], 1)
    mixing = mixing.reshape(2 * count_acq, 2 * count_acq)
    main = jnp.einsum("kc,bchw->bkhw", mixing, x, preferred_element_type=jnp.float32)
    main = main.astype(jnp.bfloat16).reshape(blocks_per_tile, count_acq, 2, padded_rows, local_cols)
    edge = jnp.einsum("kc,chw->khw", mixing, edge, preferred_element_type=jnp.float32)
    edge = edge.astype(jnp.bfloat16).reshape(count_acq, 2, padded_rows, LANES)
    return pair_maps(main, edge, pre_ids, post_ids, tile_rows, tile_cols)


def solution(mesh):
    in_specs = (P("tx", None, None, "ty"), P(), P(), P(), P())
    out_specs = (P(None, "ty", "tx"), P(None, "ty", "tx"))
    return jax.shard_map(shards, mesh=mesh, in_specs=in_specs, out_specs=out_specs, check_vma=False)
```

```python
import functools

import jax
import jax.numpy as jnp
from jax import lax
from jax.experimental import pallas as pl
from jax.experimental.pallas import tpu as pltpu
from jax.sharding import PartitionSpec as P

RADIUS = 4
LANES = 128
PAIRS_PER_STEP = 4
ACQ_PER_STEP = 8
FIELDS = 4


def window_rows(full, window):
    count = full.shape[0]
    total, offset, span, part = None, 0, 1, full
    remaining = window
    while remaining:
        if remaining & 1:
            shifted = part if offset == 0 else pltpu.roll(part, count - offset, 0)
            total = shifted if total is None else total + shifted
            offset += span
        remaining >>= 1
        if remaining:
            part = part + pltpu.roll(part, count - span, 0)
            span *= 2
    return total


def box_means(field_ref, rows_ref, stack_ref, band_ref, count, tile_rows, tile_cols):
    window = 2 * RADIUS + 1
    padded_cols = tile_cols + LANES
    rows = count * tile_rows
    for f in range(count):
        acc = window_rows(field_ref[f], window)[:tile_rows]
        rows_ref[pl.ds(f * tile_rows, tile_rows), pl.ds(LANES, padded_cols)] = acc
        rows_ref[pl.ds(f * tile_rows, tile_rows), pl.ds(0, LANES)] = acc[:, padded_cols - LANES :]
    rowsum = rows_ref[...]
    high = rowsum.astype(jnp.bfloat16)
    low = (rowsum - high.astype(jnp.float32)).astype(jnp.bfloat16)
    width = 3 * LANES
    for j in range(tile_cols // LANES):
        stack_ref[pl.ds(j * rows, rows), pl.ds(0, width)] = high[:, j * LANES : j * LANES + width]
        stack_ref[pl.ds(j * rows, rows), pl.ds(width, width)] = low[:, j * LANES : j * LANES + width]
    sums = jnp.dot(stack_ref[...], band_ref[...], preferred_element_type=jnp.float32)
    return sums / float(window * window)


def pieces_of(main_ref, edge_ref, index, tile_cols):
    block_cols = main_ref.shape[-1]
    pieces = [(c * block_cols, main_ref[c, index]) for c in range(main_ref.shape[0])]
    pieces.append((tile_cols, edge_ref[index]))
    return pieces


def power_kernel(main_ref, edge_ref, band_ref, out_ref, field_ref, rows_ref, stack_ref, *, tile_rows, tile_cols):
    step = main_ref.shape[1]
    for a in range(step):
        for at, piece in pieces_of(main_ref, edge_ref, a, tile_cols):
            re = piece[0].astype(jnp.float32)
            im = piece[1].astype(jnp.float32)
            field_ref[a, :, pl.ds(at, piece.shape[-1])] = re * re + im * im
    means = box_means(field_ref, rows_ref, stack_ref, band_ref, step, tile_rows, tile_cols)
    rows = step * tile_rows
    for j in range(tile_cols // LANES):
        for a in range(step):
            base = j * rows + a * tile_rows
            out_ref[a, :, pl.ds(j * LANES, LANES)] = means[base : base + tile_rows] + 1e-06


def pair_kernel(pre_ref, post_ref, *refs, tile_rows, tile_cols):
    del pre_ref, post_ref
    pp = PAIRS_PER_STEP
    sides = refs[: 6 * pp]
    band_ref, coh_ref, chg_ref, field_ref, rows_ref, stack_ref = refs[6 * pp :]
    for p in range(pp):
        a_main, a_edge, b_main, b_edge = sides[6 * p : 6 * p + 4]
        a_pieces = pieces_of(a_main, a_edge, 0, tile_cols)
        b_pieces = pieces_of(b_main, b_edge, 0, tile_cols)
        for (at, a), (_, b) in zip(a_pieces, b_pieces):
            width = a.shape[-1]
            pr = a[0].astype(jnp.float32)
            pi = a[1].astype(jnp.float32)
            qr = b[0].astype(jnp.float32)
            qi = b[1].astype(jnp.float32)
            field_ref[2 * p, :, pl.ds(at, width)] = pr * qr + pi * qi
            field_ref[2 * p + 1, :, pl.ds(at, width)] = pi * qr - pr * qi
    means = box_means(field_ref, rows_ref, stack_ref, band_ref, 2 * pp, tile_rows, tile_cols)
    rows = 2 * pp * tile_rows
    for j in range(tile_cols // LANES):
        for p in range(pp):
            pre_power = sides[6 * p + 4][0, :, pl.ds(j * LANES, LANES)]
            post_power = sides[6 * p + 5][0, :, pl.ds(j * LANES, LANES)]
            base = j * rows + 2 * p * tile_rows
            real_mean = means[base : base + tile_rows]
            imag_mean = means[base + tile_rows : base + 2 * tile_rows]
            coh = jnp.sqrt(real_mean * real_mean + imag_mean * imag_mean) / jnp.sqrt(
                pre_power * post_power
            )
            coh_ref[p, :, pl.ds(j * LANES, LANES)] = coh
            chg_ref[p, :, pl.ds(j * LANES, LANES)] = jnp.log(post_power / pre_power)


def scratch(count, padded_rows, tile_rows, tile_cols):
    padded_cols = tile_cols + LANES
    return [
        pltpu.VMEM((count, padded_rows, padded_cols), jnp.float32),
        pltpu.VMEM((count * tile_rows, padded_cols + LANES), jnp.float32),
        pltpu.VMEM(((tile_cols // LANES) * count * tile_rows, 6 * LANES), jnp.bfloat16),
    ]


def pair_maps(main, edge, pre_ids, post_ids, tile_rows, tile_cols):
    count_pairs = pre_ids.shape[0]
    pp = PAIRS_PER_STEP
    ap = ACQ_PER_STEP
    blocks_per_tile, count_acq, _, padded_rows, block_cols = main.shape
    width = 3 * LANES
    lane_in = jnp.arange(width)[:, None]
    lane_out = jnp.arange(LANES)[None, :]
    gap = lane_in - LANES - lane_out
    band = jnp.where((gap >= -RADIUS) & (gap <= RADIUS), 1.0, 0.0).astype(jnp.bfloat16)
    band = jnp.concatenate([band, band], axis=0)
    kw = dict(tile_rows=tile_rows, tile_cols=tile_cols)

    power = pl.pallas_call(
        functools.partial(power_kernel, **kw),
        grid=(count_acq // ap,),
        in_specs=[
            pl.BlockSpec((blocks_per_tile, ap, 2, padded_rows, block_cols), lambda i: (0, i, 0, 0, 0)),
            pl.BlockSpec((ap, 2, padded_rows, LANES), lambda i: (i, 0, 0, 0)),
            pl.BlockSpec((2 * width, LANES), lambda i: (0, 0)),
        ],
        out_specs=pl.BlockSpec((ap, tile_rows, tile_cols), lambda i: (i, 0, 0)),
        out_shape=jax.ShapeDtypeStruct((count_acq, tile_rows, tile_cols), jnp.float32),
        scratch_shapes=scratch(ap, padded_rows, tile_rows, tile_cols),
    )(main, edge, band)

    main_block = (blocks_per_tile, 1, 2, padded_rows, block_cols)
    edge_block = (1, 2, padded_rows, LANES)
    power_block = (1, tile_rows, tile_cols)

    def specs(p):
        return [
            pl.BlockSpec(main_block, lambda i, pre, post: (0, pre[i * pp + p], 0, 0, 0)),
            pl.BlockSpec(edge_block, lambda i, pre, post: (pre[i * pp + p], 0, 0, 0)),
            pl.BlockSpec(main_block, lambda i, pre, post: (0, post[i * pp + p], 0, 0, 0)),
            pl.BlockSpec(edge_block, lambda i, pre, post: (post[i * pp + p], 0, 0, 0)),
            pl.BlockSpec(power_block, lambda i, pre, post: (pre[i * pp + p], 0, 0)),
            pl.BlockSpec(power_block, lambda i, pre, post: (post[i * pp + p], 0, 0)),
        ]

    in_specs = []
    operands = []
    for p in range(pp):
        in_specs += specs(p)
        operands += [main, edge, main, edge, power, power]
    in_specs.append(pl.BlockSpec((2 * width, LANES), lambda i, pre, post: (0, 0)))
    operands.append(band)
    out_block = pl.BlockSpec((pp, tile_rows, tile_cols), lambda i, pre, post: (i, 0, 0))
    grid_spec = pltpu.PrefetchScalarGridSpec(
        num_scalar_prefetch=2,
        grid=(count_pairs // pp,),
        in_specs=in_specs,
        out_specs=[out_block, out_block],
        scratch_shapes=scratch(2 * pp, padded_rows, tile_rows, tile_cols),
    )
    out_shape = jax.ShapeDtypeStruct((count_pairs, tile_rows, tile_cols), jnp.float32)
    return pl.pallas_call(
        functools.partial(pair_kernel, **kw),
        grid_spec=grid_spec,
        out_shape=[out_shape, out_shape],
    )(pre_ids, post_ids, *operands)


def shards(stack, filt_re, filt_im, pre_ids, post_ids):
    count_acq = filt_re.shape[0]
    n_rows = lax.axis_size("ty")
    n_cols = lax.axis_size("tx")
    local_acq, _, height, local_cols = stack.shape
    tile_rows = height // n_rows
    blocks_per_tile = n_rows // n_cols
    tile_cols = local_cols * blocks_per_tile
    padded_rows = tile_rows + 2 * RADIUS

    me_col = lax.axis_index("tx")
    me_row = lax.axis_index("ty")
    x = jnp.pad(stack, ((0, 0), (0, 0), (RADIUS, RADIUS), (0, 0)))
    start = me_col * blocks_per_tile + me_row % blocks_per_tile
    received = []
    for m in range(n_rows):
        pairs = []
        for col in range(n_cols):
            for row in range(n_rows):
                to_row = (m + col * blocks_per_tile + row % blocks_per_tile) % n_rows
                pairs.append((col * n_rows + row, (row // blocks_per_tile) * n_rows + to_row))
        first = ((start + m) % n_rows) * tile_rows
        chunk = lax.dynamic_slice_in_dim(x, first, padded_rows, axis=2)
        received.append(lax.ppermute(chunk, ("tx", "ty"), pairs))
    received = jnp.stack(received, axis=0)
    source = jnp.arange(blocks_per_tile)[:, None] + blocks_per_tile * jnp.arange(n_cols)[None, :]
    order = (me_row - source) % n_rows
    x = jnp.take(received, order.reshape(-1), axis=0)
    x = x.reshape(blocks_per_tile, 2 * count_acq, padded_rows, local_cols)

    forward = [(i, i + 1) for i in range(n_cols - 1)]
    backward = [(target, source) for source, target in forward]
    strip_shape = x.shape[1:3] + (RADIUS,)
    flat = (2 * count_acq * padded_rows * RADIUS // LANES, LANES)
    left = x[blocks_per_tile - 1, :, :, local_cols - RADIUS :].reshape(flat)
    right = x[0, :, :, :RADIUS].reshape(flat)
    left = lax.ppermute(left, "tx", forward).reshape(strip_shape)
    right = lax.ppermute(right, "tx", backward).reshape(strip_shape)
    gap = jnp.zeros((2 * count_acq, padded_rows, LANES - 2 * RADIUS), x.dtype)
    edge = jnp.concatenate([right, gap, left], axis=2)

    mixing = jnp.stack([jnp.stack([filt_re, -filt_im], -1), jnp.stack([filt_im, filt_re], -1)], 1)
    mixing = mixing.reshape(2 * count_acq, 2 * count_acq)
    main = jnp.einsum("kc,bchw->bkhw", mixing, x, preferred_element_type=jnp.float32)
    main = main.astype(jnp.bfloat16).reshape(blocks_per_tile, count_acq, 2, padded_rows, local_cols)
    edge = jnp.einsum("kc,chw->khw", mixing, edge, preferred_element_type=jnp.float32)
    edge = edge.astype(jnp.bfloat16).reshape(count_acq, 2, padded_rows, LANES)
    return pair_maps(main, edge, pre_ids, post_ids, tile_rows, tile_cols)


def solution(mesh):
    in_specs = (P("tx", None, None, "ty"), P(), P(), P(), P())
    out_specs = (P(None, "ty", "tx"), P(None, "ty", "tx"))
    return jax.shard_map(shards, mesh=mesh, in_specs=in_specs, out_specs=out_specs, check_vma=False)
```

```python
import functools

import jax
import jax.numpy as jnp
from jax import lax
from jax.experimental import pallas as pl
from jax.experimental.pallas import tpu as pltpu
from jax.sharding import PartitionSpec as P

RADIUS = 4
LANES = 128
PAIRS_PER_STEP = 4
FIELDS = 4


def window_rows(full, window):
    count = full.shape[0]
    total, offset, span, part = None, 0, 1, full
    remaining = window
    while remaining:
        if remaining & 1:
            shifted = part if offset == 0 else pltpu.roll(part, count - offset, 0)
            total = shifted if total is None else total + shifted
            offset += span
        remaining >>= 1
        if remaining:
            part = part + pltpu.roll(part, count - span, 0)
            span *= 2
    return total


def pair_kernel(pre_ref, post_ref, *refs, tile_rows, tile_cols):
    del pre_ref, post_ref
    pp = PAIRS_PER_STEP
    sides = refs[: 4 * pp]
    band_ref, coh_ref, chg_ref, field_ref, rows_ref, stack_ref = refs[4 * pp :]
    window = 2 * RADIUS + 1
    padded_cols = tile_cols + LANES
    rows = pp * FIELDS * tile_rows
    blocks = tile_cols // LANES
    for p in range(pp):
        a_main, a_edge, b_main, b_edge = sides[4 * p : 4 * p + 4]
        pieces = [(c * a_main.shape[-1], a_main[c, 0], b_main[c, 0]) for c in range(a_main.shape[0])]
        pieces.append((tile_cols, a_edge[0], b_edge[0]))
        for at, a, b in pieces:
            width = a.shape[-1]
            pr = a[0].astype(jnp.float32)
            pi = a[1].astype(jnp.float32)
            qr = b[0].astype(jnp.float32)
            qi = b[1].astype(jnp.float32)
            fields = (pr * pr + pi * pi, qr * qr + qi * qi, pr * qr + pi * qi, pi * qr - pr * qi)
            for f, value in enumerate(fields):
                field_ref[f, :, pl.ds(at, width)] = value
        for f in range(FIELDS):
            acc = window_rows(field_ref[f], window)[:tile_rows]
            at = (p * FIELDS + f) * tile_rows
            rows_ref[pl.ds(at, tile_rows), pl.ds(LANES, padded_cols)] = acc
            rows_ref[pl.ds(at, tile_rows), pl.ds(0, LANES)] = acc[:, padded_cols - LANES :]
    rowsum = rows_ref[...]
    high = rowsum.astype(jnp.bfloat16)
    low = (rowsum - high.astype(jnp.float32)).astype(jnp.bfloat16)
    width = 3 * LANES
    for j in range(blocks):
        stack_ref[pl.ds(j * rows, rows), pl.ds(0, width)] = high[:, j * LANES : j * LANES + width]
        stack_ref[pl.ds(j * rows, rows), pl.ds(width, width)] = low[:, j * LANES : j * LANES + width]
    sums = jnp.dot(stack_ref[...], band_ref[...], preferred_element_type=jnp.float32)
    means = sums / float(window * window)
    for j in range(blocks):
        for p in range(pp):
            base = j * rows + p * FIELDS * tile_rows
            pre_power = means[base : base + tile_rows] + 1e-06
            post_power = means[base + tile_rows : base + 2 * tile_rows] + 1e-06
            real_mean = means[base + 2 * tile_rows : base + 3 * tile_rows]
            imag_mean = means[base + 3 * tile_rows : base + 4 * tile_rows]
            coh = jnp.sqrt(real_mean * real_mean + imag_mean * imag_mean) / jnp.sqrt(
                pre_power * post_power
            )
            coh_ref[p, :, pl.ds(j * LANES, LANES)] = coh
            chg_ref[p, :, pl.ds(j * LANES, LANES)] = jnp.log(post_power / pre_power)


def pair_maps(main, edge, pre_ids, post_ids, tile_rows, tile_cols):
    count_pairs = pre_ids.shape[0]
    pp = PAIRS_PER_STEP
    blocks_per_tile, _, _, padded_rows, block_cols = main.shape
    width = 3 * LANES
    lane_in = jnp.arange(width)[:, None]
    lane_out = jnp.arange(LANES)[None, :]
    gap = lane_in - LANES - lane_out
    band = jnp.where((gap >= -RADIUS) & (gap <= RADIUS), 1.0, 0.0).astype(jnp.bfloat16)
    band = jnp.concatenate([band, band], axis=0)
    main_block = (blocks_per_tile, 1, 2, padded_rows, block_cols)
    edge_block = (1, 2, padded_rows, LANES)

    def specs(p, which):
        def main_index(i, pre, post):
            ids = pre if which == 0 else post
            return (0, ids[i * pp + p], 0, 0, 0)

        def edge_index(i, pre, post):
            ids = pre if which == 0 else post
            return (ids[i * pp + p], 0, 0, 0)

        return [pl.BlockSpec(main_block, main_index), pl.BlockSpec(edge_block, edge_index)]

    in_specs = []
    operands = []
    for p in range(pp):
        in_specs += specs(p, 0) + specs(p, 1)
        operands += [main, edge, main, edge]
    in_specs.append(pl.BlockSpec((2 * width, LANES), lambda i, pre, post: (0, 0)))
    operands.append(band)
    out_block = pl.BlockSpec((pp, tile_rows, tile_cols), lambda i, pre, post: (i, 0, 0))
    rows = pp * FIELDS * tile_rows
    blocks = tile_cols // LANES
    padded_cols = tile_cols + LANES
    grid_spec = pltpu.PrefetchScalarGridSpec(
        num_scalar_prefetch=2,
        grid=(count_pairs // pp,),
        in_specs=in_specs,
        out_specs=[out_block, out_block],
        scratch_shapes=[
            pltpu.VMEM((FIELDS, padded_rows, padded_cols), jnp.float32),
            pltpu.VMEM((rows, padded_cols + LANES), jnp.float32),
            pltpu.VMEM((blocks * rows, 2 * width), jnp.bfloat16),
        ],
    )
    out_shape = jax.ShapeDtypeStruct((count_pairs, tile_rows, tile_cols), jnp.float32)
    kernel = functools.partial(pair_kernel, tile_rows=tile_rows, tile_cols=tile_cols)
    return pl.pallas_call(
        kernel,
        grid_spec=grid_spec,
        out_shape=[out_shape, out_shape],
    )(pre_ids, post_ids, *operands)


def shards(stack, filt_re, filt_im, pre_ids, post_ids):
    count_acq = filt_re.shape[0]
    n_rows = lax.axis_size("ty")
    n_cols = lax.axis_size("tx")
    local_acq, _, height, local_cols = stack.shape
    tile_rows = height // n_rows
    blocks_per_tile = n_rows // n_cols
    tile_cols = local_cols * blocks_per_tile
    padded_rows = tile_rows + 2 * RADIUS

    me_col = lax.axis_index("tx")
    me_row = lax.axis_index("ty")
    x = jnp.pad(stack, ((0, 0), (0, 0), (RADIUS, RADIUS), (0, 0)))
    start = me_col * blocks_per_tile + me_row % blocks_per_tile
    received = []
    for m in range(n_rows):
        pairs = []
        for col in range(n_cols):
            for row in range(n_rows):
                to_row = (m + col * blocks_per_tile + row % blocks_per_tile) % n_rows
                pairs.append((col * n_rows + row, (row // blocks_per_tile) * n_rows + to_row))
        first = ((start + m) % n_rows) * tile_rows
        chunk = lax.dynamic_slice_in_dim(x, first, padded_rows, axis=2)
        chunk = chunk.reshape(local_acq * 2 * padded_rows, local_cols)
        received.append(lax.ppermute(chunk, ("tx", "ty"), pairs))
    received = jnp.stack(received, axis=0)
    source = jnp.arange(blocks_per_tile)[:, None] + blocks_per_tile * jnp.arange(n_cols)[None, :]
    order = (me_row - source) % n_rows
    x = jnp.take(received, order.reshape(-1), axis=0)
    x = x.reshape(blocks_per_tile, 2 * count_acq, padded_rows, local_cols)

    forward = [(i, i + 1) for i in range(n_cols - 1)]
    backward = [(target, source) for source, target in forward]
    strip_shape = x.shape[1:3] + (RADIUS,)
    flat = (2 * count_acq * padded_rows * RADIUS // LANES, LANES)
    left = x[blocks_per_tile - 1, :, :, local_cols - RADIUS :].reshape(flat)
    right = x[0, :, :, :RADIUS].reshape(flat)
    left = lax.ppermute(left, "tx", forward).reshape(strip_shape)
    right = lax.ppermute(right, "tx", backward).reshape(strip_shape)
    gap = jnp.zeros((2 * count_acq, padded_rows, LANES - 2 * RADIUS), x.dtype)
    edge = jnp.concatenate([right, gap, left], axis=2)

    mixing = jnp.stack([jnp.stack([filt_re, -filt_im], -1), jnp.stack([filt_im, filt_re], -1)], 1)
    mixing = mixing.reshape(2 * count_acq, 2 * count_acq)
    main = jnp.einsum("kc,bchw->bkhw", mixing, x, preferred_element_type=jnp.float32)
    main = main.astype(jnp.bfloat16).reshape(blocks_per_tile, count_acq, 2, padded_rows, local_cols)
    edge = jnp.einsum("kc,chw->khw", mixing, edge, preferred_element_type=jnp.float32)
    edge = edge.astype(jnp.bfloat16).reshape(count_acq, 2, padded_rows, LANES)
    return pair_maps(main, edge, pre_ids, post_ids, tile_rows, tile_cols)


def solution(mesh):
    in_specs = (P("tx", None, None, "ty"), P(), P(), P(), P())
    out_specs = (P(None, "ty", "tx"), P(None, "ty", "tx"))
    return jax.shard_map(shards, mesh=mesh, in_specs=in_specs, out_specs=out_specs, check_vma=False)
```

```python
import functools

import jax
import jax.numpy as jnp
from jax import lax
from jax.experimental import pallas as pl
from jax.experimental.pallas import tpu as pltpu
from jax.sharding import PartitionSpec as P

RADIUS = 4
LANES = 128
PAIRS_PER_STEP = 4
FIELDS = 4


def window_rows(full, window):
    count = full.shape[0]
    total, offset, span, part = None, 0, 1, full
    remaining = window
    while remaining:
        if remaining & 1:
            shifted = part if offset == 0 else pltpu.roll(part, count - offset, 0)
            total = shifted if total is None else total + shifted
            offset += span
        remaining >>= 1
        if remaining:
            part = part + pltpu.roll(part, count - span, 0)
            span *= 2
    return total


def pair_kernel(pre_ref, post_ref, *refs, tile_rows, tile_cols):
    del pre_ref, post_ref
    pp = PAIRS_PER_STEP
    sides = refs[: 4 * pp]
    band_ref, coh_ref, chg_ref, field_ref, rows_ref, stack_ref = refs[4 * pp :]
    window = 2 * RADIUS + 1
    padded_cols = tile_cols + LANES
    rows = pp * FIELDS * tile_rows
    blocks = tile_cols // LANES
    for p in range(pp):
        a_main, a_edge, b_main, b_edge = sides[4 * p : 4 * p + 4]
        pieces = [(c * a_main.shape[-1], a_main[c, 0], b_main[c, 0]) for c in range(a_main.shape[0])]
        pieces.append((tile_cols, a_edge[0], b_edge[0]))
        for at, a, b in pieces:
            width = a.shape[-1]
            pr = a[0].astype(jnp.float32)
            pi = a[1].astype(jnp.float32)
            qr = b[0].astype(jnp.float32)
            qi = b[1].astype(jnp.float32)
            fields = (pr * pr + pi * pi, qr * qr + qi * qi, pr * qr + pi * qi, pi * qr - pr * qi)
            for f, value in enumerate(fields):
                field_ref[f, :, pl.ds(at, width)] = value
        for f in range(FIELDS):
            acc = window_rows(field_ref[f], window)[:tile_rows]
            at = (p * FIELDS + f) * tile_rows
            rows_ref[pl.ds(at, tile_rows), pl.ds(LANES, padded_cols)] = acc
            rows_ref[pl.ds(at, tile_rows), pl.ds(0, LANES)] = acc[:, padded_cols - LANES :]
    rowsum = rows_ref[...]
    high = rowsum.astype(jnp.bfloat16)
    low = (rowsum - high.astype(jnp.float32)).astype(jnp.bfloat16)
    width = 3 * LANES
    for j in range(blocks):
        stack_ref[pl.ds(j * rows, rows), pl.ds(0, width)] = high[:, j * LANES : j * LANES + width]
        stack_ref[pl.ds(j * rows, rows), pl.ds(width, width)] = low[:, j * LANES : j * LANES + width]
    sums = jnp.dot(stack_ref[...], band_ref[...], preferred_element_type=jnp.float32)
    means = sums / float(window * window)
    for j in range(blocks):
        for p in range(pp):
            base = j * rows + p * FIELDS * tile_rows
            pre_power = means[base : base + tile_rows] + 1e-06
            post_power = means[base + tile_rows : base + 2 * tile_rows] + 1e-06
            real_mean = means[base + 2 * tile_rows : base + 3 * tile_rows]
            imag_mean = means[base + 3 * tile_rows : base + 4 * tile_rows]
            coh = jnp.sqrt(real_mean * real_mean + imag_mean * imag_mean) / jnp.sqrt(
                pre_power * post_power
            )
            coh_ref[p, :, pl.ds(j * LANES, LANES)] = coh
            chg_ref[p, :, pl.ds(j * LANES, LANES)] = jnp.log(post_power / pre_power)


def pair_maps(main, edge, pre_ids, post_ids, tile_rows, tile_cols):
    count_pairs = pre_ids.shape[0]
    pp = PAIRS_PER_STEP
    blocks_per_tile, _, _, padded_rows, block_cols = main.shape
    width = 3 * LANES
    lane_in = jnp.arange(width)[:, None]
    lane_out = jnp.arange(LANES)[None, :]
    gap = lane_in - LANES - lane_out
    band = jnp.where((gap >= -RADIUS) & (gap <= RADIUS), 1.0, 0.0).astype(jnp.bfloat16)
    band = jnp.concatenate([band, band], axis=0)
    main_block = (blocks_per_tile, 1, 2, padded_rows, block_cols)
    edge_block = (1, 2, padded_rows, LANES)

    def specs(p, which):
        def main_index(i, pre, post):
            ids = pre if which == 0 else post
            return (0, ids[i * pp + p], 0, 0, 0)

        def edge_index(i, pre, post):
            ids = pre if which == 0 else post
            return (ids[i * pp + p], 0, 0, 0)

        return [pl.BlockSpec(main_block, main_index), pl.BlockSpec(edge_block, edge_index)]

    in_specs = []
    operands = []
    for p in range(pp):
        in_specs += specs(p, 0) + specs(p, 1)
        operands += [main, edge, main, edge]
    in_specs.append(pl.BlockSpec((2 * width, LANES), lambda i, pre, post: (0, 0)))
    operands.append(band)
    out_block = pl.BlockSpec((pp, tile_rows, tile_cols), lambda i, pre, post: (i, 0, 0))
    rows = pp * FIELDS * tile_rows
    blocks = tile_cols // LANES
    padded_cols = tile_cols + LANES
    grid_spec = pltpu.PrefetchScalarGridSpec(
        num_scalar_prefetch=2,
        grid=(count_pairs // pp,),
        in_specs=in_specs,
        out_specs=[out_block, out_block],
        scratch_shapes=[
            pltpu.VMEM((FIELDS, padded_rows, padded_cols), jnp.float32),
            pltpu.VMEM((rows, padded_cols + LANES), jnp.float32),
            pltpu.VMEM((blocks * rows, 2 * width), jnp.bfloat16),
        ],
    )
    out_shape = jax.ShapeDtypeStruct((count_pairs, tile_rows, tile_cols), jnp.float32)
    kernel = functools.partial(pair_kernel, tile_rows=tile_rows, tile_cols=tile_cols)
    return pl.pallas_call(
        kernel,
        grid_spec=grid_spec,
        out_shape=[out_shape, out_shape],
    )(pre_ids, post_ids, *operands)


def shards(stack, filt_re, filt_im, pre_ids, post_ids):
    count_acq = filt_re.shape[0]
    n_rows = lax.axis_size("ty")
    n_cols = lax.axis_size("tx")
    local_acq, _, height, local_cols = stack.shape
    tile_rows = height // n_rows
    blocks_per_tile = n_rows // n_cols
    tile_cols = local_cols * blocks_per_tile
    padded_rows = tile_rows + 2 * RADIUS

    me_col = lax.axis_index("tx")
    me_row = lax.axis_index("ty")
    x = jnp.pad(stack, ((0, 0), (0, 0), (RADIUS, RADIUS), (0, 0)))
    start = me_col * blocks_per_tile + me_row % blocks_per_tile
    received = []
    for m in range(n_rows):
        pairs = []
        for col in range(n_cols):
            for row in range(n_rows):
                to_row = (m + col * blocks_per_tile + row % blocks_per_tile) % n_rows
                pairs.append((col * n_rows + row, (row // blocks_per_tile) * n_rows + to_row))
        first = ((start + m) % n_rows) * tile_rows
        chunk = lax.dynamic_slice_in_dim(x, first, padded_rows, axis=2)
        chunk = chunk.reshape(local_acq * 2 * padded_rows, local_cols)
        received.append(lax.ppermute(chunk, ("tx", "ty"), pairs))
    received = jnp.stack(received, axis=0)
    source = jnp.arange(blocks_per_tile)[:, None] + blocks_per_tile * jnp.arange(n_cols)[None, :]
    order = (me_row - source) % n_rows
    x = jnp.take(received, order.reshape(-1), axis=0)
    x = x.reshape(blocks_per_tile, 2 * count_acq, padded_rows, local_cols)

    forward = [(i, i + 1) for i in range(n_cols - 1)]
    backward = [(target, source) for source, target in forward]
    left = lax.ppermute(x[blocks_per_tile - 1, :, :, local_cols - LANES :], "tx", forward)
    right = lax.ppermute(x[0, :, :, :LANES], "tx", backward)
    lane = lax.broadcasted_iota(jnp.int32, right.shape, 2)
    zeros = jnp.zeros_like(right)
    edge = jnp.where(lane < RADIUS, right, jnp.where(lane >= LANES - RADIUS, left, zeros))

    mixing = jnp.stack([jnp.stack([filt_re, -filt_im], -1), jnp.stack([filt_im, filt_re], -1)], 1)
    mixing = mixing.reshape(2 * count_acq, 2 * count_acq)
    main = jnp.einsum("kc,bchw->bkhw", mixing, x, preferred_element_type=jnp.float32)
    main = main.astype(jnp.bfloat16).reshape(blocks_per_tile, count_acq, 2, padded_rows, local_cols)
    edge = jnp.einsum("kc,chw->khw", mixing, edge, preferred_element_type=jnp.float32)
    edge = edge.astype(jnp.bfloat16).reshape(count_acq, 2, padded_rows, LANES)
    return pair_maps(main, edge, pre_ids, post_ids, tile_rows, tile_cols)


def solution(mesh):
    in_specs = (P("tx", None, None, "ty"), P(), P(), P(), P())
    out_specs = (P(None, "ty", "tx"), P(None, "ty", "tx"))
    return jax.shard_map(shards, mesh=mesh, in_specs=in_specs, out_specs=out_specs, check_vma=False)
```

```python
import functools

import jax
import jax.numpy as jnp
from jax import lax
from jax.experimental import pallas as pl
from jax.experimental.pallas import tpu as pltpu
from jax.sharding import PartitionSpec as P

RADIUS = 4
LANES = 128
PAIRS_PER_STEP = 4
FIELDS = 4


def window_rows(full, window):
    count = full.shape[0]
    total, offset, span, part = None, 0, 1, full
    remaining = window
    while remaining:
        if remaining & 1:
            shifted = part if offset == 0 else pltpu.roll(part, count - offset, 0)
            total = shifted if total is None else total + shifted
            offset += span
        remaining >>= 1
        if remaining:
            part = part + pltpu.roll(part, count - span, 0)
            span *= 2
    return total


def pair_kernel(pre_ref, post_ref, *refs, tile_rows, tile_cols):
    del pre_ref, post_ref
    pp = PAIRS_PER_STEP
    sides = refs[: 4 * pp]
    band_ref, coh_ref, chg_ref, field_ref, rows_ref, stack_ref = refs[4 * pp :]
    window = 2 * RADIUS + 1
    padded_cols = tile_cols + LANES
    rows = pp * FIELDS * tile_rows
    blocks = tile_cols // LANES
    for p in range(pp):
        a_main, a_edge, b_main, b_edge = sides[4 * p : 4 * p + 4]
        pieces = [(c * a_main.shape[-1], a_main[c, 0], b_main[c, 0]) for c in range(a_main.shape[0])]
        pieces.append((tile_cols, a_edge[0], b_edge[0]))
        for at, a, b in pieces:
            width = a.shape[-1]
            pr = a[0].astype(jnp.float32)
            pi = a[1].astype(jnp.float32)
            qr = b[0].astype(jnp.float32)
            qi = b[1].astype(jnp.float32)
            fields = (pr * pr + pi * pi, qr * qr + qi * qi, pr * qr + pi * qi, pi * qr - pr * qi)
            for f, value in enumerate(fields):
                field_ref[f, :, pl.ds(at, width)] = value
        for f in range(FIELDS):
            acc = window_rows(field_ref[f], window)[:tile_rows]
            at = (p * FIELDS + f) * tile_rows
            rows_ref[pl.ds(at, tile_rows), pl.ds(LANES, padded_cols)] = acc
            rows_ref[pl.ds(at, tile_rows), pl.ds(0, LANES)] = acc[:, padded_cols - LANES :]
    rowsum = rows_ref[...]
    high = rowsum.astype(jnp.bfloat16)
    low = (rowsum - high.astype(jnp.float32)).astype(jnp.bfloat16)
    width = 3 * LANES
    for j in range(blocks):
        stack_ref[pl.ds(j * rows, rows), pl.ds(0, width)] = high[:, j * LANES : j * LANES + width]
        stack_ref[pl.ds(j * rows, rows), pl.ds(width, width)] = low[:, j * LANES : j * LANES + width]
    sums = jnp.dot(stack_ref[...], band_ref[...], preferred_element_type=jnp.float32)
    means = sums / float(window * window)
    for j in range(blocks):
        for p in range(pp):
            base = j * rows + p * FIELDS * tile_rows
            pre_power = means[base : base + tile_rows] + 1e-06
            post_power = means[base + tile_rows : base + 2 * tile_rows] + 1e-06
            real_mean = means[base + 2 * tile_rows : base + 3 * tile_rows]
            imag_mean = means[base + 3 * tile_rows : base + 4 * tile_rows]
            coh = jnp.sqrt(real_mean * real_mean + imag_mean * imag_mean) / jnp.sqrt(
                pre_power * post_power
            )
            coh_ref[p, :, pl.ds(j * LANES, LANES)] = coh
            chg_ref[p, :, pl.ds(j * LANES, LANES)] = jnp.log(post_power / pre_power)


def pair_maps(main, edge, pre_ids, post_ids, tile_rows, tile_cols):
    count_pairs = pre_ids.shape[0]
    pp = PAIRS_PER_STEP
    blocks_per_tile, _, _, padded_rows, block_cols = main.shape
    width = 3 * LANES
    lane_in = jnp.arange(width)[:, None]
    lane_out = jnp.arange(LANES)[None, :]
    gap = lane_in - LANES - lane_out
    band = jnp.where((gap >= -RADIUS) & (gap <= RADIUS), 1.0, 0.0).astype(jnp.bfloat16)
    band = jnp.concatenate([band, band], axis=0)
    main_block = (blocks_per_tile, 1, 2, padded_rows, block_cols)
    edge_block = (1, 2, padded_rows, LANES)

    def specs(p, which):
        def main_index(i, pre, post):
            ids = pre if which == 0 else post
            return (0, ids[i * pp + p], 0, 0, 0)

        def edge_index(i, pre, post):
            ids = pre if which == 0 else post
            return (ids[i * pp + p], 0, 0, 0)

        return [pl.BlockSpec(main_block, main_index), pl.BlockSpec(edge_block, edge_index)]

    in_specs = []
    operands = []
    for p in range(pp):
        in_specs += specs(p, 0) + specs(p, 1)
        operands += [main, edge, main, edge]
    in_specs.append(pl.BlockSpec((2 * width, LANES), lambda i, pre, post: (0, 0)))
    operands.append(band)
    out_block = pl.BlockSpec((pp, tile_rows, tile_cols), lambda i, pre, post: (i, 0, 0))
    rows = pp * FIELDS * tile_rows
    blocks = tile_cols // LANES
    padded_cols = tile_cols + LANES
    grid_spec = pltpu.PrefetchScalarGridSpec(
        num_scalar_prefetch=2,
        grid=(count_pairs // pp,),
        in_specs=in_specs,
        out_specs=[out_block, out_block],
        scratch_shapes=[
            pltpu.VMEM((FIELDS, padded_rows, padded_cols), jnp.float32),
            pltpu.VMEM((rows, padded_cols + LANES), jnp.float32),
            pltpu.VMEM((blocks * rows, 2 * width), jnp.bfloat16),
        ],
    )
    out_shape = jax.ShapeDtypeStruct((count_pairs, tile_rows, tile_cols), jnp.float32)
    kernel = functools.partial(pair_kernel, tile_rows=tile_rows, tile_cols=tile_cols)
    return pl.pallas_call(
        kernel,
        grid_spec=grid_spec,
        out_shape=[out_shape, out_shape],
    )(pre_ids, post_ids, *operands)


def shards(stack, filt_re, filt_im, pre_ids, post_ids):
    count_acq = filt_re.shape[0]
    n_rows = lax.axis_size("ty")
    n_cols = lax.axis_size("tx")
    local_acq, _, height, local_cols = stack.shape
    tile_rows = height // n_rows
    blocks_per_tile = n_rows // n_cols
    tile_cols = local_cols * blocks_per_tile
    padded_rows = tile_rows + 2 * RADIUS

    me_col = lax.axis_index("tx")
    me_row = lax.axis_index("ty")
    x = jnp.pad(stack, ((0, 0), (0, 0), (RADIUS, RADIUS), (0, 0)))
    start = me_col * blocks_per_tile + me_row % blocks_per_tile
    received = []
    for m in range(n_rows):
        pairs = []
        for col in range(n_cols):
            for row in range(n_rows):
                to_row = (m + col * blocks_per_tile + row % blocks_per_tile) % n_rows
                pairs.append((col * n_rows + row, (row // blocks_per_tile) * n_rows + to_row))
        first = ((start + m) % n_rows) * tile_rows
        chunk = lax.dynamic_slice_in_dim(x, first, padded_rows, axis=2)
        chunk = chunk.reshape(local_acq * 2 * padded_rows, local_cols)
        received.append(lax.ppermute(chunk, ("tx", "ty"), pairs))
    received = jnp.stack(received, axis=0)
    source = jnp.arange(blocks_per_tile)[:, None] + blocks_per_tile * jnp.arange(n_cols)[None, :]
    order = (me_row - source) % n_rows
    x = jnp.take(received, order.reshape(-1), axis=0)
    x = x.reshape(blocks_per_tile, 2 * count_acq, padded_rows, local_cols)

    forward = [(i, i + 1) for i in range(n_cols - 1)]
    backward = [(target, source) for source, target in forward]
    mixing = jnp.stack([jnp.stack([filt_re, -filt_im], -1), jnp.stack([filt_im, filt_re], -1)], 1)
    mixing = mixing.reshape(2 * count_acq, 2 * count_acq)
    main = jnp.einsum("kc,bchw->bkhw", mixing, x, preferred_element_type=jnp.float32)
    main = main.astype(jnp.bfloat16).reshape(blocks_per_tile, count_acq, 2, padded_rows, local_cols)

    left = lax.ppermute(main[blocks_per_tile - 1, :, :, :, local_cols - LANES :], "tx", forward)
    right = lax.ppermute(main[0, :, :, :, :LANES], "tx", backward)
    lane = lax.broadcasted_iota(jnp.int32, right.shape, 3)
    zeros = jnp.zeros_like(right)
    edge = jnp.where(lane < RADIUS, right, jnp.where(lane >= LANES - RADIUS, left, zeros))
    return pair_maps(main, edge, pre_ids, post_ids, tile_rows, tile_cols)


def solution(mesh):
    in_specs = (P("tx", None, None, "ty"), P(), P(), P(), P())
    out_specs = (P(None, "ty", "tx"), P(None, "ty", "tx"))
    return jax.shard_map(shards, mesh=mesh, in_specs=in_specs, out_specs=out_specs, check_vma=False)
```

```python
import functools

import jax
import jax.numpy as jnp
from jax import lax
from jax.experimental import pallas as pl
from jax.experimental.pallas import tpu as pltpu
from jax.sharding import PartitionSpec as P

RADIUS = 4
LANES = 128
PAIRS_PER_STEP = 4
FIELDS = 4


def window_rows(full, window):
    count = full.shape[0]
    total, offset, span, part = None, 0, 1, full
    remaining = window
    while remaining:
        if remaining & 1:
            shifted = part if offset == 0 else pltpu.roll(part, count - offset, 0)
            total = shifted if total is None else total + shifted
            offset += span
        remaining >>= 1
        if remaining:
            part = part + pltpu.roll(part, count - span, 0)
            span *= 2
    return total


def pair_kernel(pre_ref, post_ref, *refs, tile_rows, tile_cols):
    del pre_ref, post_ref
    pp = PAIRS_PER_STEP
    sides = refs[: 4 * pp]
    band_ref, coh_ref, chg_ref, field_ref, rows_ref, stack_ref = refs[4 * pp :]
    window = 2 * RADIUS + 1
    padded_cols = tile_cols + LANES
    rows = pp * FIELDS * tile_rows
    blocks = tile_cols // LANES
    for p in range(pp):
        a_main, a_edge, b_main, b_edge = sides[4 * p : 4 * p + 4]
        pieces = [(c * a_main.shape[-1], a_main[c, 0], b_main[c, 0]) for c in range(a_main.shape[0])]
        pieces.append((tile_cols, a_edge[0], b_edge[0]))
        for at, a, b in pieces:
            width = a.shape[-1]
            pr = a[0].astype(jnp.float32)
            pi = a[1].astype(jnp.float32)
            qr = b[0].astype(jnp.float32)
            qi = b[1].astype(jnp.float32)
            fields = (pr * pr + pi * pi, qr * qr + qi * qi, pr * qr + pi * qi, pi * qr - pr * qi)
            for f, value in enumerate(fields):
                field_ref[f, :, pl.ds(at, width)] = value
        for f in range(FIELDS):
            acc = window_rows(field_ref[f], window)[:tile_rows]
            at = (p * FIELDS + f) * tile_rows
            rows_ref[pl.ds(at, tile_rows), pl.ds(LANES, padded_cols)] = acc
            rows_ref[pl.ds(at, tile_rows), pl.ds(0, LANES)] = acc[:, padded_cols - LANES :]
    rowsum = rows_ref[...]
    high = rowsum.astype(jnp.bfloat16)
    low = (rowsum - high.astype(jnp.float32)).astype(jnp.bfloat16)
    width = 3 * LANES
    for j in range(blocks):
        stack_ref[pl.ds(j * rows, rows), pl.ds(0, width)] = high[:, j * LANES : j * LANES + width]
        stack_ref[pl.ds(j * rows, rows), pl.ds(width, width)] = low[:, j * LANES : j * LANES + width]
    sums = jnp.dot(stack_ref[...], band_ref[...], preferred_element_type=jnp.float32)
    means = sums / float(window * window)
    for j in range(blocks):
        for p in range(pp):
            base = j * rows + p * FIELDS * tile_rows
            pre_power = means[base : base + tile_rows] + 1e-06
            post_power = means[base + tile_rows : base + 2 * tile_rows] + 1e-06
            real_mean = means[base + 2 * tile_rows : base + 3 * tile_rows]
            imag_mean = means[base + 3 * tile_rows : base + 4 * tile_rows]
            coh = jnp.sqrt(real_mean * real_mean + imag_mean * imag_mean) / jnp.sqrt(
                pre_power * post_power
            )
            coh_ref[p, :, pl.ds(j * LANES, LANES)] = coh
            chg_ref[p, :, pl.ds(j * LANES, LANES)] = jnp.log(post_power / pre_power)


def pair_maps(main, edge, pre_ids, post_ids, tile_rows, tile_cols):
    count_pairs = pre_ids.shape[0]
    pp = PAIRS_PER_STEP
    blocks_per_tile, _, _, padded_rows, block_cols = main.shape
    width = 3 * LANES
    lane_in = jnp.arange(width)[:, None]
    lane_out = jnp.arange(LANES)[None, :]
    gap = lane_in - LANES - lane_out
    band = jnp.where((gap >= -RADIUS) & (gap <= RADIUS), 1.0, 0.0).astype(jnp.bfloat16)
    band = jnp.concatenate([band, band], axis=0)
    main_block = (blocks_per_tile, 1, 2, padded_rows, block_cols)
    edge_block = (1, 2, padded_rows, LANES)

    def specs(p, which):
        def main_index(i, pre, post):
            ids = pre if which == 0 else post
            return (0, ids[i * pp + p], 0, 0, 0)

        def edge_index(i, pre, post):
            ids = pre if which == 0 else post
            return (ids[i * pp + p], 0, 0, 0)

        return [pl.BlockSpec(main_block, main_index), pl.BlockSpec(edge_block, edge_index)]

    in_specs = []
    operands = []
    for p in range(pp):
        in_specs += specs(p, 0) + specs(p, 1)
        operands += [main, edge, main, edge]
    in_specs.append(pl.BlockSpec((2 * width, LANES), lambda i, pre, post: (0, 0)))
    operands.append(band)
    out_block = pl.BlockSpec((pp, tile_rows, tile_cols), lambda i, pre, post: (i, 0, 0))
    rows = pp * FIELDS * tile_rows
    blocks = tile_cols // LANES
    padded_cols = tile_cols + LANES
    grid_spec = pltpu.PrefetchScalarGridSpec(
        num_scalar_prefetch=2,
        grid=(count_pairs // pp,),
        in_specs=in_specs,
        out_specs=[out_block, out_block],
        scratch_shapes=[
            pltpu.VMEM((FIELDS, padded_rows, padded_cols), jnp.float32),
            pltpu.VMEM((rows, padded_cols + LANES), jnp.float32),
            pltpu.VMEM((blocks * rows, 2 * width), jnp.bfloat16),
        ],
    )
    out_shape = jax.ShapeDtypeStruct((count_pairs, tile_rows, tile_cols), jnp.float32)
    kernel = functools.partial(pair_kernel, tile_rows=tile_rows, tile_cols=tile_cols)
    return pl.pallas_call(
        kernel,
        grid_spec=grid_spec,
        out_shape=[out_shape, out_shape],
    )(pre_ids, post_ids, *operands)


def shards(stack, filt_re, filt_im, pre_ids, post_ids):
    count_acq = filt_re.shape[0]
    n_rows = lax.axis_size("ty")
    n_cols = lax.axis_size("tx")
    local_acq, _, height, local_cols = stack.shape
    tile_rows = height // n_rows
    blocks_per_tile = n_rows // n_cols
    tile_cols = local_cols * blocks_per_tile
    padded_rows = tile_rows + 2 * RADIUS
    sent_rows = tile_rows + RADIUS

    me_col = lax.axis_index("tx")
    me_row = lax.axis_index("ty")
    x = jnp.pad(stack, ((0, 0), (0, 0), (RADIUS, RADIUS), (0, 0)))
    start = me_col * blocks_per_tile + me_row % blocks_per_tile
    received = []
    for m in range(n_rows):
        pairs = []
        for col in range(n_cols):
            for row in range(n_rows):
                to_row = (m + col * blocks_per_tile + row % blocks_per_tile) % n_rows
                pairs.append((col * n_rows + row, (row // blocks_per_tile) * n_rows + to_row))
        to_block = (start + m) % n_rows
        first = to_block * tile_rows + RADIUS * (to_block % 2)
        chunk = lax.dynamic_slice_in_dim(x, first, sent_rows, axis=2)
        chunk = chunk.reshape(local_acq * 2 * sent_rows, local_cols)
        received.append(lax.ppermute(chunk, ("tx", "ty"), pairs))
    received = jnp.stack(received, axis=0)
    source = jnp.arange(blocks_per_tile)[:, None] + blocks_per_tile * jnp.arange(n_cols)[None, :]
    order = (me_row - source) % n_rows
    x = jnp.take(received, order.reshape(-1), axis=0)
    x = x.reshape(blocks_per_tile, 2 * count_acq, sent_rows, local_cols)
    even = me_row % 2 == 0
    share = jnp.where(even, x[:, :, sent_rows - RADIUS :], x[:, :, :RADIUS])
    share_shape = share.shape
    partners = [(i, i + 1 - 2 * (i % 2)) for i in range(n_rows)]
    share = lax.ppermute(share.reshape(-1, local_cols), "ty", partners).reshape(share_shape)
    x = jnp.where(even, jnp.concatenate([x, share], axis=2), jnp.concatenate([share, x], axis=2))

    forward = [(i, i + 1) for i in range(n_cols - 1)]
    backward = [(target, source) for source, target in forward]
    left = lax.ppermute(x[blocks_per_tile - 1, :, :, local_cols - LANES :], "tx", forward)
    right = lax.ppermute(x[0, :, :, :LANES], "tx", backward)
    lane = lax.broadcasted_iota(jnp.int32, right.shape, 2)
    zeros = jnp.zeros_like(right)
    edge = jnp.where(lane < RADIUS, right, jnp.where(lane >= LANES - RADIUS, left, zeros))

    mixing = jnp.stack([jnp.stack([filt_re, -filt_im], -1), jnp.stack([filt_im, filt_re], -1)], 1)
    mixing = mixing.reshape(2 * count_acq, 2 * count_acq)
    main = jnp.einsum("kc,bchw->bkhw", mixing, x, preferred_element_type=jnp.float32)
    main = main.astype(jnp.bfloat16).reshape(blocks_per_tile, count_acq, 2, padded_rows, local_cols)
    edge = jnp.einsum("kc,chw->khw", mixing, edge, preferred_element_type=jnp.float32)
    edge = edge.astype(jnp.bfloat16).reshape(count_acq, 2, padded_rows, LANES)
    return pair_maps(main, edge, pre_ids, post_ids, tile_rows, tile_cols)


def solution(mesh):
    in_specs = (P("tx", None, None, "ty"), P(), P(), P(), P())
    out_specs = (P(None, "ty", "tx"), P(None, "ty", "tx"))
    return jax.shard_map(shards, mesh=mesh, in_specs=in_specs, out_specs=out_specs, check_vma=False)
```

```python
import functools

import jax
import jax.numpy as jnp
from jax import lax
from jax.experimental import pallas as pl
from jax.experimental.pallas import tpu as pltpu
from jax.sharding import PartitionSpec as P

RADIUS = 4
LANES = 128
PAIRS_PER_STEP = 4
FIELDS = 4


def window_rows(full, window):
    count = full.shape[0]
    total, offset, span, part = None, 0, 1, full
    remaining = window
    while remaining:
        if remaining & 1:
            shifted = part if offset == 0 else pltpu.roll(part, count - offset, 0)
            total = shifted if total is None else total + shifted
            offset += span
        remaining >>= 1
        if remaining:
            part = part + pltpu.roll(part, count - span, 0)
            span *= 2
    return total


def pair_kernel(pre_ref, post_ref, odd_ref, *refs, tile_rows, tile_cols):
    del pre_ref, post_ref
    pp = PAIRS_PER_STEP
    sides = refs[: 4 * pp]
    band_ref, coh_ref, chg_ref, field_ref, rows_ref, stack_ref = refs[4 * pp :]
    window = 2 * RADIUS + 1
    padded_cols = tile_cols + LANES
    rows = pp * FIELDS * tile_rows
    blocks = tile_cols // LANES
    for p in range(pp):
        a_main, a_edge, b_main, b_edge = sides[4 * p : 4 * p + 4]
        pieces = [(c * a_main.shape[-1], a_main[c, 0], b_main[c, 0]) for c in range(a_main.shape[0])]
        pieces.append((tile_cols, a_edge[0], b_edge[0]))
        for at, a, b in pieces:
            width = a.shape[-1]
            pr = a[0].astype(jnp.float32)
            pi = a[1].astype(jnp.float32)
            qr = b[0].astype(jnp.float32)
            qi = b[1].astype(jnp.float32)
            fields = (pr * pr + pi * pi, qr * qr + qi * qi, pr * qr + pi * qi, pi * qr - pr * qi)
            for f, value in enumerate(fields):
                field_ref[f, :, pl.ds(at, width)] = value
        for f in range(FIELDS):
            cyclic = window_rows(field_ref[f], window)
            rotated = pltpu.roll(cyclic, RADIUS, 0)
            acc = jnp.where(odd_ref[0] == 0, cyclic[:tile_rows], rotated[:tile_rows])
            at = (p * FIELDS + f) * tile_rows
            rows_ref[pl.ds(at, tile_rows), pl.ds(LANES, padded_cols)] = acc
            rows_ref[pl.ds(at, tile_rows), pl.ds(0, LANES)] = acc[:, padded_cols - LANES :]
    rowsum = rows_ref[...]
    high = rowsum.astype(jnp.bfloat16)
    low = (rowsum - high.astype(jnp.float32)).astype(jnp.bfloat16)
    width = 3 * LANES
    for j in range(blocks):
        stack_ref[pl.ds(j * rows, rows), pl.ds(0, width)] = high[:, j * LANES : j * LANES + width]
        stack_ref[pl.ds(j * rows, rows), pl.ds(width, width)] = low[:, j * LANES : j * LANES + width]
    sums = jnp.dot(stack_ref[...], band_ref[...], preferred_element_type=jnp.float32)
    means = sums / float(window * window)
    for j in range(blocks):
        for p in range(pp):
            base = j * rows + p * FIELDS * tile_rows
            pre_power = means[base : base + tile_rows] + 1e-06
            post_power = means[base + tile_rows : base + 2 * tile_rows] + 1e-06
            real_mean = means[base + 2 * tile_rows : base + 3 * tile_rows]
            imag_mean = means[base + 3 * tile_rows : base + 4 * tile_rows]
            coh = jnp.sqrt(real_mean * real_mean + imag_mean * imag_mean) / jnp.sqrt(
                pre_power * post_power
            )
            coh_ref[p, :, pl.ds(j * LANES, LANES)] = coh
            chg_ref[p, :, pl.ds(j * LANES, LANES)] = jnp.log(post_power / pre_power)


def pair_maps(main, edge, pre_ids, post_ids, odd, tile_rows, tile_cols):
    count_pairs = pre_ids.shape[0]
    pp = PAIRS_PER_STEP
    blocks_per_tile, _, _, padded_rows, block_cols = main.shape
    width = 3 * LANES
    lane_in = jnp.arange(width)[:, None]
    lane_out = jnp.arange(LANES)[None, :]
    gap = lane_in - LANES - lane_out
    band = jnp.where((gap >= -RADIUS) & (gap <= RADIUS), 1.0, 0.0).astype(jnp.bfloat16)
    band = jnp.concatenate([band, band], axis=0)
    main_block = (blocks_per_tile, 1, 2, padded_rows, block_cols)
    edge_block = (1, 2, padded_rows, LANES)

    def specs(p, which):
        def main_index(i, pre, post, odd):
            ids = pre if which == 0 else post
            return (0, ids[i * pp + p], 0, 0, 0)

        def edge_index(i, pre, post, odd):
            ids = pre if which == 0 else post
            return (ids[i * pp + p], 0, 0, 0)

        return [pl.BlockSpec(main_block, main_index), pl.BlockSpec(edge_block, edge_index)]

    in_specs = []
    operands = []
    for p in range(pp):
        in_specs += specs(p, 0) + specs(p, 1)
        operands += [main, edge, main, edge]
    in_specs.append(pl.BlockSpec((2 * width, LANES), lambda i, pre, post, odd: (0, 0)))
    operands.append(band)
    out_block = pl.BlockSpec((pp, tile_rows, tile_cols), lambda i, pre, post, odd: (i, 0, 0))
    rows = pp * FIELDS * tile_rows
    blocks = tile_cols // LANES
    padded_cols = tile_cols + LANES
    grid_spec = pltpu.PrefetchScalarGridSpec(
        num_scalar_prefetch=3,
        grid=(count_pairs // pp,),
        in_specs=in_specs,
        out_specs=[out_block, out_block],
        scratch_shapes=[
            pltpu.VMEM((FIELDS, padded_rows, padded_cols), jnp.float32),
            pltpu.VMEM((rows, padded_cols + LANES), jnp.float32),
            pltpu.VMEM((blocks * rows, 2 * width), jnp.bfloat16),
        ],
    )
    out_shape = jax.ShapeDtypeStruct((count_pairs, tile_rows, tile_cols), jnp.float32)
    kernel = functools.partial(pair_kernel, tile_rows=tile_rows, tile_cols=tile_cols)
    return pl.pallas_call(
        kernel,
        grid_spec=grid_spec,
        out_shape=[out_shape, out_shape],
    )(pre_ids, post_ids, odd, *operands)


def shards(stack, filt_re, filt_im, pre_ids, post_ids):
    count_acq = filt_re.shape[0]
    n_rows = lax.axis_size("ty")
    n_cols = lax.axis_size("tx")
    local_acq, _, height, local_cols = stack.shape
    tile_rows = height // n_rows
    blocks_per_tile = n_rows // n_cols
    tile_cols = local_cols * blocks_per_tile
    padded_rows = tile_rows + 2 * RADIUS
    sent_rows = tile_rows + RADIUS

    me_col = lax.axis_index("tx")
    me_row = lax.axis_index("ty")
    x = jnp.pad(stack, ((0, 0), (0, 0), (RADIUS, RADIUS), (0, 0)))
    start = me_col * blocks_per_tile + me_row % blocks_per_tile
    received = []
    for m in range(n_rows):
        pairs = []
        for col in range(n_cols):
            for row in range(n_rows):
                to_row = (m + col * blocks_per_tile + row % blocks_per_tile) % n_rows
                pairs.append((col * n_rows + row, (row // blocks_per_tile) * n_rows + to_row))
        to_block = (start + m) % n_rows
        first = to_block * tile_rows + RADIUS * (to_block % 2)
        chunk = lax.dynamic_slice_in_dim(x, first, sent_rows, axis=2)
        chunk = chunk.reshape(local_acq * 2 * sent_rows, local_cols)
        received.append(lax.ppermute(chunk, ("tx", "ty"), pairs))
    received = jnp.stack(received, axis=0)
    source = jnp.arange(blocks_per_tile)[:, None] + blocks_per_tile * jnp.arange(n_cols)[None, :]
    order = (me_row - source) % n_rows
    x = jnp.take(received, order.reshape(-1), axis=0)
    x = x.reshape(blocks_per_tile, 2 * count_acq, sent_rows, local_cols)
    odd = me_row % 2
    share = lax.dynamic_slice_in_dim(x, (1 - odd) * tile_rows, RADIUS, axis=2)
    share_shape = share.shape
    partners = [(i, i + 1 - 2 * (i % 2)) for i in range(n_rows)]
    share = lax.ppermute(share.reshape(-1, local_cols), "ty", partners).reshape(share_shape)
    x = jnp.concatenate([x, share], axis=2)

    forward = [(i, i + 1) for i in range(n_cols - 1)]
    backward = [(target, source) for source, target in forward]
    left = lax.ppermute(x[blocks_per_tile - 1, :, :, local_cols - LANES :], "tx", forward)
    right = lax.ppermute(x[0, :, :, :LANES], "tx", backward)
    lane = lax.broadcasted_iota(jnp.int32, right.shape, 2)
    zeros = jnp.zeros_like(right)
    edge = jnp.where(lane < RADIUS, right, jnp.where(lane >= LANES - RADIUS, left, zeros))

    mixing = jnp.stack([jnp.stack([filt_re, -filt_im], -1), jnp.stack([filt_im, filt_re], -1)], 1)
    mixing = mixing.reshape(2 * count_acq, 2 * count_acq)
    main = jnp.einsum("kc,bchw->bkhw", mixing, x, preferred_element_type=jnp.float32)
    main = main.astype(jnp.bfloat16).reshape(blocks_per_tile, count_acq, 2, padded_rows, local_cols)
    edge = jnp.einsum("kc,chw->khw", mixing, edge, preferred_element_type=jnp.float32)
    edge = edge.astype(jnp.bfloat16).reshape(count_acq, 2, padded_rows, LANES)
    return pair_maps(main, edge, pre_ids, post_ids, odd.reshape(1).astype(jnp.int32), tile_rows, tile_cols)


def solution(mesh):
    in_specs = (P("tx", None, None, "ty"), P(), P(), P(), P())
    out_specs = (P(None, "ty", "tx"), P(None, "ty", "tx"))
    return jax.shard_map(shards, mesh=mesh, in_specs=in_specs, out_specs=out_specs, check_vma=False)
```

```python
import functools

import jax
import jax.numpy as jnp
from jax import lax
from jax.experimental import pallas as pl
from jax.experimental.pallas import tpu as pltpu
from jax.sharding import PartitionSpec as P

RADIUS = 4
LANES = 128
PAIRS_PER_STEP = 4
FIELDS = 4


def window_rows(full, window):
    count = full.shape[0]
    total, offset, span, part = None, 0, 1, full
    remaining = window
    while remaining:
        if remaining & 1:
            shifted = part if offset == 0 else pltpu.roll(part, count - offset, 0)
            total = shifted if total is None else total + shifted
            offset += span
        remaining >>= 1
        if remaining:
            part = part + pltpu.roll(part, count - span, 0)
            span *= 2
    return total


def pair_kernel(pre_ref, post_ref, main_ref, edge_ref, band_ref, coh_ref, chg_ref, field_ref, rows_ref, stack_ref, *, tile_rows, tile_cols):
    pp = PAIRS_PER_STEP
    step = pl.program_id(0)
    sides = []
    for p in range(pp):
        for ids in (pre_ref, post_ref):
            at = ids[step * pp + p]
            sides += [main_ref.at[:, pl.ds(at, 1)], edge_ref.at[pl.ds(at, 1)]]
    window = 2 * RADIUS + 1
    padded_cols = tile_cols + LANES
    rows = pp * FIELDS * tile_rows
    blocks = tile_cols // LANES
    for p in range(pp):
        a_main, a_edge, b_main, b_edge = sides[4 * p : 4 * p + 4]
        pieces = [(c * a_main.shape[-1], a_main[c, 0], b_main[c, 0]) for c in range(a_main.shape[0])]
        pieces.append((tile_cols, a_edge[0], b_edge[0]))
        for at, a, b in pieces:
            width = a.shape[-1]
            pr = a[0].astype(jnp.float32)
            pi = a[1].astype(jnp.float32)
            qr = b[0].astype(jnp.float32)
            qi = b[1].astype(jnp.float32)
            fields = (pr * pr + pi * pi, qr * qr + qi * qi, pr * qr + pi * qi, pi * qr - pr * qi)
            for f, value in enumerate(fields):
                field_ref[f, :, pl.ds(at, width)] = value
        for f in range(FIELDS):
            acc = window_rows(field_ref[f], window)[:tile_rows]
            at = (p * FIELDS + f) * tile_rows
            rows_ref[pl.ds(at, tile_rows), pl.ds(LANES, padded_cols)] = acc
            rows_ref[pl.ds(at, tile_rows), pl.ds(0, LANES)] = acc[:, padded_cols - LANES :]
    rowsum = rows_ref[...]
    high = rowsum.astype(jnp.bfloat16)
    low = (rowsum - high.astype(jnp.float32)).astype(jnp.bfloat16)
    width = 3 * LANES
    for j in range(blocks):
        stack_ref[pl.ds(j * rows, rows), pl.ds(0, width)] = high[:, j * LANES : j * LANES + width]
        stack_ref[pl.ds(j * rows, rows), pl.ds(width, width)] = low[:, j * LANES : j * LANES + width]
    sums = jnp.dot(stack_ref[...], band_ref[...], preferred_element_type=jnp.float32)
    means = sums / float(window * window)
    for j in range(blocks):
        for p in range(pp):
            base = j * rows + p * FIELDS * tile_rows
            pre_power = means[base : base + tile_rows] + 1e-06
            post_power = means[base + tile_rows : base + 2 * tile_rows] + 1e-06
            real_mean = means[base + 2 * tile_rows : base + 3 * tile_rows]
            imag_mean = means[base + 3 * tile_rows : base + 4 * tile_rows]
            coh = jnp.sqrt(real_mean * real_mean + imag_mean * imag_mean) / jnp.sqrt(
                pre_power * post_power
            )
            coh_ref[p, :, pl.ds(j * LANES, LANES)] = coh
            chg_ref[p, :, pl.ds(j * LANES, LANES)] = jnp.log(post_power / pre_power)


def pair_maps(main, edge, pre_ids, post_ids, tile_rows, tile_cols):
    count_pairs = pre_ids.shape[0]
    pp = PAIRS_PER_STEP
    blocks_per_tile, _, _, padded_rows, block_cols = main.shape
    width = 3 * LANES
    lane_in = jnp.arange(width)[:, None]
    lane_out = jnp.arange(LANES)[None, :]
    gap = lane_in - LANES - lane_out
    band = jnp.where((gap >= -RADIUS) & (gap <= RADIUS), 1.0, 0.0).astype(jnp.bfloat16)
    band = jnp.concatenate([band, band], axis=0)
    in_specs = [
        pl.BlockSpec(main.shape, lambda i, pre, post: (0,) * main.ndim),
        pl.BlockSpec(edge.shape, lambda i, pre, post: (0,) * edge.ndim),
        pl.BlockSpec((2 * width, LANES), lambda i, pre, post: (0, 0)),
    ]
    operands = [main, edge, band]
    out_block = pl.BlockSpec((pp, tile_rows, tile_cols), lambda i, pre, post: (i, 0, 0))
    rows = pp * FIELDS * tile_rows
    blocks = tile_cols // LANES
    padded_cols = tile_cols + LANES
    grid_spec = pltpu.PrefetchScalarGridSpec(
        num_scalar_prefetch=2,
        grid=(count_pairs // pp,),
        in_specs=in_specs,
        out_specs=[out_block, out_block],
        scratch_shapes=[
            pltpu.VMEM((FIELDS, padded_rows, padded_cols), jnp.float32),
            pltpu.VMEM((rows, padded_cols + LANES), jnp.float32),
            pltpu.VMEM((blocks * rows, 2 * width), jnp.bfloat16),
        ],
    )
    out_shape = jax.ShapeDtypeStruct((count_pairs, tile_rows, tile_cols), jnp.float32)
    kernel = functools.partial(pair_kernel, tile_rows=tile_rows, tile_cols=tile_cols)
    return pl.pallas_call(
        kernel,
        grid_spec=grid_spec,
        out_shape=[out_shape, out_shape],
    )(pre_ids, post_ids, *operands)


def shards(stack, filt_re, filt_im, pre_ids, post_ids):
    count_acq = filt_re.shape[0]
    n_rows = lax.axis_size("ty")
    n_cols = lax.axis_size("tx")
    local_acq, _, height, local_cols = stack.shape
    tile_rows = height // n_rows
    blocks_per_tile = n_rows // n_cols
    tile_cols = local_cols * blocks_per_tile
    padded_rows = tile_rows + 2 * RADIUS

    me_col = lax.axis_index("tx")
    me_row = lax.axis_index("ty")
    x = jnp.pad(stack, ((0, 0), (0, 0), (RADIUS, RADIUS), (0, 0)))
    start = me_col * blocks_per_tile + me_row % blocks_per_tile
    received = []
    for m in range(n_rows):
        pairs = []
        for col in range(n_cols):
            for row in range(n_rows):
                to_row = (m + col * blocks_per_tile + row % blocks_per_tile) % n_rows
                pairs.append((col * n_rows + row, (row // blocks_per_tile) * n_rows + to_row))
        first = ((start + m) % n_rows) * tile_rows
        chunk = lax.dynamic_slice_in_dim(x, first, padded_rows, axis=2)
        chunk = chunk.reshape(local_acq * 2 * padded_rows, local_cols)
        received.append(lax.ppermute(chunk, ("tx", "ty"), pairs))
    received = jnp.stack(received, axis=0)
    source = jnp.arange(blocks_per_tile)[:, None] + blocks_per_tile * jnp.arange(n_cols)[None, :]
    order = (me_row - source) % n_rows
    x = jnp.take(received, order.reshape(-1), axis=0)
    x = x.reshape(blocks_per_tile, 2 * count_acq, padded_rows, local_cols)

    forward = [(i, i + 1) for i in range(n_cols - 1)]
    backward = [(target, source) for source, target in forward]
    left = lax.ppermute(x[blocks_per_tile - 1, :, :, local_cols - LANES :], "tx", forward)
    right = lax.ppermute(x[0, :, :, :LANES], "tx", backward)
    lane = lax.broadcasted_iota(jnp.int32, right.shape, 2)
    zeros = jnp.zeros_like(right)
    edge = jnp.where(lane < RADIUS, right, jnp.where(lane >= LANES - RADIUS, left, zeros))

    mixing = jnp.stack([jnp.stack([filt_re, -filt_im], -1), jnp.stack([filt_im, filt_re], -1)], 1)
    mixing = mixing.reshape(2 * count_acq, 2 * count_acq)
    main = jnp.einsum("kc,bchw->bkhw", mixing, x, preferred_element_type=jnp.float32)
    main = main.astype(jnp.bfloat16).reshape(blocks_per_tile, count_acq, 2, padded_rows, local_cols)
    edge = jnp.einsum("kc,chw->khw", mixing, edge, preferred_element_type=jnp.float32)
    edge = edge.astype(jnp.bfloat16).reshape(count_acq, 2, padded_rows, LANES)
    return pair_maps(main, edge, pre_ids, post_ids, tile_rows, tile_cols)


def solution(mesh):
    in_specs = (P("tx", None, None, "ty"), P(), P(), P(), P())
    out_specs = (P(None, "ty", "tx"), P(None, "ty", "tx"))
    return jax.shard_map(shards, mesh=mesh, in_specs=in_specs, out_specs=out_specs, check_vma=False)
```

```python
import functools

import jax
import jax.numpy as jnp
from jax import lax
from jax.experimental import pallas as pl
from jax.experimental.pallas import tpu as pltpu
from jax.sharding import PartitionSpec as P

RADIUS = 4
LANES = 128
PAIRS_PER_STEP = 4
FIELDS = 4


def window_rows(full, window):
    count = full.shape[0]
    total, offset, span, part = None, 0, 1, full
    remaining = window
    while remaining:
        if remaining & 1:
            shifted = part if offset == 0 else pltpu.roll(part, count - offset, 0)
            total = shifted if total is None else total + shifted
            offset += span
        remaining >>= 1
        if remaining:
            part = part + pltpu.roll(part, count - span, 0)
            span *= 2
    return total


def pair_kernel(pre_ref, post_ref, main_ref, edge_ref, band_ref, coh_ref, chg_ref, field_ref, rows_ref, stack_ref, power_ref, *, tile_rows, tile_cols):
    pp = PAIRS_PER_STEP
    count = 2 * pp
    step = pl.program_id(0)
    window = 2 * RADIUS + 1
    padded_cols = tile_cols + LANES
    rows = count * tile_rows
    blocks = tile_cols // LANES
    block_cols = main_ref.shape[-1]

    def pieces(index):
        parts = [(c * block_cols, main_ref[c, index]) for c in range(main_ref.shape[0])]
        parts.append((tile_cols, edge_ref[index]))
        return parts

    def box_pass():
        for f in range(count):
            acc = window_rows(field_ref[f], window)[:tile_rows]
            rows_ref[pl.ds(f * tile_rows, tile_rows), pl.ds(LANES, padded_cols)] = acc
            rows_ref[pl.ds(f * tile_rows, tile_rows), pl.ds(0, LANES)] = acc[:, padded_cols - LANES :]
        rowsum = rows_ref[...]
        high = rowsum.astype(jnp.bfloat16)
        low = (rowsum - high.astype(jnp.float32)).astype(jnp.bfloat16)
        width = 3 * LANES
        for j in range(blocks):
            stack_ref[pl.ds(j * rows, rows), pl.ds(0, width)] = high[:, j * LANES : j * LANES + width]
            stack_ref[pl.ds(j * rows, rows), pl.ds(width, width)] = low[:, j * LANES : j * LANES + width]
        sums = jnp.dot(stack_ref[...], band_ref[...], preferred_element_type=jnp.float32)
        return sums / float(window * window)

    @pl.when(step == 0)
    def _():
        def chunk(k, carry):
            for a in range(count):
                for at, piece in pieces(k * count + a):
                    re = piece[0].astype(jnp.float32)
                    im = piece[1].astype(jnp.float32)
                    field_ref[a, :, pl.ds(at, piece.shape[-1])] = re * re + im * im
            means = box_pass()
            for j in range(blocks):
                for a in range(count):
                    base = j * rows + a * tile_rows
                    power_ref[k * count + a, :, pl.ds(j * LANES, LANES)] = (
                        means[base : base + tile_rows] + 1e-06
                    )
            return carry

        lax.fori_loop(0, main_ref.shape[1] // count, chunk, 0)

    pre_at = [pre_ref[step * pp + p] for p in range(pp)]
    post_at = [post_ref[step * pp + p] for p in range(pp)]
    for p in range(pp):
        for (at, a), (_, b) in zip(pieces(pre_at[p]), pieces(post_at[p])):
            width = a.shape[-1]
            pr = a[0].astype(jnp.float32)
            pi = a[1].astype(jnp.float32)
            qr = b[0].astype(jnp.float32)
            qi = b[1].astype(jnp.float32)
            field_ref[2 * p, :, pl.ds(at, width)] = pr * qr + pi * qi
            field_ref[2 * p + 1, :, pl.ds(at, width)] = pi * qr - pr * qi
    means = box_pass()
    for j in range(blocks):
        for p in range(pp):
            pre_power = power_ref[pre_at[p], :, pl.ds(j * LANES, LANES)]
            post_power = power_ref[post_at[p], :, pl.ds(j * LANES, LANES)]
            base = j * rows + 2 * p * tile_rows
            real_mean = means[base : base + tile_rows]
            imag_mean = means[base + tile_rows : base + 2 * tile_rows]
            coh = jnp.sqrt(real_mean * real_mean + imag_mean * imag_mean) / jnp.sqrt(
                pre_power * post_power
            )
            coh_ref[p, :, pl.ds(j * LANES, LANES)] = coh
            chg_ref[p, :, pl.ds(j * LANES, LANES)] = jnp.log(post_power / pre_power)


def pair_maps(main, edge, pre_ids, post_ids, tile_rows, tile_cols):
    count_pairs = pre_ids.shape[0]
    pp = PAIRS_PER_STEP
    blocks_per_tile, _, _, padded_rows, block_cols = main.shape
    width = 3 * LANES
    lane_in = jnp.arange(width)[:, None]
    lane_out = jnp.arange(LANES)[None, :]
    gap = lane_in - LANES - lane_out
    band = jnp.where((gap >= -RADIUS) & (gap <= RADIUS), 1.0, 0.0).astype(jnp.bfloat16)
    band = jnp.concatenate([band, band], axis=0)
    in_specs = [
        pl.BlockSpec(main.shape, lambda i, pre, post: (0,) * main.ndim),
        pl.BlockSpec(edge.shape, lambda i, pre, post: (0,) * edge.ndim),
        pl.BlockSpec((2 * width, LANES), lambda i, pre, post: (0, 0)),
    ]
    operands = [main, edge, band]
    out_block = pl.BlockSpec((pp, tile_rows, tile_cols), lambda i, pre, post: (i, 0, 0))
    rows = 2 * pp * tile_rows
    blocks = tile_cols // LANES
    padded_cols = tile_cols + LANES
    grid_spec = pltpu.PrefetchScalarGridSpec(
        num_scalar_prefetch=2,
        grid=(count_pairs // pp,),
        in_specs=in_specs,
        out_specs=[out_block, out_block],
        scratch_shapes=[
            pltpu.VMEM((2 * pp, padded_rows, padded_cols), jnp.float32),
            pltpu.VMEM((rows, padded_cols + LANES), jnp.float32),
            pltpu.VMEM((blocks * rows, 2 * width), jnp.bfloat16),
            pltpu.VMEM((main.shape[1], tile_rows, tile_cols), jnp.float32),
        ],
    )
    out_shape = jax.ShapeDtypeStruct((count_pairs, tile_rows, tile_cols), jnp.float32)
    kernel = functools.partial(pair_kernel, tile_rows=tile_rows, tile_cols=tile_cols)
    return pl.pallas_call(
        kernel,
        grid_spec=grid_spec,
        out_shape=[out_shape, out_shape],
    )(pre_ids, post_ids, *operands)


def shards(stack, filt_re, filt_im, pre_ids, post_ids):
    count_acq = filt_re.shape[0]
    n_rows = lax.axis_size("ty")
    n_cols = lax.axis_size("tx")
    local_acq, _, height, local_cols = stack.shape
    tile_rows = height // n_rows
    blocks_per_tile = n_rows // n_cols
    tile_cols = local_cols * blocks_per_tile
    padded_rows = tile_rows + 2 * RADIUS

    me_col = lax.axis_index("tx")
    me_row = lax.axis_index("ty")
    x = jnp.pad(stack, ((0, 0), (0, 0), (RADIUS, RADIUS), (0, 0)))
    start = me_col * blocks_per_tile + me_row % blocks_per_tile
    received = []
    for m in range(n_rows):
        pairs = []
        for col in range(n_cols):
            for row in range(n_rows):
                to_row = (m + col * blocks_per_tile + row % blocks_per_tile) % n_rows
                pairs.append((col * n_rows + row, (row // blocks_per_tile) * n_rows + to_row))
        first = ((start + m) % n_rows) * tile_rows
        chunk = lax.dynamic_slice_in_dim(x, first, padded_rows, axis=2)
        chunk = chunk.reshape(local_acq * 2 * padded_rows, local_cols)
        received.append(lax.ppermute(chunk, ("tx", "ty"), pairs))
    received = jnp.stack(received, axis=0)
    source = jnp.arange(blocks_per_tile)[:, None] + blocks_per_tile * jnp.arange(n_cols)[None, :]
    order = (me_row - source) % n_rows
    x = jnp.take(received, order.reshape(-1), axis=0)
    x = x.reshape(blocks_per_tile, 2 * count_acq, padded_rows, local_cols)

    forward = [(i, i + 1) for i in range(n_cols - 1)]
    backward = [(target, source) for source, target in forward]
    left = lax.ppermute(x[blocks_per_tile - 1, :, :, local_cols - LANES :], "tx", forward)
    right = lax.ppermute(x[0, :, :, :LANES], "tx", backward)
    lane = lax.broadcasted_iota(jnp.int32, right.shape, 2)
    zeros = jnp.zeros_like(right)
    edge = jnp.where(lane < RADIUS, right, jnp.where(lane >= LANES - RADIUS, left, zeros))

    mixing = jnp.stack([jnp.stack([filt_re, -filt_im], -1), jnp.stack([filt_im, filt_re], -1)], 1)
    mixing = mixing.reshape(2 * count_acq, 2 * count_acq)
    main = jnp.einsum("kc,bchw->bkhw", mixing, x, preferred_element_type=jnp.float32)
    main = main.astype(jnp.bfloat16).reshape(blocks_per_tile, count_acq, 2, padded_rows, local_cols)
    edge = jnp.einsum("kc,chw->khw", mixing, edge, preferred_element_type=jnp.float32)
    edge = edge.astype(jnp.bfloat16).reshape(count_acq, 2, padded_rows, LANES)
    return pair_maps(main, edge, pre_ids, post_ids, tile_rows, tile_cols)


def solution(mesh):
    in_specs = (P("tx", None, None, "ty"), P(), P(), P(), P())
    out_specs = (P(None, "ty", "tx"), P(None, "ty", "tx"))
    return jax.shard_map(shards, mesh=mesh, in_specs=in_specs, out_specs=out_specs, check_vma=False)
```

```python
import functools

import jax
import jax.numpy as jnp
from jax import lax
from jax.experimental import pallas as pl
from jax.experimental.pallas import tpu as pltpu
from jax.sharding import PartitionSpec as P

RADIUS = 4
LANES = 128
PAIRS_PER_STEP = 8
FIELDS = 4


def window_rows(full, window):
    count = full.shape[0]
    total, offset, span, part = None, 0, 1, full
    remaining = window
    while remaining:
        if remaining & 1:
            shifted = part if offset == 0 else pltpu.roll(part, count - offset, 0)
            total = shifted if total is None else total + shifted
            offset += span
        remaining >>= 1
        if remaining:
            part = part + pltpu.roll(part, count - span, 0)
            span *= 2
    return total


def pair_kernel(pre_ref, post_ref, main_ref, edge_ref, band_ref, coh_ref, chg_ref, field_ref, rows_ref, stack_ref, power_ref, *, tile_rows, tile_cols):
    pp = PAIRS_PER_STEP
    count = 2 * pp
    step = pl.program_id(0)
    window = 2 * RADIUS + 1
    padded_cols = tile_cols + LANES
    rows = count * tile_rows
    blocks = tile_cols // LANES
    block_cols = main_ref.shape[-1]

    def pieces(index):
        parts = [(c * block_cols, main_ref[c, index]) for c in range(main_ref.shape[0])]
        parts.append((tile_cols, edge_ref[index]))
        return parts

    def box_pass():
        for f in range(count):
            acc = window_rows(field_ref[f], window)[:tile_rows]
            rows_ref[pl.ds(f * tile_rows, tile_rows), pl.ds(LANES, padded_cols)] = acc
            rows_ref[pl.ds(f * tile_rows, tile_rows), pl.ds(0, LANES)] = acc[:, padded_cols - LANES :]
        rowsum = rows_ref[...]
        high = rowsum.astype(jnp.bfloat16)
        low = (rowsum - high.astype(jnp.float32)).astype(jnp.bfloat16)
        width = 3 * LANES
        for j in range(blocks):
            stack_ref[pl.ds(j * rows, rows), pl.ds(0, width)] = high[:, j * LANES : j * LANES + width]
            stack_ref[pl.ds(j * rows, rows), pl.ds(width, width)] = low[:, j * LANES : j * LANES + width]
        sums = jnp.dot(stack_ref[...], band_ref[...], preferred_element_type=jnp.float32)
        return sums / float(window * window)

    @pl.when(step == 0)
    def _():
        def chunk(k, carry):
            for a in range(count):
                for at, piece in pieces(k * count + a):
                    re = piece[0].astype(jnp.float32)
                    im = piece[1].astype(jnp.float32)
                    field_ref[a, :, pl.ds(at, piece.shape[-1])] = re * re + im * im
            means = box_pass()
            for j in range(blocks):
                for a in range(count):
                    base = j * rows + a * tile_rows
                    power_ref[k * count + a, :, pl.ds(j * LANES, LANES)] = (
                        means[base : base + tile_rows] + 1e-06
                    )
            return carry

        lax.fori_loop(0, main_ref.shape[1] // count, chunk, 0)

    pre_at = [pre_ref[step * pp + p] for p in range(pp)]
    post_at = [post_ref[step * pp + p] for p in range(pp)]
    for p in range(pp):
        for (at, a), (_, b) in zip(pieces(pre_at[p]), pieces(post_at[p])):
            width = a.shape[-1]
            pr = a[0].astype(jnp.float32)
            pi = a[1].astype(jnp.float32)
            qr = b[0].astype(jnp.float32)
            qi = b[1].astype(jnp.float32)
            field_ref[2 * p, :, pl.ds(at, width)] = pr * qr + pi * qi
            field_ref[2 * p + 1, :, pl.ds(at, width)] = pi * qr - pr * qi
    means = box_pass()
    for j in range(blocks):
        for p in range(pp):
            pre_power = power_ref[pre_at[p], :, pl.ds(j * LANES, LANES)]
            post_power = power_ref[post_at[p], :, pl.ds(j * LANES, LANES)]
            base = j * rows + 2 * p * tile_rows
            real_mean = means[base : base + tile_rows]
            imag_mean = means[base + tile_rows : base + 2 * tile_rows]
            coh = jnp.sqrt(real_mean * real_mean + imag_mean * imag_mean) / jnp.sqrt(
                pre_power * post_power
            )
            coh_ref[p, :, pl.ds(j * LANES, LANES)] = coh
            chg_ref[p, :, pl.ds(j * LANES, LANES)] = jnp.log(post_power / pre_power)


def pair_maps(main, edge, pre_ids, post_ids, tile_rows, tile_cols):
    count_pairs = pre_ids.shape[0]
    pp = PAIRS_PER_STEP
    blocks_per_tile, _, _, padded_rows, block_cols = main.shape
    width = 3 * LANES
    lane_in = jnp.arange(width)[:, None]
    lane_out = jnp.arange(LANES)[None, :]
    gap = lane_in - LANES - lane_out
    band = jnp.where((gap >= -RADIUS) & (gap <= RADIUS), 1.0, 0.0).astype(jnp.bfloat16)
    band = jnp.concatenate([band, band], axis=0)
    in_specs = [
        pl.BlockSpec(main.shape, lambda i, pre, post: (0,) * main.ndim),
        pl.BlockSpec(edge.shape, lambda i, pre, post: (0,) * edge.ndim),
        pl.BlockSpec((2 * width, LANES), lambda i, pre, post: (0, 0)),
    ]
    operands = [main, edge, band]
    out_block = pl.BlockSpec((pp, tile_rows, tile_cols), lambda i, pre, post: (i, 0, 0))
    rows = 2 * pp * tile_rows
    blocks = tile_cols // LANES
    padded_cols = tile_cols + LANES
    grid_spec = pltpu.PrefetchScalarGridSpec(
        num_scalar_prefetch=2,
        grid=(count_pairs // pp,),
        in_specs=in_specs,
        out_specs=[out_block, out_block],
        scratch_shapes=[
            pltpu.VMEM((2 * pp, padded_rows, padded_cols), jnp.float32),
            pltpu.VMEM((rows, padded_cols + LANES), jnp.float32),
            pltpu.VMEM((blocks * rows, 2 * width), jnp.bfloat16),
            pltpu.VMEM((main.shape[1], tile_rows, tile_cols), jnp.float32),
        ],
    )
    out_shape = jax.ShapeDtypeStruct((count_pairs, tile_rows, tile_cols), jnp.float32)
    kernel = functools.partial(pair_kernel, tile_rows=tile_rows, tile_cols=tile_cols)
    return pl.pallas_call(
        kernel,
        grid_spec=grid_spec,
        out_shape=[out_shape, out_shape],
    )(pre_ids, post_ids, *operands)


def shards(stack, filt_re, filt_im, pre_ids, post_ids):
    count_acq = filt_re.shape[0]
    n_rows = lax.axis_size("ty")
    n_cols = lax.axis_size("tx")
    local_acq, _, height, local_cols = stack.shape
    tile_rows = height // n_rows
    blocks_per_tile = n_rows // n_cols
    tile_cols = local_cols * blocks_per_tile
    padded_rows = tile_rows + 2 * RADIUS

    me_col = lax.axis_index("tx")
    me_row = lax.axis_index("ty")
    x = jnp.pad(stack, ((0, 0), (0, 0), (RADIUS, RADIUS), (0, 0)))
    start = me_col * blocks_per_tile + me_row % blocks_per_tile
    received = []
    for m in range(n_rows):
        pairs = []
        for col in range(n_cols):
            for row in range(n_rows):
                to_row = (m + col * blocks_per_tile + row % blocks_per_tile) % n_rows
                pairs.append((col * n_rows + row, (row // blocks_per_tile) * n_rows + to_row))
        first = ((start + m) % n_rows) * tile_rows
        chunk = lax.dynamic_slice_in_dim(x, first, padded_rows, axis=2)
        chunk = chunk.reshape(local_acq * 2 * padded_rows, local_cols)
        received.append(lax.ppermute(chunk, ("tx", "ty"), pairs))
    received = jnp.stack(received, axis=0)
    source = jnp.arange(blocks_per_tile)[:, None] + blocks_per_tile * jnp.arange(n_cols)[None, :]
    order = (me_row - source) % n_rows
    x = jnp.take(received, order.reshape(-1), axis=0)
    x = x.reshape(blocks_per_tile, 2 * count_acq, padded_rows, local_cols)

    forward = [(i, i + 1) for i in range(n_cols - 1)]
    backward = [(target, source) for source, target in forward]
    left = lax.ppermute(x[blocks_per_tile - 1, :, :, local_cols - LANES :], "tx", forward)
    right = lax.ppermute(x[0, :, :, :LANES], "tx", backward)
    lane = lax.broadcasted_iota(jnp.int32, right.shape, 2)
    zeros = jnp.zeros_like(right)
    edge = jnp.where(lane < RADIUS, right, jnp.where(lane >= LANES - RADIUS, left, zeros))

    mixing = jnp.stack([jnp.stack([filt_re, -filt_im], -1), jnp.stack([filt_im, filt_re], -1)], 1)
    mixing = mixing.reshape(2 * count_acq, 2 * count_acq)
    main = jnp.einsum("kc,bchw->bkhw", mixing, x, preferred_element_type=jnp.float32)
    main = main.astype(jnp.bfloat16).reshape(blocks_per_tile, count_acq, 2, padded_rows, local_cols)
    edge = jnp.einsum("kc,chw->khw", mixing, edge, preferred_element_type=jnp.float32)
    edge = edge.astype(jnp.bfloat16).reshape(count_acq, 2, padded_rows, LANES)
    return pair_maps(main, edge, pre_ids, post_ids, tile_rows, tile_cols)


def solution(mesh):
    in_specs = (P("tx", None, None, "ty"), P(), P(), P(), P())
    out_specs = (P(None, "ty", "tx"), P(None, "ty", "tx"))
    return jax.shard_map(shards, mesh=mesh, in_specs=in_specs, out_specs=out_specs, check_vma=False)
```

```python
import functools

import jax
import jax.numpy as jnp
from jax import lax
from jax.experimental import pallas as pl
from jax.experimental.pallas import tpu as pltpu
from jax.sharding import PartitionSpec as P

RADIUS = 4
LANES = 128
PAIRS_PER_STEP = 8
FIELDS = 4


def window_rows(full, window):
    count = full.shape[0]
    total, offset, span, part = None, 0, 1, full
    remaining = window
    while remaining:
        if remaining & 1:
            shifted = part if offset == 0 else pltpu.roll(part, count - offset, 0)
            total = shifted if total is None else total + shifted
            offset += span
        remaining >>= 1
        if remaining:
            part = part + pltpu.roll(part, count - span, 0)
            span *= 2
    return total


def pair_kernel(pre_ref, post_ref, main_ref, edge_ref, band_ref, coh_ref, chg_ref, field_ref, rows_ref, stack_ref, power_ref, *, tile_rows, tile_cols):
    pp = PAIRS_PER_STEP
    count = 2 * pp
    step = pl.program_id(0)
    window = 2 * RADIUS + 1
    padded_cols = tile_cols + LANES
    rows = count * tile_rows
    blocks = tile_cols // LANES
    block_cols = main_ref.shape[-1]

    def pieces(index):
        parts = [(c * block_cols, main_ref[c, index]) for c in range(main_ref.shape[0])]
        parts.append((tile_cols, edge_ref[index]))
        return parts

    def box_pass():
        for f in range(count):
            acc = window_rows(field_ref[f], window)[:tile_rows]
            rows_ref[pl.ds(f * tile_rows, tile_rows), pl.ds(LANES, padded_cols)] = acc
            rows_ref[pl.ds(f * tile_rows, tile_rows), pl.ds(0, LANES)] = acc[:, padded_cols - LANES :]
        rowsum = rows_ref[...]
        high = rowsum.astype(jnp.bfloat16)
        low = (rowsum - high.astype(jnp.float32)).astype(jnp.bfloat16)
        width = 3 * LANES
        for j in range(blocks):
            stack_ref[pl.ds(j * rows, rows), pl.ds(0, width)] = high[:, j * LANES : j * LANES + width]
            stack_ref[pl.ds(j * rows, rows), pl.ds(width, width)] = low[:, j * LANES : j * LANES + width]
        sums = jnp.dot(stack_ref[...], band_ref[...], preferred_element_type=jnp.float32)
        return sums / float(window * window)

    @pl.when(step == 0)
    def _():
        def chunk(k, carry):
            for a in range(count):
                for at, piece in pieces(k * count + a):
                    re = piece[0].astype(jnp.float32)
                    im = piece[1].astype(jnp.float32)
                    field_ref[a, :, pl.ds(at, piece.shape[-1])] = re * re + im * im
            means = box_pass()
            for j in range(blocks):
                for a in range(count):
                    base = j * rows + a * tile_rows
                    power_ref[k * count + a, :, pl.ds(j * LANES, LANES)] = (
                        means[base : base + tile_rows] + 1e-06
                    )
            return carry

        lax.fori_loop(0, main_ref.shape[1] // count, chunk, 0)

    pre_at = [pre_ref[step * pp + p] for p in range(pp)]
    post_at = [post_ref[step * pp + p] for p in range(pp)]
    for p in range(pp):
        for (at, a), (_, b) in zip(pieces(pre_at[p]), pieces(post_at[p])):
            width = a.shape[-1]
            pr = a[0].astype(jnp.float32)
            pi = a[1].astype(jnp.float32)
            qr = b[0].astype(jnp.float32)
            qi = b[1].astype(jnp.float32)
            field_ref[2 * p, :, pl.ds(at, width)] = pr * qr + pi * qi
            field_ref[2 * p + 1, :, pl.ds(at, width)] = pi * qr - pr * qi
    means = box_pass()
    for j in range(blocks):
        for p in range(pp):
            pre_power = power_ref[pre_at[p], :, pl.ds(j * LANES, LANES)]
            post_power = power_ref[post_at[p], :, pl.ds(j * LANES, LANES)]
            base = j * rows + 2 * p * tile_rows
            real_mean = means[base : base + tile_rows]
            imag_mean = means[base + tile_rows : base + 2 * tile_rows]
            coh = jnp.sqrt(real_mean * real_mean + imag_mean * imag_mean) / jnp.sqrt(
                pre_power * post_power
            )
            coh_ref[p, :, pl.ds(j * LANES, LANES)] = coh
            chg_ref[p, :, pl.ds(j * LANES, LANES)] = jnp.log(post_power / pre_power)


def pair_maps(main, edge, pre_ids, post_ids, tile_rows, tile_cols):
    count_pairs = pre_ids.shape[0]
    pp = PAIRS_PER_STEP
    blocks_per_tile, _, _, padded_rows, block_cols = main.shape
    width = 3 * LANES
    lane_in = jnp.arange(width)[:, None]
    lane_out = jnp.arange(LANES)[None, :]
    gap = lane_in - LANES - lane_out
    band = jnp.where((gap >= -RADIUS) & (gap <= RADIUS), 1.0, 0.0).astype(jnp.bfloat16)
    band = jnp.concatenate([band, band], axis=0)
    in_specs = [
        pl.BlockSpec(main.shape, lambda i, pre, post: (0,) * main.ndim),
        pl.BlockSpec(edge.shape, lambda i, pre, post: (0,) * edge.ndim),
        pl.BlockSpec((2 * width, LANES), lambda i, pre, post: (0, 0)),
    ]
    operands = [main, edge, band]
    out_block = pl.BlockSpec((pp, tile_rows, tile_cols), lambda i, pre, post: (i, 0, 0))
    rows = 2 * pp * tile_rows
    blocks = tile_cols // LANES
    padded_cols = tile_cols + LANES
    grid_spec = pltpu.PrefetchScalarGridSpec(
        num_scalar_prefetch=2,
        grid=(count_pairs // pp,),
        in_specs=in_specs,
        out_specs=[out_block, out_block],
        scratch_shapes=[
            pltpu.VMEM((2 * pp, padded_rows, padded_cols), jnp.float32),
            pltpu.VMEM((rows, padded_cols + LANES), jnp.float32),
            pltpu.VMEM((blocks * rows, 2 * width), jnp.bfloat16),
            pltpu.VMEM((main.shape[1], tile_rows, tile_cols), jnp.float32),
        ],
    )
    out_shape = jax.ShapeDtypeStruct((count_pairs, tile_rows, tile_cols), jnp.float32)
    kernel = functools.partial(pair_kernel, tile_rows=tile_rows, tile_cols=tile_cols)
    return pl.pallas_call(
        kernel,
        grid_spec=grid_spec,
        out_shape=[out_shape, out_shape],
    )(pre_ids, post_ids, *operands)


def shards(stack, filt_re, filt_im, pre_ids, post_ids):
    count_acq = filt_re.shape[0]
    n_rows = lax.axis_size("ty")
    n_cols = lax.axis_size("tx")
    local_acq, _, height, local_cols = stack.shape
    tile_rows = height // n_rows
    blocks_per_tile = n_rows // n_cols
    tile_cols = local_cols * blocks_per_tile
    padded_rows = tile_rows + 2 * RADIUS

    me_col = lax.axis_index("tx")
    me_row = lax.axis_index("ty")
    start = me_col * blocks_per_tile + me_row % blocks_per_tile
    received = []
    for m in range(n_rows):
        pairs = []
        for col in range(n_cols):
            for row in range(n_rows):
                to_row = (m + col * blocks_per_tile + row % blocks_per_tile) % n_rows
                pairs.append((col * n_rows + row, (row // blocks_per_tile) * n_rows + to_row))
        block = (start + m) % n_rows
        first = block * tile_rows
        top = lax.dynamic_slice_in_dim(stack, jnp.maximum(first - RADIUS, 0), RADIUS, axis=2)
        top = jnp.where(block > 0, top, jnp.zeros_like(top))
        bottom = lax.dynamic_slice_in_dim(
            stack, jnp.minimum(first + tile_rows, height - RADIUS), RADIUS, axis=2
        )
        bottom = jnp.where(block < n_rows - 1, bottom, jnp.zeros_like(bottom))
        middle = lax.dynamic_slice_in_dim(stack, first, tile_rows, axis=2)
        chunk = jnp.concatenate([top, middle, bottom], axis=2)
        chunk = chunk.reshape(local_acq * 2 * padded_rows, local_cols)
        received.append(lax.ppermute(chunk, ("tx", "ty"), pairs))
    received = jnp.stack(received, axis=0)
    source = jnp.arange(blocks_per_tile)[:, None] + blocks_per_tile * jnp.arange(n_cols)[None, :]
    order = (me_row - source) % n_rows
    x = jnp.take(received, order.reshape(-1), axis=0)
    x = x.reshape(blocks_per_tile, 2 * count_acq, padded_rows, local_cols)

    forward = [(i, i + 1) for i in range(n_cols - 1)]
    backward = [(target, source) for source, target in forward]
    left = lax.ppermute(x[blocks_per_tile - 1, :, :, local_cols - LANES :], "tx", forward)
    right = lax.ppermute(x[0, :, :, :LANES], "tx", backward)
    lane = lax.broadcasted_iota(jnp.int32, right.shape, 2)
    zeros = jnp.zeros_like(right)
    edge = jnp.where(lane < RADIUS, right, jnp.where(lane >= LANES - RADIUS, left, zeros))

    mixing = jnp.stack([jnp.stack([filt_re, -filt_im], -1), jnp.stack([filt_im, filt_re], -1)], 1)
    mixing = mixing.reshape(2 * count_acq, 2 * count_acq)
    main = jnp.einsum("kc,bchw->bkhw", mixing, x, preferred_element_type=jnp.float32)
    main = main.astype(jnp.bfloat16).reshape(blocks_per_tile, count_acq, 2, padded_rows, local_cols)
    edge = jnp.einsum("kc,chw->khw", mixing, edge, preferred_element_type=jnp.float32)
    edge = edge.astype(jnp.bfloat16).reshape(count_acq, 2, padded_rows, LANES)
    return pair_maps(main, edge, pre_ids, post_ids, tile_rows, tile_cols)


def solution(mesh):
    in_specs = (P("tx", None, None, "ty"), P(), P(), P(), P())
    out_specs = (P(None, "ty", "tx"), P(None, "ty", "tx"))
    return jax.shard_map(shards, mesh=mesh, in_specs=in_specs, out_specs=out_specs, check_vma=False)
```

```python
import functools

import jax
import jax.numpy as jnp
from jax import lax
from jax.experimental import pallas as pl
from jax.experimental.pallas import tpu as pltpu
from jax.sharding import PartitionSpec as P

RADIUS = 4
LANES = 128
PAIRS_PER_STEP = 8
FIELDS = 4


def window_rows(full, window):
    count = full.shape[0]
    total, offset, span, part = None, 0, 1, full
    remaining = window
    while remaining:
        if remaining & 1:
            shifted = part if offset == 0 else pltpu.roll(part, count - offset, 0)
            total = shifted if total is None else total + shifted
            offset += span
        remaining >>= 1
        if remaining:
            part = part + pltpu.roll(part, count - span, 0)
            span *= 2
    return total


def pair_kernel(pre_ref, post_ref, main_ref, edge_ref, band_ref, coh_ref, chg_ref, field_ref, rows_ref, stack_ref, power_ref, *, tile_rows, tile_cols):
    pp = PAIRS_PER_STEP
    count = 2 * pp
    step = pl.program_id(0)
    window = 2 * RADIUS + 1
    padded_cols = tile_cols + LANES
    rows = count * tile_rows
    blocks = tile_cols // LANES
    block_cols = main_ref.shape[-1]

    def pieces(index):
        parts = [(c * block_cols, main_ref[c, index]) for c in range(main_ref.shape[0])]
        parts.append((tile_cols, edge_ref[index]))
        return parts

    def box_pass():
        for f in range(count):
            acc = window_rows(field_ref[f], window)[:tile_rows]
            rows_ref[pl.ds(f * tile_rows, tile_rows), pl.ds(LANES, padded_cols)] = acc
            rows_ref[pl.ds(f * tile_rows, tile_rows), pl.ds(0, LANES)] = acc[:, padded_cols - LANES :]
        rowsum = rows_ref[...]
        high = rowsum.astype(jnp.bfloat16)
        low = (rowsum - high.astype(jnp.float32)).astype(jnp.bfloat16)
        width = 3 * LANES
        for j in range(blocks):
            stack_ref[pl.ds(j * rows, rows), pl.ds(0, width)] = high[:, j * LANES : j * LANES + width]
            stack_ref[pl.ds(j * rows, rows), pl.ds(width, width)] = low[:, j * LANES : j * LANES + width]
        sums = jnp.dot(stack_ref[...], band_ref[...], preferred_element_type=jnp.float32)
        return sums / float(window * window)

    @pl.when(step == 0)
    def _():
        def chunk(k, carry):
            for a in range(count):
                for at, piece in pieces(k * count + a):
                    re = piece[0].astype(jnp.float32)
                    im = piece[1].astype(jnp.float32)
                    field_ref[a, :, pl.ds(at, piece.shape[-1])] = re * re + im * im
            means = box_pass()
            for j in range(blocks):
                for a in range(count):
                    base = j * rows + a * tile_rows
                    power_ref[k * count + a, :, pl.ds(j * LANES, LANES)] = (
                        means[base : base + tile_rows] + 1e-06
                    )
            return carry

        lax.fori_loop(0, main_ref.shape[1] // count, chunk, 0)

    pre_at = [pre_ref[step * pp + p] for p in range(pp)]
    post_at = [post_ref[step * pp + p] for p in range(pp)]
    for p in range(pp):
        for (at, a), (_, b) in zip(pieces(pre_at[p]), pieces(post_at[p])):
            width = a.shape[-1]
            pr = a[0].astype(jnp.float32)
            pi = a[1].astype(jnp.float32)
            qr = b[0].astype(jnp.float32)
            qi = b[1].astype(jnp.float32)
            field_ref[2 * p, :, pl.ds(at, width)] = pr * qr + pi * qi
            field_ref[2 * p + 1, :, pl.ds(at, width)] = pi * qr - pr * qi
    means = box_pass()
    for j in range(blocks):
        for p in range(pp):
            pre_power = power_ref[pre_at[p], :, pl.ds(j * LANES, LANES)]
            post_power = power_ref[post_at[p], :, pl.ds(j * LANES, LANES)]
            base = j * rows + 2 * p * tile_rows
            real_mean = means[base : base + tile_rows]
            imag_mean = means[base + tile_rows : base + 2 * tile_rows]
            coh = jnp.sqrt(real_mean * real_mean + imag_mean * imag_mean) / jnp.sqrt(
                pre_power * post_power
            )
            coh_ref[p, :, pl.ds(j * LANES, LANES)] = coh
            chg_ref[p, :, pl.ds(j * LANES, LANES)] = jnp.log(post_power / pre_power)


def pair_maps(main, edge, pre_ids, post_ids, tile_rows, tile_cols):
    count_pairs = pre_ids.shape[0]
    pp = PAIRS_PER_STEP
    blocks_per_tile, _, _, padded_rows, block_cols = main.shape
    width = 3 * LANES
    lane_in = jnp.arange(width)[:, None]
    lane_out = jnp.arange(LANES)[None, :]
    gap = lane_in - LANES - lane_out
    band = jnp.where((gap >= -RADIUS) & (gap <= RADIUS), 1.0, 0.0).astype(jnp.bfloat16)
    band = jnp.concatenate([band, band], axis=0)
    in_specs = [
        pl.BlockSpec(main.shape, lambda i, pre, post: (0,) * main.ndim),
        pl.BlockSpec(edge.shape, lambda i, pre, post: (0,) * edge.ndim),
        pl.BlockSpec((2 * width, LANES), lambda i, pre, post: (0, 0)),
    ]
    operands = [main, edge, band]
    out_block = pl.BlockSpec((pp, tile_rows, tile_cols), lambda i, pre, post: (i, 0, 0))
    rows = 2 * pp * tile_rows
    blocks = tile_cols // LANES
    padded_cols = tile_cols + LANES
    grid_spec = pltpu.PrefetchScalarGridSpec(
        num_scalar_prefetch=2,
        grid=(count_pairs // pp,),
        in_specs=in_specs,
        out_specs=[out_block, out_block],
        scratch_shapes=[
            pltpu.VMEM((2 * pp, padded_rows, padded_cols), jnp.float32),
            pltpu.VMEM((rows, padded_cols + LANES), jnp.float32),
            pltpu.VMEM((blocks * rows, 2 * width), jnp.bfloat16),
            pltpu.VMEM((main.shape[1], tile_rows, tile_cols), jnp.float32),
        ],
    )
    out_shape = jax.ShapeDtypeStruct((count_pairs, tile_rows, tile_cols), jnp.float32)
    kernel = functools.partial(pair_kernel, tile_rows=tile_rows, tile_cols=tile_cols)
    return pl.pallas_call(
        kernel,
        grid_spec=grid_spec,
        out_shape=[out_shape, out_shape],
    )(pre_ids, post_ids, *operands)


def shards(stack, filt_re, filt_im, pre_ids, post_ids):
    count_acq = filt_re.shape[0]
    n_rows = lax.axis_size("ty")
    n_cols = lax.axis_size("tx")
    local_acq, _, height, local_cols = stack.shape
    tile_rows = height // n_rows
    blocks_per_tile = n_rows // n_cols
    tile_cols = local_cols * blocks_per_tile
    padded_rows = tile_rows + 2 * RADIUS

    me_col = lax.axis_index("tx")
    me_row = lax.axis_index("ty")
    x = jnp.pad(stack, ((0, 0), (0, 0), (RADIUS, RADIUS), (0, 0)))
    start = me_col * blocks_per_tile + me_row % blocks_per_tile
    received = []
    for m in range(n_rows):
        pairs = []
        for col in range(n_cols):
            for row in range(n_rows):
                to_row = (m + col * blocks_per_tile + row % blocks_per_tile) % n_rows
                pairs.append((col * n_rows + row, (row // blocks_per_tile) * n_rows + to_row))
        first = ((start + m) % n_rows) * tile_rows
        chunk = lax.dynamic_slice_in_dim(x, first, padded_rows, axis=2)
        chunk = chunk.reshape(local_acq * 2 * padded_rows, local_cols)
        received.append(lax.ppermute(chunk, ("tx", "ty"), pairs))
    received = jnp.stack(received, axis=0)
    source = jnp.arange(blocks_per_tile)[:, None] + blocks_per_tile * jnp.arange(n_cols)[None, :]
    order = (me_row - source) % n_rows
    x = jnp.take(received, order.reshape(-1), axis=0)
    x = x.reshape(blocks_per_tile, 2 * count_acq, padded_rows, local_cols)

    forward = [(i, i + 1) for i in range(n_cols - 1)]
    backward = [(target, source) for source, target in forward]
    halo_shape = (2 * count_acq, padded_rows, LANES)
    left = jnp.take(received, order[blocks_per_tile - 1], axis=0)[:, :, local_cols - LANES :]
    right = jnp.take(received, order[0], axis=0)[:, :, :LANES]
    left = lax.ppermute(left, "tx", forward).reshape(halo_shape)
    right = lax.ppermute(right, "tx", backward).reshape(halo_shape)
    lane = lax.broadcasted_iota(jnp.int32, right.shape, 2)
    zeros = jnp.zeros_like(right)
    edge = jnp.where(lane < RADIUS, right, jnp.where(lane >= LANES - RADIUS, left, zeros))

    mixing = jnp.stack([jnp.stack([filt_re, -filt_im], -1), jnp.stack([filt_im, filt_re], -1)], 1)
    mixing = mixing.reshape(2 * count_acq, 2 * count_acq)
    main = jnp.einsum("kc,bchw->bkhw", mixing, x, preferred_element_type=jnp.float32)
    main = main.astype(jnp.bfloat16).reshape(blocks_per_tile, count_acq, 2, padded_rows, local_cols)
    edge = jnp.einsum("kc,chw->khw", mixing, edge, preferred_element_type=jnp.float32)
    edge = edge.astype(jnp.bfloat16).reshape(count_acq, 2, padded_rows, LANES)
    return pair_maps(main, edge, pre_ids, post_ids, tile_rows, tile_cols)


def solution(mesh):
    in_specs = (P("tx", None, None, "ty"), P(), P(), P(), P())
    out_specs = (P(None, "ty", "tx"), P(None, "ty", "tx"))
    return jax.shard_map(shards, mesh=mesh, in_specs=in_specs, out_specs=out_specs, check_vma=False)
```

```python
import functools

import jax
import jax.numpy as jnp
from jax import lax
from jax.experimental import pallas as pl
from jax.experimental.pallas import tpu as pltpu
from jax.sharding import PartitionSpec as P

RADIUS = 4
LANES = 128
PAIRS_PER_STEP = 8
FIELDS = 4


def window_rows(full, window):
    count = full.shape[0]
    total, offset, span, part = None, 0, 1, full
    remaining = window
    while remaining:
        if remaining & 1:
            shifted = part if offset == 0 else pltpu.roll(part, count - offset, 0)
            total = shifted if total is None else total + shifted
            offset += span
        remaining >>= 1
        if remaining:
            part = part + pltpu.roll(part, count - span, 0)
            span *= 2
    return total


def pair_kernel(pre_ref, post_ref, main_ref, edge_ref, band_ref, coh_ref, chg_ref, field_ref, rows_ref, stack_ref, power_ref, *, tile_rows, tile_cols):
    pp = PAIRS_PER_STEP
    count = 2 * pp
    step = pl.program_id(0)
    window = 2 * RADIUS + 1
    padded_cols = tile_cols + LANES
    rows = count * tile_rows
    blocks = tile_cols // LANES
    block_cols = main_ref.shape[-1]

    def pieces(index):
        parts = [(c * block_cols, main_ref[c, index]) for c in range(main_ref.shape[0])]
        parts.append((tile_cols, edge_ref[index]))
        return parts

    def box_pass():
        for f in range(count):
            acc = window_rows(field_ref[f], window)[:tile_rows]
            rows_ref[pl.ds(f * tile_rows, tile_rows), pl.ds(LANES, padded_cols)] = acc
            rows_ref[pl.ds(f * tile_rows, tile_rows), pl.ds(0, LANES)] = acc[:, padded_cols - LANES :]
        rowsum = rows_ref[...]
        high = rowsum.astype(jnp.bfloat16)
        low = (rowsum - high.astype(jnp.float32)).astype(jnp.bfloat16)
        width = 3 * LANES
        for j in range(blocks):
            stack_ref[pl.ds(j * rows, rows), pl.ds(0, width)] = high[:, j * LANES : j * LANES + width]
            stack_ref[pl.ds(j * rows, rows), pl.ds(width, width)] = low[:, j * LANES : j * LANES + width]
        sums = jnp.dot(stack_ref[...], band_ref[...], preferred_element_type=jnp.float32)
        return sums / float(window * window)

    @pl.when(step == 0)
    def _():
        def chunk(k, carry):
            for a in range(count):
                for at, piece in pieces(k * count + a):
                    re = piece[0].astype(jnp.float32)
                    im = piece[1].astype(jnp.float32)
                    field_ref[a, :, pl.ds(at, piece.shape[-1])] = re * re + im * im
            means = box_pass()
            for j in range(blocks):
                for a in range(count):
                    base = j * rows + a * tile_rows
                    power_ref[k * count + a, :, pl.ds(j * LANES, LANES)] = (
                        means[base : base + tile_rows] + 1e-06
                    )
            return carry

        lax.fori_loop(0, main_ref.shape[1] // count, chunk, 0)

    pre_at = [pre_ref[step * pp + p] for p in range(pp)]
    post_at = [post_ref[step * pp + p] for p in range(pp)]
    for p in range(pp):
        for (at, a), (_, b) in zip(pieces(pre_at[p]), pieces(post_at[p])):
            width = a.shape[-1]
            pr = a[0].astype(jnp.float32)
            pi = a[1].astype(jnp.float32)
            qr = b[0].astype(jnp.float32)
            qi = b[1].astype(jnp.float32)
            field_ref[2 * p, :, pl.ds(at, width)] = pr * qr + pi * qi
            field_ref[2 * p + 1, :, pl.ds(at, width)] = pi * qr - pr * qi
    means = box_pass()
    for j in range(blocks):
        for p in range(pp):
            pre_power = power_ref[pre_at[p], :, pl.ds(j * LANES, LANES)]
            post_power = power_ref[post_at[p], :, pl.ds(j * LANES, LANES)]
            base = j * rows + 2 * p * tile_rows
            real_mean = means[base : base + tile_rows]
            imag_mean = means[base + tile_rows : base + 2 * tile_rows]
            coh = jnp.sqrt(real_mean * real_mean + imag_mean * imag_mean) / jnp.sqrt(
                pre_power * post_power
            )
            coh_ref[p, :, pl.ds(j * LANES, LANES)] = coh
            chg_ref[p, :, pl.ds(j * LANES, LANES)] = jnp.log(post_power / pre_power)


def pair_maps(main, edge, pre_ids, post_ids, tile_rows, tile_cols):
    count_pairs = pre_ids.shape[0]
    pp = PAIRS_PER_STEP
    blocks_per_tile, _, _, padded_rows, block_cols = main.shape
    width = 3 * LANES
    lane_in = jnp.arange(width)[:, None]
    lane_out = jnp.arange(LANES)[None, :]
    gap = lane_in - LANES - lane_out
    band = jnp.where((gap >= -RADIUS) & (gap <= RADIUS), 1.0, 0.0).astype(jnp.bfloat16)
    band = jnp.concatenate([band, band], axis=0)
    in_specs = [
        pl.BlockSpec(main.shape, lambda i, pre, post: (0,) * main.ndim),
        pl.BlockSpec(edge.shape, lambda i, pre, post: (0,) * edge.ndim),
        pl.BlockSpec((2 * width, LANES), lambda i, pre, post: (0, 0)),
    ]
    operands = [main, edge, band]
    out_block = pl.BlockSpec((pp, tile_rows, tile_cols), lambda i, pre, post: (i, 0, 0))
    rows = 2 * pp * tile_rows
    blocks = tile_cols // LANES
    padded_cols = tile_cols + LANES
    grid_spec = pltpu.PrefetchScalarGridSpec(
        num_scalar_prefetch=2,
        grid=(count_pairs // pp,),
        in_specs=in_specs,
        out_specs=[out_block, out_block],
        scratch_shapes=[
            pltpu.VMEM((2 * pp, padded_rows, padded_cols), jnp.float32),
            pltpu.VMEM((rows, padded_cols + LANES), jnp.float32),
            pltpu.VMEM((blocks * rows, 2 * width), jnp.bfloat16),
            pltpu.VMEM((main.shape[1], tile_rows, tile_cols), jnp.float32),
        ],
    )
    out_shape = jax.ShapeDtypeStruct((count_pairs, tile_rows, tile_cols), jnp.float32)
    kernel = functools.partial(pair_kernel, tile_rows=tile_rows, tile_cols=tile_cols)
    return pl.pallas_call(
        kernel,
        grid_spec=grid_spec,
        out_shape=[out_shape, out_shape],
    )(pre_ids, post_ids, *operands)


def shards(stack, filt_re, filt_im, pre_ids, post_ids):
    count_acq = filt_re.shape[0]
    n_rows = lax.axis_size("ty")
    n_cols = lax.axis_size("tx")
    local_acq, _, height, local_cols = stack.shape
    tile_rows = height // n_rows
    blocks_per_tile = n_rows // n_cols
    tile_cols = local_cols * blocks_per_tile
    padded_rows = tile_rows + 2 * RADIUS

    me_col = lax.axis_index("tx")
    me_row = lax.axis_index("ty")
    x = jnp.pad(stack, ((0, 0), (0, 0), (RADIUS, RADIUS), (0, 0)))
    start = me_col * blocks_per_tile + me_row % blocks_per_tile
    received = []
    for m in range(n_rows):
        pairs = []
        for col in range(n_cols):
            for row in range(n_rows):
                to_row = (m + col * blocks_per_tile + row % blocks_per_tile) % n_rows
                pairs.append((col * n_rows + row, (row // blocks_per_tile) * n_rows + to_row))
        first = ((start + m) % n_rows) * tile_rows
        chunk = lax.dynamic_slice_in_dim(x, first, padded_rows, axis=2)
        chunk = chunk.reshape(local_acq * 2 * padded_rows, local_cols)
        received.append(lax.ppermute(chunk, ("tx", "ty"), pairs))
    x = jnp.zeros((n_rows,) + received[0].shape, received[0].dtype)
    for m, chunk in enumerate(received):
        s = (me_row - m) % n_rows
        x = lax.dynamic_update_index_in_dim(x, chunk, (s % blocks_per_tile) * n_cols + s // blocks_per_tile, 0)
    x = x.reshape(blocks_per_tile, 2 * count_acq, padded_rows, local_cols)

    forward = [(i, i + 1) for i in range(n_cols - 1)]
    backward = [(target, source) for source, target in forward]
    left = lax.ppermute(x[blocks_per_tile - 1, :, :, local_cols - LANES :], "tx", forward)
    right = lax.ppermute(x[0, :, :, :LANES], "tx", backward)
    lane = lax.broadcasted_iota(jnp.int32, right.shape, 2)
    zeros = jnp.zeros_like(right)
    edge = jnp.where(lane < RADIUS, right, jnp.where(lane >= LANES - RADIUS, left, zeros))

    mixing = jnp.stack([jnp.stack([filt_re, -filt_im], -1), jnp.stack([filt_im, filt_re], -1)], 1)
    mixing = mixing.reshape(2 * count_acq, 2 * count_acq)
    main = jnp.einsum("kc,bchw->bkhw", mixing, x, preferred_element_type=jnp.float32)
    main = main.astype(jnp.bfloat16).reshape(blocks_per_tile, count_acq, 2, padded_rows, local_cols)
    edge = jnp.einsum("kc,chw->khw", mixing, edge, preferred_element_type=jnp.float32)
    edge = edge.astype(jnp.bfloat16).reshape(count_acq, 2, padded_rows, LANES)
    return pair_maps(main, edge, pre_ids, post_ids, tile_rows, tile_cols)


def solution(mesh):
    in_specs = (P("tx", None, None, "ty"), P(), P(), P(), P())
    out_specs = (P(None, "ty", "tx"), P(None, "ty", "tx"))
    return jax.shard_map(shards, mesh=mesh, in_specs=in_specs, out_specs=out_specs, check_vma=False)
```

```python
import functools

import jax
import jax.numpy as jnp
from jax import lax
from jax.experimental import pallas as pl
from jax.experimental.pallas import tpu as pltpu
from jax.sharding import PartitionSpec as P

RADIUS = 4
LANES = 128
PAIRS_PER_STEP = 16
FIELDS = 4


def window_rows(full, window):
    count = full.shape[0]
    total, offset, span, part = None, 0, 1, full
    remaining = window
    while remaining:
        if remaining & 1:
            shifted = part if offset == 0 else pltpu.roll(part, count - offset, 0)
            total = shifted if total is None else total + shifted
            offset += span
        remaining >>= 1
        if remaining:
            part = part + pltpu.roll(part, count - span, 0)
            span *= 2
    return total


def pair_kernel(pre_ref, post_ref, main_ref, edge_ref, band_ref, coh_ref, chg_ref, field_ref, rows_ref, stack_ref, power_ref, *, tile_rows, tile_cols):
    pp = PAIRS_PER_STEP
    count = 2 * pp
    step = pl.program_id(0)
    window = 2 * RADIUS + 1
    padded_cols = tile_cols + LANES
    rows = count * tile_rows
    blocks = tile_cols // LANES
    block_cols = main_ref.shape[-1]

    def pieces(index):
        parts = [(c * block_cols, main_ref[c, index]) for c in range(main_ref.shape[0])]
        parts.append((tile_cols, edge_ref[index]))
        return parts

    def box_pass():
        for f in range(count):
            acc = window_rows(field_ref[f], window)[:tile_rows]
            rows_ref[pl.ds(f * tile_rows, tile_rows), pl.ds(LANES, padded_cols)] = acc
            rows_ref[pl.ds(f * tile_rows, tile_rows), pl.ds(0, LANES)] = acc[:, padded_cols - LANES :]
        rowsum = rows_ref[...]
        high = rowsum.astype(jnp.bfloat16)
        low = (rowsum - high.astype(jnp.float32)).astype(jnp.bfloat16)
        width = 3 * LANES
        for j in range(blocks):
            stack_ref[pl.ds(j * rows, rows), pl.ds(0, width)] = high[:, j * LANES : j * LANES + width]
            stack_ref[pl.ds(j * rows, rows), pl.ds(width, width)] = low[:, j * LANES : j * LANES + width]
        sums = jnp.dot(stack_ref[...], band_ref[...], preferred_element_type=jnp.float32)
        return sums / float(window * window)

    @pl.when(step == 0)
    def _():
        def chunk(k, carry):
            for a in range(count):
                for at, piece in pieces(k * count + a):
                    re = piece[0].astype(jnp.float32)
                    im = piece[1].astype(jnp.float32)
                    field_ref[a, :, pl.ds(at, piece.shape[-1])] = re * re + im * im
            means = box_pass()
            for j in range(blocks):
                for a in range(count):
                    base = j * rows + a * tile_rows
                    power_ref[k * count + a, :, pl.ds(j * LANES, LANES)] = (
                        means[base : base + tile_rows] + 1e-06
                    )
            return carry

        lax.fori_loop(0, main_ref.shape[1] // count, chunk, 0)

    pre_at = [pre_ref[step * pp + p] for p in range(pp)]
    post_at = [post_ref[step * pp + p] for p in range(pp)]
    for p in range(pp):
        for (at, a), (_, b) in zip(pieces(pre_at[p]), pieces(post_at[p])):
            width = a.shape[-1]
            pr = a[0].astype(jnp.float32)
            pi = a[1].astype(jnp.float32)
            qr = b[0].astype(jnp.float32)
            qi = b[1].astype(jnp.float32)
            field_ref[2 * p, :, pl.ds(at, width)] = pr * qr + pi * qi
            field_ref[2 * p + 1, :, pl.ds(at, width)] = pi * qr - pr * qi
    means = box_pass()
    for j in range(blocks):
        for p in range(pp):
            pre_power = power_ref[pre_at[p], :, pl.ds(j * LANES, LANES)]
            post_power = power_ref[post_at[p], :, pl.ds(j * LANES, LANES)]
            base = j * rows + 2 * p * tile_rows
            real_mean = means[base : base + tile_rows]
            imag_mean = means[base + tile_rows : base + 2 * tile_rows]
            coh = jnp.sqrt(real_mean * real_mean + imag_mean * imag_mean) / jnp.sqrt(
                pre_power * post_power
            )
            coh_ref[p, :, pl.ds(j * LANES, LANES)] = coh
            chg_ref[p, :, pl.ds(j * LANES, LANES)] = jnp.log(post_power / pre_power)


def pair_maps(main, edge, pre_ids, post_ids, tile_rows, tile_cols):
    count_pairs = pre_ids.shape[0]
    pp = PAIRS_PER_STEP
    blocks_per_tile, _, _, padded_rows, block_cols = main.shape
    width = 3 * LANES
    lane_in = jnp.arange(width)[:, None]
    lane_out = jnp.arange(LANES)[None, :]
    gap = lane_in - LANES - lane_out
    band = jnp.where((gap >= -RADIUS) & (gap <= RADIUS), 1.0, 0.0).astype(jnp.bfloat16)
    band = jnp.concatenate([band, band], axis=0)
    in_specs = [
        pl.BlockSpec(main.shape, lambda i, pre, post: (0,) * main.ndim),
        pl.BlockSpec(edge.shape, lambda i, pre, post: (0,) * edge.ndim),
        pl.BlockSpec((2 * width, LANES), lambda i, pre, post: (0, 0)),
    ]
    operands = [main, edge, band]
    out_block = pl.BlockSpec((pp, tile_rows, tile_cols), lambda i, pre, post: (i, 0, 0))
    rows = 2 * pp * tile_rows
    blocks = tile_cols // LANES
    padded_cols = tile_cols + LANES
    grid_spec = pltpu.PrefetchScalarGridSpec(
        num_scalar_prefetch=2,
        grid=(count_pairs // pp,),
        in_specs=in_specs,
        out_specs=[out_block, out_block],
        scratch_shapes=[
            pltpu.VMEM((2 * pp, padded_rows, padded_cols), jnp.float32),
            pltpu.VMEM((rows, padded_cols + LANES), jnp.float32),
            pltpu.VMEM((blocks * rows, 2 * width), jnp.bfloat16),
            pltpu.VMEM((main.shape[1], tile_rows, tile_cols), jnp.float32),
        ],
    )
    out_shape = jax.ShapeDtypeStruct((count_pairs, tile_rows, tile_cols), jnp.float32)
    kernel = functools.partial(pair_kernel, tile_rows=tile_rows, tile_cols=tile_cols)
    return pl.pallas_call(
        kernel,
        grid_spec=grid_spec,
        out_shape=[out_shape, out_shape],
    )(pre_ids, post_ids, *operands)


def shards(stack, filt_re, filt_im, pre_ids, post_ids):
    count_acq = filt_re.shape[0]
    n_rows = lax.axis_size("ty")
    n_cols = lax.axis_size("tx")
    local_acq, _, height, local_cols = stack.shape
    tile_rows = height // n_rows
    blocks_per_tile = n_rows // n_cols
    tile_cols = local_cols * blocks_per_tile
    padded_rows = tile_rows + 2 * RADIUS

    me_col = lax.axis_index("tx")
    me_row = lax.axis_index("ty")
    x = jnp.pad(stack, ((0, 0), (0, 0), (RADIUS, RADIUS), (0, 0)))
    start = me_col * blocks_per_tile + me_row % blocks_per_tile
    received = []
    for m in range(n_rows):
        pairs = []
        for col in range(n_cols):
            for row in range(n_rows):
                to_row = (m + col * blocks_per_tile + row % blocks_per_tile) % n_rows
                pairs.append((col * n_rows + row, (row // blocks_per_tile) * n_rows + to_row))
        first = ((start + m) % n_rows) * tile_rows
        chunk = lax.dynamic_slice_in_dim(x, first, padded_rows, axis=2)
        chunk = chunk.reshape(local_acq * 2 * padded_rows, local_cols)
        received.append(lax.ppermute(chunk, ("tx", "ty"), pairs))
    received = jnp.stack(received, axis=0)
    source = jnp.arange(blocks_per_tile)[:, None] + blocks_per_tile * jnp.arange(n_cols)[None, :]
    order = (me_row - source) % n_rows
    x = jnp.take(received, order.reshape(-1), axis=0)
    x = x.reshape(blocks_per_tile, 2 * count_acq, padded_rows, local_cols)

    forward = [(i, i + 1) for i in range(n_cols - 1)]
    backward = [(target, source) for source, target in forward]
    left = lax.ppermute(x[blocks_per_tile - 1, :, :, local_cols - LANES :], "tx", forward)
    right = lax.ppermute(x[0, :, :, :LANES], "tx", backward)
    lane = lax.broadcasted_iota(jnp.int32, right.shape, 2)
    zeros = jnp.zeros_like(right)
    edge = jnp.where(lane < RADIUS, right, jnp.where(lane >= LANES - RADIUS, left, zeros))

    mixing = jnp.stack([jnp.stack([filt_re, -filt_im], -1), jnp.stack([filt_im, filt_re], -1)], 1)
    mixing = mixing.reshape(2 * count_acq, 2 * count_acq)
    main = jnp.einsum("kc,bchw->bkhw", mixing, x, preferred_element_type=jnp.float32)
    main = main.astype(jnp.bfloat16).reshape(blocks_per_tile, count_acq, 2, padded_rows, local_cols)
    edge = jnp.einsum("kc,chw->khw", mixing, edge, preferred_element_type=jnp.float32)
    edge = edge.astype(jnp.bfloat16).reshape(count_acq, 2, padded_rows, LANES)
    return pair_maps(main, edge, pre_ids, post_ids, tile_rows, tile_cols)


def solution(mesh):
    in_specs = (P("tx", None, None, "ty"), P(), P(), P(), P())
    out_specs = (P(None, "ty", "tx"), P(None, "ty", "tx"))
    return jax.shard_map(shards, mesh=mesh, in_specs=in_specs, out_specs=out_specs, check_vma=False)
```
